32 devices in a mesh: date: 8 (over z, y), az: 4 (over x, core).
Axes of the slice: x: 2, y: 2, z: 4, core: 2. Of those that a mesh axis runs over, the one named last changes fastest.
Arguments:
- slc: bfloat16 [8, 2, 640, 4096], P('date', None, 'az'), may hold values from -18 to 18
- az_offset: int32 [8], P('date'), may hold values from -12 to 12
- az_kernel: int32 [8], P('date'), may hold values from 0 to 63
- rg_offset: int32 [8, 640], P('date', 'az'), may hold values from -12 to 12
- rg_kernel: int32 [8, 640], P('date', 'az'), may hold values from 0 to 63
- partners: int32 [8, 4], P('date'), may hold values from 0 to 7, as said below
Outputs:
- interferograms: float32 [8, 4, 2, 32, 1024], P('date', None, None, 'az')
The draws below stay inside these ranges and needn't reach their ends.
Inputs may be any that keep to these rules, and one draw needn't show every extreme that they name: `partners`: each row holds 4 distinct dates other than its own date, each within 4 dates of it; some date has a partner 4 dates later and some date one 4 dates earlier.
All inputs are finite; a program needn't handle non-finite values.
Results may differ from the reference program's by a relative error of at most 0.004.
Values may be sent and summed in bfloat16 or wider, within the bound.
No kernel may reach another device: no remote copies, remote signals or barrier semaphores. Data moves between devices by JAX's collectives and lax.ppermute only.
A program may use at most 128 MiB of HBM per device.

```python
import jax
import jax.numpy as jnp
from jax import lax

RANGE = 4096
PARTNERS = 4
GAP = 4
OFFAZ = 12
OFFRG = 12
NFRAC = 64
LOOK_AZ = 20
LOOK_RG = 4
DATES = 8
LINES = 640


def draw_az_offset(key, part):
    first, second = jax.random.split(jax.random.fold_in(key, 11))
    values = jax.random.randint(first, (DATES,), -OFFAZ, OFFAZ + 1)
    order = jax.random.permutation(second, DATES)
    values = values.at[order[0]].set(-OFFAZ).at[order[1]].set(OFFAZ)
    return values.astype(jnp.int32)


def draw_rg_offset(key, part):
    first, second = jax.random.split(jax.random.fold_in(key, 23))
    values = jax.random.randint(first, (DATES * LINES,), -OFFRG, OFFRG + 1)
    order = jax.random.permutation(second, DATES * LINES)
    values = values.at[order[0]].set(-OFFRG).at[order[1]].set(OFFRG)
    return values.reshape(DATES, LINES).astype(jnp.int32)


def draw_partners(key, part):
    steps = jnp.concatenate([jnp.arange(-GAP, 0), jnp.arange(1, GAP + 1)]).astype(jnp.int32)
    dates = jnp.arange(DATES, dtype=jnp.int32)[:, None]
    candidate = dates + steps[None, :]
    valid = (candidate >= 0) & (candidate < DATES)
    scores = jax.random.randint(jax.random.fold_in(key, 37), (DATES, 2 * GAP), 0, 1000)
    scores = scores * (2 * GAP) + jnp.arange(2 * GAP, dtype=jnp.int32)[None, :]
    scores = jnp.where(valid, scores, scores + 1048576)
    order = jnp.argsort(scores, axis=1, stable=True)[:, :PARTNERS]
    return jnp.take_along_axis(candidate, order, axis=1).astype(jnp.int32)


def touch_ends(entries, own_key, low, top_value):
    spot = [jax.random.randint(jax.random.fold_in(own_key, axis), (), 0, length) for axis, length in enumerate(entries.shape)]
    longest = entries.shape.index(max(entries.shape))
    neighbour = spot[:longest] + [(spot[longest] + 1) % entries.shape[longest]] + spot[longest + 1:]
    return entries.at[tuple(spot)].set(low).at[tuple(neighbour)].set(top_value)


def levels(stream_key, shape, cuts, low, high):
    def one(axis_at, parts):
        steps = jax.random.uniform(jax.random.fold_in(jax.random.fold_in(stream_key, 6), axis_at), (parts,), jnp.float32, low / len(cuts), high / len(cuts))
        return jnp.repeat(jnp.exp(steps), shape[axis_at] // parts).reshape((-1,) + (1,) * (len(shape) - axis_at - 1))

    gain = one(*cuts[0])
    for cut in cuts[1:]:
        gain = gain * one(*cut)
    return gain


def gaussian(key, dims, deviation, reach, cuts=(), kind=jnp.bfloat16):
    values = jax.random.normal(key, dims, jnp.float32) * deviation
    if len(cuts) > 0:
        values = levels(key, dims, cuts, -0.22, 0.18) * values
    return jnp.clip(values, min=-reach, max=reach).astype(kind)


def setup_inputs(seed: int = 0) -> dict:
    arg_keys = jax.random.split(jax.random.key(seed), 7)
    return {
        "slc": gaussian(arg_keys[0], (DATES, 2, LINES, RANGE), 3.0, 18.0, ((0, 8), (2, 4))),
        "az_offset": draw_az_offset(jax.random.fold_in(arg_keys[6], 71), 0),
        "az_kernel": touch_ends(jax.random.randint(arg_keys[2], (DATES,), 0, NFRAC), jax.random.fold_in(arg_keys[2], 1), 0, NFRAC - 1).astype(jnp.int32),
        "rg_offset": draw_rg_offset(jax.random.fold_in(arg_keys[6], 71), 0),
        "rg_kernel": touch_ends(jax.random.randint(arg_keys[4], (DATES, LINES), 0, NFRAC), jax.random.fold_in(arg_keys[4], 1), 0, NFRAC - 1).astype(jnp.int32),
        "partners": draw_partners(jax.random.fold_in(arg_keys[6], 71), 0),
    }


def kernel_table():
    frac = jnp.arange(NFRAC, dtype=jnp.float32)[:, None] / NFRAC
    taps = jnp.arange(8, dtype=jnp.float32)[None, :]
    place = taps - 3.0 - frac
    return jnp.sinc(place) * (0.5 + 0.5 * jnp.cos(jnp.pi * place / 4.5))


def resample(image, shift_lines, kern_lines, shift_range, kern_range):
    table = kernel_table()
    nlines = image.shape[1]
    border = OFFAZ + 4
    padded = jnp.pad(image, ((0, 0), (border, border), (0, 0)))
    start = (border + shift_lines - 3).astype(jnp.int32)
    window = lax.dynamic_slice_in_dim(padded, start, nlines + 7, 1)
    weights = table[kern_lines]
    along = jnp.zeros((2, nlines, RANGE), jnp.float32)
    for tap in range(8):
        along = along + weights[tap] * window[:, tap:tap + nlines, :].astype(jnp.float32)
    margin = OFFRG + 4
    widened = jnp.pad(along, ((0, 0), (0, 0), (margin, margin)))
    starts = (margin + shift_range - 3).astype(jnp.int32)

    def one_line(row, first):
        return lax.dynamic_slice_in_dim(row, first, RANGE + 7, 1)

    rows = jax.vmap(one_line, in_axes=(1, 0), out_axes=1)(widened, starts)
    range_weights = table[kern_range]
    result = jnp.zeros((2, nlines, RANGE), jnp.float32)
    for tap in range(8):
        result = result + range_weights[None, :, tap, None] * rows[:, :, tap:tap + RANGE]
    return result.astype(jnp.bfloat16)


def looks(first, second):
    first_re = first[0].astype(jnp.float32)
    first_im = first[1].astype(jnp.float32)
    second_re = second[0].astype(jnp.float32)
    second_im = second[1].astype(jnp.float32)
    real_part = first_re * second_re + first_im * second_im
    imag_part = first_im * second_re - first_re * second_im
    product = jnp.stack([real_part, imag_part])
    nlines = product.shape[1]
    summed = product.reshape(2, nlines // LOOK_AZ, LOOK_AZ, RANGE).sum(axis=2)
    summed = summed.reshape(2, nlines // LOOK_AZ, RANGE // LOOK_RG, LOOK_RG).sum(axis=3)
    return summed / (LOOK_AZ * LOOK_RG)


def reference(slc, az_offset, az_kernel, rg_offset, rg_kernel, partners):
    def resample_date(items):
        return resample(items[0], items[1], items[2], items[3], items[4])

    stacked = lax.map(resample_date, (slc, az_offset, az_kernel, rg_offset, rg_kernel))

    def per_date(index):
        own = lax.dynamic_index_in_dim(stacked, index, 0, keepdims=False)
        listed = lax.dynamic_index_in_dim(partners, index, 0, keepdims=False)
        outputs = []
        for slot in range(PARTNERS):
            other = lax.dynamic_index_in_dim(stacked, listed[slot], 0, keepdims=False)
            outputs.append(looks(own, other))
        return jnp.stack(outputs)

    return lax.map(per_date, jnp.arange(DATES, dtype=jnp.int32))
```

```python
import jax
import jax.numpy as jnp
from jax import lax
from jax.sharding import PartitionSpec as P

PARTNERS = 4
GAP = 4
OFFAZ = 12
OFFRG = 12
NFRAC = 64
LOOK_AZ = 20
LOOK_RG = 4


def padded_2(cells, sides, width):
    for axis, dim in sides:
        count = lax.axis_size(axis)
        ends = count - 1
        head = lax.slice_in_dim(cells, 0, width, axis=dim)
        tail = lax.slice_in_dim(cells, cells.shape[dim] - width, cells.shape[dim], axis=dim)
        cells = jnp.concatenate(
            [
                lax.ppermute(tail, axis, [(i, (i + 1) % count) for i in range(ends)]),
                cells,
                lax.ppermute(head, axis, [((i + 1) % count, i) for i in range(ends)]),
            ],
            axis=dim,
        )
    return cells


def shifted(block, axis, distance):
    count = lax.axis_size(axis)
    route = [(i + distance, i) for i in range(count) if 0 <= i + distance < count]
    return lax.ppermute(block, axis, route)


def swapped(block, axis):
    count = lax.axis_size(axis)
    return lax.ppermute(block, axis, [(i, i ^ 1) for i in range(count)])


def kernel_table():
    frac = jnp.arange(NFRAC, dtype=jnp.float32)[:, None] / NFRAC
    taps = jnp.arange(8, dtype=jnp.float32)[None, :]
    place = taps - 3.0 - frac
    return jnp.sinc(place) * (0.5 + 0.5 * jnp.cos(jnp.pi * place / 4.5))


def resample_block(padded, shift_lines, kern_lines, shift_range, kern_range):
    table = kernel_table()
    nlines = shift_range.shape[0]
    nrange = padded.shape[2]
    border = OFFAZ + 4
    start = border + shift_lines - 3
    window = lax.dynamic_slice_in_dim(padded, start, nlines + 7, 1)
    weights = table[kern_lines]
    along = jnp.zeros((2, nlines, nrange), jnp.float32)
    for tap in range(8):
        along = along + weights[tap] * window[:, tap : tap + nlines, :].astype(jnp.float32)
    margin = OFFRG + 4
    widened = jnp.pad(along, ((0, 0), (0, 0), (margin, margin)))
    selector = (kern_range[:, None] == jnp.arange(NFRAC, dtype=jnp.int32)[None, :]).astype(
        jnp.float32
    )
    range_weights = jnp.dot(selector, table, precision=lax.Precision.HIGHEST)
    targets = shift_range[:, None] + jnp.arange(8, dtype=jnp.int32)[None, :] - 3
    result = jnp.zeros((2, nlines, nrange), jnp.float32)
    for offset in range(-OFFRG - 3, OFFRG + 5):
        coeff = jnp.sum(jnp.where(targets == offset, range_weights, 0.0), axis=1)
        result = (
            result
            + coeff[None, :, None] * widened[:, :, margin + offset : margin + offset + nrange]
        )
    return result.astype(jnp.bfloat16)


def looks(first, second):
    first_re = first[0].astype(jnp.float32)
    first_im = first[1].astype(jnp.float32)
    second_re = second[0].astype(jnp.float32)
    second_im = second[1].astype(jnp.float32)
    real_part = first_re * second_re + first_im * second_im
    imag_part = first_im * second_re - first_re * second_im
    product = jnp.stack([real_part, imag_part])
    nlines = product.shape[1]
    nrange = product.shape[2]
    summed = product.reshape(2, nlines // LOOK_AZ, LOOK_AZ, nrange // LOOK_RG, LOOK_RG).sum(axis=(2, 4))
    return summed / (LOOK_AZ * LOOK_RG)


def conj(block):
    return jnp.stack([block[0], -block[1]])


def shards(slc, az_offset, az_kernel, rg_offset, rg_kernel, partners):
    padded = padded_2(slc, (("az", 2),), OFFAZ + 4)
    resampled = resample_block(padded[0], az_offset[0], az_kernel[0], rg_offset[0], rg_kernel[0])
    half = resampled.shape[2] // 2
    own_left = resampled[:, :, :half]
    own_right = resampled[:, :, half:]
    date = lax.axis_index("date")
    even = date % 2 == 0

    left_2 = shifted(own_left, "date", 2)
    left_4 = shifted(left_2, "date", 2)
    left_a = swapped(left_2, "date")
    left_x = swapped(jnp.where(even, left_4, own_left), "date")
    right_2 = shifted(own_right, "date", -2)
    right_4 = shifted(right_2, "date", -2)
    right_a = swapped(right_2, "date")
    right_x = swapped(jnp.where(even, own_right, right_4), "date")

    ahead_2 = looks(own_left, left_2)
    ahead_4 = looks(own_left, left_4)
    ahead_a = looks(own_left, left_a)
    ahead_x = looks(own_left, left_x)
    behind_2 = looks(own_right, right_2)
    behind_4 = looks(own_right, right_4)
    behind_a = looks(own_right, right_a)
    behind_x = looks(own_right, right_x)
    ahead = {
        1: jnp.where(even, ahead_x, ahead_a),
        2: ahead_2,
        3: jnp.where(even, ahead_a, ahead_x),
        4: ahead_4,
    }
    behind = {
        1: jnp.where(even, behind_a, behind_x),
        2: behind_2,
        3: jnp.where(even, behind_x, behind_a),
        4: behind_4,
    }
    full = {}
    for s in range(1, GAP + 1):
        right_of_ahead = conj(shifted(behind[s], "date", s))
        left_of_behind = conj(shifted(ahead[s], "date", -s))
        full[s] = jnp.concatenate([ahead[s], right_of_ahead], axis=2)
        full[-s] = jnp.concatenate([left_of_behind, behind[s]], axis=2)

    listed = partners[0]
    outputs = []
    for slot in range(PARTNERS):
        value = jnp.zeros_like(full[1])
        for step, block in full.items():
            value = jnp.where(listed[slot] == date + step, block, value)
        outputs.append(value)
    return jnp.stack(outputs)[None]


def solution(mesh):
    in_specs = (
        P("date", None, "az", None),
        P("date"),
        P("date"),
        P("date", "az"),
        P("date", "az"),
        P("date", None),
    )
    out_specs = P("date", None, None, "az", None)
    return jax.shard_map(shards, mesh=mesh, in_specs=in_specs, out_specs=out_specs, check_vma=False)
```

```python
import jax
import jax.numpy as jnp
from jax import lax
from jax.sharding import PartitionSpec as P
from jax.experimental import pallas as pl
from jax.experimental.pallas import tpu as pltpu

PARTNERS = 4
GAP = 4
OFFAZ = 12
OFFRG = 12
NFRAC = 64
LOOK_AZ = 20
LOOK_RG = 4


def padded_2(cells, sides, width):
    for axis, dim in sides:
        count = lax.axis_size(axis)
        ends = count - 1
        head = lax.slice_in_dim(cells, 0, width, axis=dim)
        tail = lax.slice_in_dim(cells, cells.shape[dim] - width, cells.shape[dim], axis=dim)
        cells = jnp.concatenate(
            [
                lax.ppermute(tail, axis, [(i, (i + 1) % count) for i in range(ends)]),
                cells,
                lax.ppermute(head, axis, [((i + 1) % count, i) for i in range(ends)]),
            ],
            axis=dim,
        )
    return cells


def shifted(block, axis, distance):
    count = lax.axis_size(axis)
    route = [(i + distance, i) for i in range(count) if 0 <= i + distance < count]
    return lax.ppermute(block, axis, route)


def swapped(block, axis):
    count = lax.axis_size(axis)
    return lax.ppermute(block, axis, [(i, i ^ 1) for i in range(count)])


def kernel_table():
    frac = jnp.arange(NFRAC, dtype=jnp.float32)[:, None] / NFRAC
    taps = jnp.arange(8, dtype=jnp.float32)[None, :]
    place = taps - 3.0 - frac
    return jnp.sinc(place) * (0.5 + 0.5 * jnp.cos(jnp.pi * place / 4.5))


def resample_block(padded, shift_lines, kern_lines, shift_range, kern_range):
    table = kernel_table()
    nlines = shift_range.shape[0]
    nrange = padded.shape[2]
    border = OFFAZ + 4
    start = border + shift_lines - 3
    window = lax.dynamic_slice_in_dim(padded, start, nlines + 7, 1)
    weights = table[kern_lines]
    along = jnp.zeros((2, nlines, nrange), jnp.float32)
    for tap in range(8):
        along = along + weights[tap] * window[:, tap : tap + nlines, :].astype(jnp.float32)
    margin = OFFRG + 4
    widened = jnp.pad(along, ((0, 0), (0, 0), (margin, margin)))
    selector = (kern_range[:, None] == jnp.arange(NFRAC, dtype=jnp.int32)[None, :]).astype(
        jnp.float32
    )
    range_weights = jnp.dot(selector, table, precision=lax.Precision.HIGHEST)
    targets = shift_range[:, None] + jnp.arange(8, dtype=jnp.int32)[None, :] - 3
    result = jnp.zeros((2, nlines, nrange), jnp.float32)
    for offset in range(-OFFRG - 3, OFFRG + 5):
        coeff = jnp.sum(jnp.where(targets == offset, range_weights, 0.0), axis=1)
        result = (
            result
            + coeff[None, :, None] * widened[:, :, margin + offset : margin + offset + nrange]
        )
    return result.astype(jnp.bfloat16)


CHUNK = 512


def looks_kernel(first_ref, second_ref, out_ref):
    first_re = first_ref[0].astype(jnp.float32)
    first_im = first_ref[1].astype(jnp.float32)
    second_re = second_ref[0].astype(jnp.float32)
    second_im = second_ref[1].astype(jnp.float32)
    real_part = first_re * second_re + first_im * second_im
    imag_part = first_im * second_re - first_re * second_im
    rows = real_part.shape[0]
    groups = rows // LOOK_AZ
    real_lines = real_part.reshape(LOOK_AZ, groups, CHUNK).sum(axis=0)
    imag_lines = imag_part.reshape(LOOK_AZ, groups, CHUNK).sum(axis=0)
    pooling = (
        lax.broadcasted_iota(jnp.int32, (CHUNK, CHUNK // LOOK_RG), 0) // LOOK_RG
        == lax.broadcasted_iota(jnp.int32, (CHUNK, CHUNK // LOOK_RG), 1)
    ).astype(jnp.float32)
    real_looks = jnp.dot(real_lines, pooling, precision=lax.Precision.HIGHEST, preferred_element_type=jnp.float32)
    imag_looks = jnp.dot(imag_lines, pooling, precision=lax.Precision.HIGHEST, preferred_element_type=jnp.float32)
    out_ref[0] = real_looks / (LOOK_AZ * LOOK_RG)
    out_ref[1] = imag_looks / (LOOK_AZ * LOOK_RG)


def looks(first, second):
    nlines = first.shape[1]
    width = first.shape[2]
    groups = nlines // LOOK_AZ
    spec = pl.BlockSpec((2, nlines, CHUNK), lambda j: (0, 0, j))
    return pl.pallas_call(
        looks_kernel,
        grid=(width // CHUNK,),
        in_specs=[spec, spec],
        out_specs=pl.BlockSpec((2, groups, CHUNK // LOOK_RG), lambda j: (0, 0, j)),
        out_shape=jax.ShapeDtypeStruct((2, groups, width // LOOK_RG), jnp.float32),
    )(first, second)


def look_order(image):
    nlines = image.shape[1]
    groups = nlines // LOOK_AZ
    return image.reshape(2, groups, LOOK_AZ, image.shape[2]).transpose(0, 2, 1, 3).reshape(image.shape)


def conj(block):
    return jnp.stack([block[0], -block[1]])


def shards(slc, az_offset, az_kernel, rg_offset, rg_kernel, partners):
    padded = padded_2(slc, (("az", 2),), OFFAZ + 4)
    resampled = resample_block(padded[0], az_offset[0], az_kernel[0], rg_offset[0], rg_kernel[0])
    resampled = look_order(resampled)
    half = resampled.shape[2] // 2
    own_left = resampled[:, :, :half]
    own_right = resampled[:, :, half:]
    date = lax.axis_index("date")
    even = date % 2 == 0

    left_2 = shifted(own_left, "date", 2)
    left_4 = shifted(left_2, "date", 2)
    left_a = swapped(left_2, "date")
    left_x = swapped(jnp.where(even, left_4, own_left), "date")
    right_2 = shifted(own_right, "date", -2)
    right_4 = shifted(right_2, "date", -2)
    right_a = swapped(right_2, "date")
    right_x = swapped(jnp.where(even, own_right, right_4), "date")

    ahead_2 = looks(own_left, left_2)
    ahead_4 = looks(own_left, left_4)
    ahead_a = looks(own_left, left_a)
    ahead_x = looks(own_left, left_x)
    behind_2 = looks(own_right, right_2)
    behind_4 = looks(own_right, right_4)
    behind_a = looks(own_right, right_a)
    behind_x = looks(own_right, right_x)
    ahead = {
        1: jnp.where(even, ahead_x, ahead_a),
        2: ahead_2,
        3: jnp.where(even, ahead_a, ahead_x),
        4: ahead_4,
    }
    behind = {
        1: jnp.where(even, behind_a, behind_x),
        2: behind_2,
        3: jnp.where(even, behind_x, behind_a),
        4: behind_4,
    }
    full = {}
    for s in range(1, GAP + 1):
        right_of_ahead = conj(shifted(behind[s], "date", s))
        left_of_behind = conj(shifted(ahead[s], "date", -s))
        full[s] = jnp.concatenate([ahead[s], right_of_ahead], axis=2)
        full[-s] = jnp.concatenate([left_of_behind, behind[s]], axis=2)

    listed = partners[0]
    outputs = []
    for slot in range(PARTNERS):
        value = jnp.zeros_like(full[1])
        for step, block in full.items():
            value = jnp.where(listed[slot] == date + step, block, value)
        outputs.append(value)
    return jnp.stack(outputs)[None]


def solution(mesh):
    in_specs = (
        P("date", None, "az", None),
        P("date"),
        P("date"),
        P("date", "az"),
        P("date", "az"),
        P("date", None),
    )
    out_specs = P("date", None, None, "az", None)
    return jax.shard_map(shards, mesh=mesh, in_specs=in_specs, out_specs=out_specs, check_vma=False)
```

```python
import jax
import jax.numpy as jnp
from jax import lax
from jax.sharding import PartitionSpec as P
from jax.experimental import pallas as pl
from jax.experimental.pallas import tpu as pltpu

PARTNERS = 4
GAP = 4
OFFAZ = 12
OFFRG = 12
NFRAC = 64
LOOK_AZ = 20
LOOK_RG = 4


def padded_2(cells, sides, width):
    for axis, dim in sides:
        count = lax.axis_size(axis)
        ends = count - 1
        head = lax.slice_in_dim(cells, 0, width, axis=dim)
        tail = lax.slice_in_dim(cells, cells.shape[dim] - width, cells.shape[dim], axis=dim)
        cells = jnp.concatenate(
            [
                lax.ppermute(tail, axis, [(i, (i + 1) % count) for i in range(ends)]),
                cells,
                lax.ppermute(head, axis, [((i + 1) % count, i) for i in range(ends)]),
            ],
            axis=dim,
        )
    return cells


def shifted(block, axis, distance):
    count = lax.axis_size(axis)
    route = [(i + distance, i) for i in range(count) if 0 <= i + distance < count]
    return lax.ppermute(block, axis, route)


def swapped(block, axis):
    count = lax.axis_size(axis)
    return lax.ppermute(block, axis, [(i, i ^ 1) for i in range(count)])


def kernel_table():
    frac = jnp.arange(NFRAC, dtype=jnp.float32)[:, None] / NFRAC
    taps = jnp.arange(8, dtype=jnp.float32)[None, :]
    place = taps - 3.0 - frac
    return jnp.sinc(place) * (0.5 + 0.5 * jnp.cos(jnp.pi * place / 4.5))


def resample_block(padded, shift_lines, kern_lines, shift_range, kern_range):
    table = kernel_table()
    nlines = shift_range.shape[0]
    nrange = padded.shape[2]
    border = OFFAZ + 4
    start = border + shift_lines - 3
    window = lax.dynamic_slice_in_dim(padded, start, nlines + 7, 1)
    weights = table[kern_lines]
    along = jnp.zeros((2, nlines, nrange), jnp.float32)
    for tap in range(8):
        along = along + weights[tap] * window[:, tap : tap + nlines, :].astype(jnp.float32)
    margin = OFFRG + 4
    widened = jnp.pad(along, ((0, 0), (0, 0), (margin, margin)))
    selector = (kern_range[:, None] == jnp.arange(NFRAC, dtype=jnp.int32)[None, :]).astype(
        jnp.float32
    )
    range_weights = jnp.dot(selector, table, precision=lax.Precision.HIGHEST)
    targets = shift_range[:, None] + jnp.arange(8, dtype=jnp.int32)[None, :] - 3
    half = nrange // 2
    halves = []
    for first in (0, half):
        result = jnp.zeros((2, nlines, half), jnp.float32)
        for offset in range(-OFFRG - 3, OFFRG + 5):
            coeff = jnp.sum(jnp.where(targets == offset, range_weights, 0.0), axis=1)
            low = margin + first + offset
            result = result + coeff[None, :, None] * widened[:, :, low : low + half]
        halves.append(look_order(result.astype(jnp.bfloat16)))
    return halves


CHUNK = 512


def looks_kernel(first_ref, second_ref, out_ref):
    first_re = first_ref[0].astype(jnp.float32)
    first_im = first_ref[1].astype(jnp.float32)
    second_re = second_ref[0].astype(jnp.float32)
    second_im = second_ref[1].astype(jnp.float32)
    real_part = first_re * second_re + first_im * second_im
    imag_part = first_im * second_re - first_re * second_im
    rows = real_part.shape[0]
    groups = rows // LOOK_AZ
    real_lines = real_part.reshape(LOOK_AZ, groups, CHUNK).sum(axis=0)
    imag_lines = imag_part.reshape(LOOK_AZ, groups, CHUNK).sum(axis=0)
    pooling = (
        lax.broadcasted_iota(jnp.int32, (CHUNK, CHUNK // LOOK_RG), 0) // LOOK_RG
        == lax.broadcasted_iota(jnp.int32, (CHUNK, CHUNK // LOOK_RG), 1)
    ).astype(jnp.float32)
    real_looks = jnp.dot(real_lines, pooling, precision=lax.Precision.HIGHEST, preferred_element_type=jnp.float32)
    imag_looks = jnp.dot(imag_lines, pooling, precision=lax.Precision.HIGHEST, preferred_element_type=jnp.float32)
    out_ref[0] = real_looks / (LOOK_AZ * LOOK_RG)
    out_ref[1] = imag_looks / (LOOK_AZ * LOOK_RG)


def looks(first, second):
    nlines = first.shape[1]
    width = first.shape[2]
    groups = nlines // LOOK_AZ
    spec = pl.BlockSpec((2, nlines, CHUNK), lambda j: (0, 0, j))
    return pl.pallas_call(
        looks_kernel,
        grid=(width // CHUNK,),
        in_specs=[spec, spec],
        out_specs=pl.BlockSpec((2, groups, CHUNK // LOOK_RG), lambda j: (0, 0, j)),
        out_shape=jax.ShapeDtypeStruct((2, groups, width // LOOK_RG), jnp.float32),
    )(first, second)


def look_order(image):
    nlines = image.shape[1]
    groups = nlines // LOOK_AZ
    return image.reshape(2, groups, LOOK_AZ, image.shape[2]).transpose(0, 2, 1, 3).reshape(image.shape)


def conj(block):
    return jnp.stack([block[0], -block[1]])


def shards(slc, az_offset, az_kernel, rg_offset, rg_kernel, partners):
    padded = padded_2(slc, (("az", 2),), OFFAZ + 4)
    own_left, own_right = resample_block(padded[0], az_offset[0], az_kernel[0], rg_offset[0], rg_kernel[0])
    date = lax.axis_index("date")
    even = date % 2 == 0

    left_2 = shifted(own_left, "date", 2)
    left_1 = swapped(jnp.where(even, left_2, own_left), "date")
    left_4 = shifted(left_2, "date", 2)
    left_3 = shifted(left_1, "date", 2)
    right_2 = shifted(own_right, "date", -2)
    right_1 = swapped(jnp.where(even, own_right, right_2), "date")
    right_4 = shifted(right_2, "date", -2)
    right_3 = shifted(right_1, "date", -2)

    ahead = {
        1: looks(own_left, left_1),
        2: looks(own_left, left_2),
        3: looks(own_left, left_3),
        4: looks(own_left, left_4),
    }
    behind = {
        1: looks(own_right, right_1),
        2: looks(own_right, right_2),
        3: looks(own_right, right_3),
        4: looks(own_right, right_4),
    }
    full = {}
    for s in range(1, GAP + 1):
        right_of_ahead = conj(shifted(behind[s], "date", s))
        left_of_behind = conj(shifted(ahead[s], "date", -s))
        full[s] = jnp.concatenate([ahead[s], right_of_ahead], axis=2)
        full[-s] = jnp.concatenate([left_of_behind, behind[s]], axis=2)

    listed = partners[0]
    outputs = []
    for slot in range(PARTNERS):
        value = jnp.zeros_like(full[1])
        for step, block in full.items():
            value = jnp.where(listed[slot] == date + step, block, value)
        outputs.append(value)
    return jnp.stack(outputs)[None]


def solution(mesh):
    in_specs = (
        P("date", None, "az", None),
        P("date"),
        P("date"),
        P("date", "az"),
        P("date", "az"),
        P("date", None),
    )
    out_specs = P("date", None, None, "az", None)
    return jax.shard_map(shards, mesh=mesh, in_specs=in_specs, out_specs=out_specs, check_vma=False)
```

```python
import jax
import jax.numpy as jnp
from jax import lax
from jax.sharding import PartitionSpec as P
from jax.experimental import pallas as pl
from jax.experimental.pallas import tpu as pltpu

PARTNERS = 4
GAP = 4
OFFAZ = 12
OFFRG = 12
NFRAC = 64
LOOK_AZ = 20
LOOK_RG = 4


def padded_2(cells, sides, width):
    for axis, dim in sides:
        count = lax.axis_size(axis)
        ends = count - 1
        head = lax.slice_in_dim(cells, 0, width, axis=dim)
        tail = lax.slice_in_dim(cells, cells.shape[dim] - width, cells.shape[dim], axis=dim)
        cells = jnp.concatenate(
            [
                lax.ppermute(tail, axis, [(i, (i + 1) % count) for i in range(ends)]),
                cells,
                lax.ppermute(head, axis, [((i + 1) % count, i) for i in range(ends)]),
            ],
            axis=dim,
        )
    return cells


def shifted(block, axis, distance):
    count = lax.axis_size(axis)
    route = [(i + distance, i) for i in range(count) if 0 <= i + distance < count]
    return lax.ppermute(block, axis, route)


def swapped(block, axis):
    count = lax.axis_size(axis)
    return lax.ppermute(block, axis, [(i, i ^ 1) for i in range(count)])


def kernel_table():
    frac = jnp.arange(NFRAC, dtype=jnp.float32)[:, None] / NFRAC
    taps = jnp.arange(8, dtype=jnp.float32)[None, :]
    place = taps - 3.0 - frac
    return jnp.sinc(place) * (0.5 + 0.5 * jnp.cos(jnp.pi * place / 4.5))


ROWS = 16
EDGE = 128


def resample_kernel(weights_ref, window_ref, coeff_ref, shift_ref, out_ref):
    step = pl.program_id(1)
    first = pl.multiple_of(step * ROWS, ROWS)
    window = window_ref[0, pl.ds(first, ROWS + 8), :]
    along = weights_ref[0] * window[0:ROWS, :]
    for tap in range(1, 8):
        along = along + weights_ref[tap] * window[tap : tap + ROWS, :]
    nrange = along.shape[1]
    zeros = jnp.zeros((ROWS, EDGE), jnp.float32)
    row = jnp.concatenate([zeros, along, zeros], axis=1)
    width = row.shape[1]
    shift = shift_ref[...]
    for bit in range(5):
        moved = pltpu.roll(row, width - (1 << bit), 1)
        row = jnp.where(((shift >> bit) & 1) == 1, moved, row)
    coeff = coeff_ref[...]
    result = None
    for tap in range(8):
        moved = pltpu.roll(row, width - (EDGE - 15 + tap), 1)[:, :nrange]
        term = coeff[:, tap : tap + 1] * moved
        result = term if result is None else result + term
    out_ref[0] = result.astype(out_ref.dtype)


def resample_block(padded, shift_lines, kern_lines, shift_range, kern_range):
    table = kernel_table()
    nlines = shift_range.shape[0]
    nrange = padded.shape[2]
    border = OFFAZ + 4
    start = border + shift_lines - 3
    window = lax.dynamic_slice_in_dim(padded, start, nlines + 7, 1).astype(jnp.float32)
    window = jnp.pad(window, ((0, 0), (0, 1), (0, 0)))
    weights = table[kern_lines]
    coeff = jnp.take(table, kern_range, axis=0)
    shift = (shift_range + OFFRG)[:, None]
    out = pl.pallas_call(
        resample_kernel,
        grid=(2, nlines // ROWS),
        in_specs=[
            pl.BlockSpec(memory_space=pltpu.SMEM),
            pl.BlockSpec((1, nlines + 8, nrange), lambda c, t: (c, 0, 0)),
            pl.BlockSpec((ROWS, 8), lambda c, t: (t, 0)),
            pl.BlockSpec((ROWS, 1), lambda c, t: (t, 0)),
        ],
        out_specs=pl.BlockSpec((1, ROWS, nrange), lambda c, t: (c, t, 0)),
        out_shape=jax.ShapeDtypeStruct((2, nlines, nrange), jnp.bfloat16),
    )(weights, window, coeff, shift)
    half = nrange // 2
    return look_order(out[:, :, :half]), look_order(out[:, :, half:])


CHUNK = 512


def looks_kernel(first_ref, second_ref, out_ref):
    first_re = first_ref[0].astype(jnp.float32)
    first_im = first_ref[1].astype(jnp.float32)
    second_re = second_ref[0].astype(jnp.float32)
    second_im = second_ref[1].astype(jnp.float32)
    real_part = first_re * second_re + first_im * second_im
    imag_part = first_im * second_re - first_re * second_im
    rows = real_part.shape[0]
    groups = rows // LOOK_AZ
    real_lines = real_part.reshape(LOOK_AZ, groups, CHUNK).sum(axis=0)
    imag_lines = imag_part.reshape(LOOK_AZ, groups, CHUNK).sum(axis=0)
    pooling = (
        lax.broadcasted_iota(jnp.int32, (CHUNK, CHUNK // LOOK_RG), 0) // LOOK_RG
        == lax.broadcasted_iota(jnp.int32, (CHUNK, CHUNK // LOOK_RG), 1)
    ).astype(jnp.float32)
    real_looks = jnp.dot(real_lines, pooling, precision=lax.Precision.HIGHEST, preferred_element_type=jnp.float32)
    imag_looks = jnp.dot(imag_lines, pooling, precision=lax.Precision.HIGHEST, preferred_element_type=jnp.float32)
    out_ref[0] = real_looks / (LOOK_AZ * LOOK_RG)
    out_ref[1] = imag_looks / (LOOK_AZ * LOOK_RG)


def looks(first, second):
    nlines = first.shape[1]
    width = first.shape[2]
    groups = nlines // LOOK_AZ
    spec = pl.BlockSpec((2, nlines, CHUNK), lambda j: (0, 0, j))
    return pl.pallas_call(
        looks_kernel,
        grid=(width // CHUNK,),
        in_specs=[spec, spec],
        out_specs=pl.BlockSpec((2, groups, CHUNK // LOOK_RG), lambda j: (0, 0, j)),
        out_shape=jax.ShapeDtypeStruct((2, groups, width // LOOK_RG), jnp.float32),
    )(first, second)


def look_order(image):
    nlines = image.shape[1]
    groups = nlines // LOOK_AZ
    return image.reshape(2, groups, LOOK_AZ, image.shape[2]).transpose(0, 2, 1, 3).reshape(image.shape)


def conj(block):
    return jnp.stack([block[0], -block[1]])


def shards(slc, az_offset, az_kernel, rg_offset, rg_kernel, partners):
    padded = padded_2(slc, (("az", 2),), OFFAZ + 4)
    own_left, own_right = resample_block(padded[0], az_offset[0], az_kernel[0], rg_offset[0], rg_kernel[0])
    date = lax.axis_index("date")
    even = date % 2 == 0

    left_2 = shifted(own_left, "date", 2)
    left_1 = swapped(jnp.where(even, left_2, own_left), "date")
    left_4 = shifted(left_2, "date", 2)
    left_3 = shifted(left_1, "date", 2)
    right_2 = shifted(own_right, "date", -2)
    right_1 = swapped(jnp.where(even, own_right, right_2), "date")
    right_4 = shifted(right_2, "date", -2)
    right_3 = shifted(right_1, "date", -2)

    ahead = {
        1: looks(own_left, left_1),
        2: looks(own_left, left_2),
        3: looks(own_left, left_3),
        4: looks(own_left, left_4),
    }
    behind = {
        1: looks(own_right, right_1),
        2: looks(own_right, right_2),
        3: looks(own_right, right_3),
        4: looks(own_right, right_4),
    }
    full = {}
    for s in range(1, GAP + 1):
        right_of_ahead = conj(shifted(behind[s], "date", s))
        left_of_behind = conj(shifted(ahead[s], "date", -s))
        full[s] = jnp.concatenate([ahead[s], right_of_ahead], axis=2)
        full[-s] = jnp.concatenate([left_of_behind, behind[s]], axis=2)

    listed = partners[0]
    outputs = []
    for slot in range(PARTNERS):
        value = jnp.zeros_like(full[1])
        for step, block in full.items():
            value = jnp.where(listed[slot] == date + step, block, value)
        outputs.append(value)
    return jnp.stack(outputs)[None]


def solution(mesh):
    in_specs = (
        P("date", None, "az", None),
        P("date"),
        P("date"),
        P("date", "az"),
        P("date", "az"),
        P("date", None),
    )
    out_specs = P("date", None, None, "az", None)
    return jax.shard_map(shards, mesh=mesh, in_specs=in_specs, out_specs=out_specs, check_vma=False)
```

```python
import functools

import jax
import jax.numpy as jnp
from jax import lax
from jax.sharding import PartitionSpec as P
from jax.experimental import pallas as pl
from jax.experimental.pallas import tpu as pltpu

PARTNERS = 4
GAP = 4
OFFAZ = 12
OFFRG = 12
NFRAC = 64
LOOK_AZ = 20
LOOK_RG = 4


def padded_2(cells, sides, width):
    for axis, dim in sides:
        count = lax.axis_size(axis)
        ends = count - 1
        head = lax.slice_in_dim(cells, 0, width, axis=dim)
        tail = lax.slice_in_dim(cells, cells.shape[dim] - width, cells.shape[dim], axis=dim)
        cells = jnp.concatenate(
            [
                lax.ppermute(tail, axis, [(i, (i + 1) % count) for i in range(ends)]),
                cells,
                lax.ppermute(head, axis, [((i + 1) % count, i) for i in range(ends)]),
            ],
            axis=dim,
        )
    return cells


def shifted(block, axis, distance):
    count = lax.axis_size(axis)
    route = [(i + distance, i) for i in range(count) if 0 <= i + distance < count]
    return lax.ppermute(block, axis, route)


def swapped(block, axis):
    count = lax.axis_size(axis)
    return lax.ppermute(block, axis, [(i, i ^ 1) for i in range(count)])


def kernel_table():
    frac = jnp.arange(NFRAC, dtype=jnp.float32)[:, None] / NFRAC
    taps = jnp.arange(8, dtype=jnp.float32)[None, :]
    place = taps - 3.0 - frac
    return jnp.sinc(place) * (0.5 + 0.5 * jnp.cos(jnp.pi * place / 4.5))


ROWS = 16
EDGE = 128
PIECE = 512
SPAN = 768


def resample_kernel(side, weights_ref, window_ref, coeff_ref, shift_ref, out_ref, row_ref):
    step = pl.program_id(0)
    first = pl.multiple_of(step * ROWS, ROWS)
    half = out_ref.shape[2]
    width = row_ref.shape[2]
    if side == 0:
        row_ref[:, :, 0:EDGE] = jnp.zeros((2, ROWS, EDGE), jnp.float32)
        lo, hi, src = EDGE, width, 0
    else:
        row_ref[:, :, width - EDGE : width] = jnp.zeros((2, ROWS, EDGE), jnp.float32)
        lo, hi, src = 0, width - EDGE, half - EDGE
    for comp in range(2):
        for j in range(lo, hi, 256):
            take = min(256, hi - j)
            window = window_ref[comp, pl.ds(first, ROWS + 8), src + j - lo : src + j - lo + take]
            along = weights_ref[0] * window[0:ROWS, :]
            for tap in range(1, 8):
                along = along + weights_ref[tap] * window[tap : tap + ROWS, :]
            row_ref[comp, :, j : j + take] = along
    shift = shift_ref[...]
    bits = [((shift >> bit) & 1) == 1 for bit in range(5)]
    coeff = coeff_ref[...]
    for comp in range(2):
        for piece in range(0, half, PIECE):
            row = row_ref[comp, :, piece : piece + SPAN]
            for bit in range(5):
                moved = pltpu.roll(row, SPAN - (1 << bit), 1)
                row = jnp.where(bits[bit], moved, row)
            result = None
            for tap in range(8):
                moved = pltpu.roll(row, SPAN - (EDGE - 15 + tap), 1)[:, :PIECE]
                term = coeff[:, tap : tap + 1] * moved
                result = term if result is None else result + term
            out_ref[comp, :, piece : piece + PIECE] = result.astype(out_ref.dtype)


def resample_half(side, weights, window, coeff, shift):
    nlines = coeff.shape[0]
    half = window.shape[2] // 2
    return pl.pallas_call(
        functools.partial(resample_kernel, side),
        grid=(nlines // ROWS,),
        in_specs=[
            pl.BlockSpec(memory_space=pltpu.SMEM),
            pl.BlockSpec(window.shape, lambda t: (0, 0, 0)),
            pl.BlockSpec((ROWS, 8), lambda t: (t, 0)),
            pl.BlockSpec((ROWS, 1), lambda t: (t, 0)),
        ],
        out_specs=pl.BlockSpec((2, ROWS, half), lambda t: (0, t, 0)),
        out_shape=jax.ShapeDtypeStruct((2, nlines, half), jnp.bfloat16),
        scratch_shapes=[pltpu.VMEM((2, ROWS, half + 2 * EDGE), jnp.float32)],
    )(weights, window, coeff, shift)


def resample_block(padded, shift_lines, kern_lines, shift_range, kern_range):
    table = kernel_table()
    nlines = shift_range.shape[0]
    border = OFFAZ + 4
    start = border + shift_lines - 3
    window = lax.dynamic_slice_in_dim(padded, start, nlines + 7, 1).astype(jnp.float32)
    window = jnp.pad(window, ((0, 0), (0, 1), (0, 0)))
    weights = table[kern_lines]
    coeff = jnp.take(table, kern_range, axis=0)
    shift = (shift_range + OFFRG)[:, None]
    left = resample_half(0, weights, window, coeff, shift)
    right = resample_half(1, weights, window, coeff, shift)
    return look_order(left), look_order(right)


CHUNK = 512


def looks_kernel(first_ref, second_ref, out_ref):
    first_re = first_ref[0].astype(jnp.float32)
    first_im = first_ref[1].astype(jnp.float32)
    second_re = second_ref[0].astype(jnp.float32)
    second_im = second_ref[1].astype(jnp.float32)
    real_part = first_re * second_re + first_im * second_im
    imag_part = first_im * second_re - first_re * second_im
    rows = real_part.shape[0]
    groups = rows // LOOK_AZ
    real_lines = real_part.reshape(LOOK_AZ, groups, CHUNK).sum(axis=0)
    imag_lines = imag_part.reshape(LOOK_AZ, groups, CHUNK).sum(axis=0)
    pooling = (
        lax.broadcasted_iota(jnp.int32, (CHUNK, CHUNK // LOOK_RG), 0) // LOOK_RG
        == lax.broadcasted_iota(jnp.int32, (CHUNK, CHUNK // LOOK_RG), 1)
    ).astype(jnp.float32)
    real_looks = jnp.dot(real_lines, pooling, precision=lax.Precision.HIGHEST, preferred_element_type=jnp.float32)
    imag_looks = jnp.dot(imag_lines, pooling, precision=lax.Precision.HIGHEST, preferred_element_type=jnp.float32)
    out_ref[0] = real_looks / (LOOK_AZ * LOOK_RG)
    out_ref[1] = imag_looks / (LOOK_AZ * LOOK_RG)


def looks(first, second):
    nlines = first.shape[1]
    width = first.shape[2]
    groups = nlines // LOOK_AZ
    spec = pl.BlockSpec((2, nlines, CHUNK), lambda j: (0, 0, j))
    return pl.pallas_call(
        looks_kernel,
        grid=(width // CHUNK,),
        in_specs=[spec, spec],
        out_specs=pl.BlockSpec((2, groups, CHUNK // LOOK_RG), lambda j: (0, 0, j)),
        out_shape=jax.ShapeDtypeStruct((2, groups, width // LOOK_RG), jnp.float32),
    )(first, second)


def look_order(image):
    nlines = image.shape[1]
    groups = nlines // LOOK_AZ
    return image.reshape(2, groups, LOOK_AZ, image.shape[2]).transpose(0, 2, 1, 3).reshape(image.shape)


def conj(block):
    return jnp.stack([block[0], -block[1]])


def shards(slc, az_offset, az_kernel, rg_offset, rg_kernel, partners):
    padded = padded_2(slc, (("az", 2),), OFFAZ + 4)
    own_left, own_right = resample_block(padded[0], az_offset[0], az_kernel[0], rg_offset[0], rg_kernel[0])
    date = lax.axis_index("date")
    even = date % 2 == 0

    left_2 = shifted(own_left, "date", 2)
    left_1 = swapped(jnp.where(even, left_2, own_left), "date")
    left_4 = shifted(left_2, "date", 2)
    left_3 = shifted(left_1, "date", 2)
    right_2 = shifted(own_right, "date", -2)
    right_1 = swapped(jnp.where(even, own_right, right_2), "date")
    right_4 = shifted(right_2, "date", -2)
    right_3 = shifted(right_1, "date", -2)

    ahead = {
        1: looks(own_left, left_1),
        2: looks(own_left, left_2),
        3: looks(own_left, left_3),
        4: looks(own_left, left_4),
    }
    behind = {
        1: looks(own_right, right_1),
        2: looks(own_right, right_2),
        3: looks(own_right, right_3),
        4: looks(own_right, right_4),
    }
    full = {}
    for s in range(1, GAP + 1):
        right_of_ahead = conj(shifted(behind[s], "date", s))
        left_of_behind = conj(shifted(ahead[s], "date", -s))
        full[s] = jnp.concatenate([ahead[s], right_of_ahead], axis=2)
        full[-s] = jnp.concatenate([left_of_behind, behind[s]], axis=2)

    listed = partners[0]
    outputs = []
    for slot in range(PARTNERS):
        value = jnp.zeros_like(full[1])
        for step, block in full.items():
            value = jnp.where(listed[slot] == date + step, block, value)
        outputs.append(value)
    return jnp.stack(outputs)[None]


def solution(mesh):
    in_specs = (
        P("date", None, "az", None),
        P("date"),
        P("date"),
        P("date", "az"),
        P("date", "az"),
        P("date", None),
    )
    out_specs = P("date", None, None, "az", None)
    return jax.shard_map(shards, mesh=mesh, in_specs=in_specs, out_specs=out_specs, check_vma=False)
```

```python
import functools

import jax
import jax.numpy as jnp
from jax import lax
from jax.sharding import PartitionSpec as P
from jax.experimental import pallas as pl
from jax.experimental.pallas import tpu as pltpu

PARTNERS = 4
GAP = 4
OFFAZ = 12
OFFRG = 12
NFRAC = 64
LOOK_AZ = 20
LOOK_RG = 4


def padded_2(cells, sides, width):
    for axis, dim in sides:
        count = lax.axis_size(axis)
        ends = count - 1
        head = lax.slice_in_dim(cells, 0, width, axis=dim)
        tail = lax.slice_in_dim(cells, cells.shape[dim] - width, cells.shape[dim], axis=dim)
        cells = jnp.concatenate(
            [
                lax.ppermute(tail, axis, [(i, (i + 1) % count) for i in range(ends)]),
                cells,
                lax.ppermute(head, axis, [((i + 1) % count, i) for i in range(ends)]),
            ],
            axis=dim,
        )
    return cells


def shifted(block, axis, distance):
    count = lax.axis_size(axis)
    route = [(i + distance, i) for i in range(count) if 0 <= i + distance < count]
    return lax.ppermute(block, axis, route)


def swapped(block, axis):
    count = lax.axis_size(axis)
    return lax.ppermute(block, axis, [(i, i ^ 1) for i in range(count)])


def kernel_table():
    frac = jnp.arange(NFRAC, dtype=jnp.float32)[:, None] / NFRAC
    taps = jnp.arange(8, dtype=jnp.float32)[None, :]
    place = taps - 3.0 - frac
    return jnp.sinc(place) * (0.5 + 0.5 * jnp.cos(jnp.pi * place / 4.5))


ROWS = 16
EDGE = 128
PIECES = 2


def resample_kernel(side, weights_ref, window_ref, coeff_ref, shift_ref, out_ref):
    step = pl.program_id(1)
    first = pl.multiple_of(step * ROWS, ROWS)
    half = out_ref.shape[2]
    low = max(side * half - EDGE, 0)
    high = min(side * half + half + EDGE, window_ref.shape[2])
    window = window_ref[0, pl.ds(first, ROWS + 8), low:high]
    along = weights_ref[0] * window[0:ROWS, :]
    for tap in range(1, 8):
        along = along + weights_ref[tap] * window[tap : tap + ROWS, :]
    zeros = jnp.zeros((ROWS, EDGE), jnp.float32)
    row = jnp.concatenate([zeros, along] if side == 0 else [along, zeros], axis=1)
    width = row.shape[1]
    shift = shift_ref[...]
    for bit in range(5):
        moved = pltpu.roll(row, width - (1 << bit), 1)
        row = jnp.where(((shift >> bit) & 1) == 1, moved, row)
    coeff = coeff_ref[...]
    result = None
    for tap in range(8):
        moved = pltpu.roll(row, width - (EDGE - 15 + tap), 1)[:, :half]
        term = coeff[:, tap : tap + 1] * moved
        result = term if result is None else result + term
    out_ref[0] = result.astype(out_ref.dtype)


def resample_half(side, weights, window, coeff, shift):
    nlines = coeff.shape[0]
    half = window.shape[2] // 2
    return pl.pallas_call(
        functools.partial(resample_kernel, side),
        grid=(2, nlines // ROWS),
        in_specs=[
            pl.BlockSpec(memory_space=pltpu.SMEM),
            pl.BlockSpec((1,) + window.shape[1:], lambda c, t: (c, 0, 0)),
            pl.BlockSpec((ROWS, 8), lambda c, t: (t, 0)),
            pl.BlockSpec((ROWS, 1), lambda c, t: (t, 0)),
        ],
        out_specs=pl.BlockSpec((1, ROWS, half), lambda c, t: (c, t, 0)),
        out_shape=jax.ShapeDtypeStruct((2, nlines, half), jnp.bfloat16),
    )(weights, window, coeff, shift)


def resample_block(padded, shift_lines, kern_lines, shift_range, kern_range):
    table = kernel_table()
    nlines = shift_range.shape[0]
    border = OFFAZ + 4
    start = border + shift_lines - 3
    window = lax.dynamic_slice_in_dim(padded, start, nlines + 7, 1).astype(jnp.float32)
    window = jnp.pad(window, ((0, 0), (0, 1), (0, 0)))
    weights = table[kern_lines]
    coeff = jnp.take(table, kern_range, axis=0)
    shift = (shift_range + OFFRG)[:, None]
    halves = []
    for side in range(2):
        ordered = look_order(resample_half(side, weights, window, coeff, shift))
        width = ordered.shape[2] // PIECES
        halves.append([ordered[:, :, p * width : (p + 1) * width] for p in range(PIECES)])
    return halves


CHUNK = 512


def looks_kernel(first_ref, second_ref, out_ref):
    first_re = first_ref[0].astype(jnp.float32)
    first_im = first_ref[1].astype(jnp.float32)
    second_re = second_ref[0].astype(jnp.float32)
    second_im = second_ref[1].astype(jnp.float32)
    real_part = first_re * second_re + first_im * second_im
    imag_part = first_im * second_re - first_re * second_im
    rows = real_part.shape[0]
    groups = rows // LOOK_AZ
    real_lines = real_part.reshape(LOOK_AZ, groups, CHUNK).sum(axis=0)
    imag_lines = imag_part.reshape(LOOK_AZ, groups, CHUNK).sum(axis=0)
    pooling = (
        lax.broadcasted_iota(jnp.int32, (CHUNK, CHUNK // LOOK_RG), 0) // LOOK_RG
        == lax.broadcasted_iota(jnp.int32, (CHUNK, CHUNK // LOOK_RG), 1)
    ).astype(jnp.float32)
    real_looks = jnp.dot(real_lines, pooling, precision=lax.Precision.HIGHEST, preferred_element_type=jnp.float32)
    imag_looks = jnp.dot(imag_lines, pooling, precision=lax.Precision.HIGHEST, preferred_element_type=jnp.float32)
    out_ref[0] = real_looks / (LOOK_AZ * LOOK_RG)
    out_ref[1] = imag_looks / (LOOK_AZ * LOOK_RG)


def looks(first, second):
    nlines = first.shape[1]
    width = first.shape[2]
    groups = nlines // LOOK_AZ
    spec = pl.BlockSpec((2, nlines, CHUNK), lambda j: (0, 0, j))
    return pl.pallas_call(
        looks_kernel,
        grid=(width // CHUNK,),
        in_specs=[spec, spec],
        out_specs=pl.BlockSpec((2, groups, CHUNK // LOOK_RG), lambda j: (0, 0, j)),
        out_shape=jax.ShapeDtypeStruct((2, groups, width // LOOK_RG), jnp.float32),
    )(first, second)


def look_order(image):
    nlines = image.shape[1]
    groups = nlines // LOOK_AZ
    return image.reshape(2, groups, LOOK_AZ, image.shape[2]).transpose(0, 2, 1, 3).reshape(image.shape)


def conj(block):
    return jnp.stack([block[0], -block[1]])


def shards(slc, az_offset, az_kernel, rg_offset, rg_kernel, partners):
    padded = padded_2(slc, (("az", 2),), OFFAZ + 4)
    own_left, own_right = resample_block(padded[0], az_offset[0], az_kernel[0], rg_offset[0], rg_kernel[0])
    date = lax.axis_index("date")
    even = date % 2 == 0
    ahead_parts = {s: [] for s in range(1, GAP + 1)}
    behind_parts = {s: [] for s in range(1, GAP + 1)}
    for piece in range(PIECES):
        own = own_left[piece]
        left_2 = shifted(own, "date", 2)
        left_1 = swapped(jnp.where(even, left_2, own), "date")
        left_4 = shifted(left_2, "date", 2)
        left_3 = shifted(left_1, "date", 2)
        for s, other in ((2, left_2), (1, left_1), (4, left_4), (3, left_3)):
            ahead_parts[s].append(looks(own, other))
        own = own_right[piece]
        right_2 = shifted(own, "date", -2)
        right_1 = swapped(jnp.where(even, own, right_2), "date")
        right_4 = shifted(right_2, "date", -2)
        right_3 = shifted(right_1, "date", -2)
        for s, other in ((2, right_2), (1, right_1), (4, right_4), (3, right_3)):
            behind_parts[s].append(looks(own, other))
    ahead = {s: jnp.concatenate(parts, axis=2) for s, parts in ahead_parts.items()}
    behind = {s: jnp.concatenate(parts, axis=2) for s, parts in behind_parts.items()}
    full = {}
    for s in range(1, GAP + 1):
        right_of_ahead = conj(shifted(behind[s], "date", s))
        left_of_behind = conj(shifted(ahead[s], "date", -s))
        full[s] = jnp.concatenate([ahead[s], right_of_ahead], axis=2)
        full[-s] = jnp.concatenate([left_of_behind, behind[s]], axis=2)

    listed = partners[0]
    outputs = []
    for slot in range(PARTNERS):
        value = jnp.zeros_like(full[1])
        for step, block in full.items():
            value = jnp.where(listed[slot] == date + step, block, value)
        outputs.append(value)
    return jnp.stack(outputs)[None]


def solution(mesh):
    in_specs = (
        P("date", None, "az", None),
        P("date"),
        P("date"),
        P("date", "az"),
        P("date", "az"),
        P("date", None),
    )
    out_specs = P("date", None, None, "az", None)
    return jax.shard_map(shards, mesh=mesh, in_specs=in_specs, out_specs=out_specs, check_vma=False)
```

```python
import jax
import jax.numpy as jnp
from jax import lax
from jax.sharding import PartitionSpec as P
from jax.experimental import pallas as pl
from jax.experimental.pallas import tpu as pltpu

PARTNERS = 4
GAP = 4
OFFAZ = 12
OFFRG = 12
NFRAC = 64
LOOK_AZ = 20
LOOK_RG = 4


def padded_2(cells, sides, width):
    for axis, dim in sides:
        count = lax.axis_size(axis)
        ends = count - 1
        head = lax.slice_in_dim(cells, 0, width, axis=dim)
        tail = lax.slice_in_dim(cells, cells.shape[dim] - width, cells.shape[dim], axis=dim)
        cells = jnp.concatenate(
            [
                lax.ppermute(tail, axis, [(i, (i + 1) % count) for i in range(ends)]),
                cells,
                lax.ppermute(head, axis, [((i + 1) % count, i) for i in range(ends)]),
            ],
            axis=dim,
        )
    return cells


def routed(block, axis, distance, keep):
    count = lax.axis_size(axis)
    route = [(i + distance, i) for i in range(count) if 0 <= i + distance < count and keep(i, count)]
    return lax.ppermute(block, axis, route)


def shifted(block, axis, distance):
    return routed(block, axis, distance, lambda i, count: True)


def kernel_table():
    frac = jnp.arange(NFRAC, dtype=jnp.float32)[:, None] / NFRAC
    taps = jnp.arange(8, dtype=jnp.float32)[None, :]
    place = taps - 3.0 - frac
    return jnp.sinc(place) * (0.5 + 0.5 * jnp.cos(jnp.pi * place / 4.5))


ROWS = 16
EDGE = 128


def resample_kernel(weights_ref, window_ref, coeff_ref, shift_ref, out_ref):
    step = pl.program_id(1)
    first = pl.multiple_of(step * ROWS, ROWS)
    window = window_ref[0, pl.ds(first, ROWS + 8), :]
    along = weights_ref[0] * window[0:ROWS, :]
    for tap in range(1, 8):
        along = along + weights_ref[tap] * window[tap : tap + ROWS, :]
    nrange = along.shape[1]
    zeros = jnp.zeros((ROWS, EDGE), jnp.float32)
    row = jnp.concatenate([zeros, along, zeros], axis=1)
    width = row.shape[1]
    shift = shift_ref[...]
    for bit in range(5):
        moved = pltpu.roll(row, width - (1 << bit), 1)
        row = jnp.where(((shift >> bit) & 1) == 1, moved, row)
    coeff = coeff_ref[...]
    result = None
    for tap in range(8):
        moved = pltpu.roll(row, width - (EDGE - 15 + tap), 1)[:, :nrange]
        term = coeff[:, tap : tap + 1] * moved
        result = term if result is None else result + term
    out_ref[0] = result.astype(out_ref.dtype)


def resample_block(padded, shift_lines, kern_lines, shift_range, kern_range):
    table = kernel_table()
    nlines = shift_range.shape[0]
    nrange = padded.shape[2]
    border = OFFAZ + 4
    start = border + shift_lines - 3
    window = lax.dynamic_slice_in_dim(padded, start, nlines + 7, 1).astype(jnp.float32)
    window = jnp.pad(window, ((0, 0), (0, 1), (0, 0)))
    weights = table[kern_lines]
    coeff = jnp.take(table, kern_range, axis=0)
    shift = (shift_range + OFFRG)[:, None]
    out = pl.pallas_call(
        resample_kernel,
        grid=(2, nlines // ROWS),
        in_specs=[
            pl.BlockSpec(memory_space=pltpu.SMEM),
            pl.BlockSpec((1, nlines + 8, nrange), lambda c, t: (c, 0, 0)),
            pl.BlockSpec((ROWS, 8), lambda c, t: (t, 0)),
            pl.BlockSpec((ROWS, 1), lambda c, t: (t, 0)),
        ],
        out_specs=pl.BlockSpec((1, ROWS, nrange), lambda c, t: (c, t, 0)),
        out_shape=jax.ShapeDtypeStruct((2, nlines, nrange), jnp.bfloat16),
    )(weights, window, coeff, shift)
    half = nrange // 2
    return look_order(out[:, :, :half]), look_order(out[:, :, half:])


CHUNK = 512


def looks_kernel(first_ref, second_ref, out_ref):
    first_re = first_ref[0].astype(jnp.float32)
    first_im = first_ref[1].astype(jnp.float32)
    second_re = second_ref[0].astype(jnp.float32)
    second_im = second_ref[1].astype(jnp.float32)
    real_part = first_re * second_re + first_im * second_im
    imag_part = first_im * second_re - first_re * second_im
    rows = real_part.shape[0]
    groups = rows // LOOK_AZ
    real_lines = real_part.reshape(LOOK_AZ, groups, CHUNK).sum(axis=0)
    imag_lines = imag_part.reshape(LOOK_AZ, groups, CHUNK).sum(axis=0)
    pooling = (
        lax.broadcasted_iota(jnp.int32, (CHUNK, CHUNK // LOOK_RG), 0) // LOOK_RG
        == lax.broadcasted_iota(jnp.int32, (CHUNK, CHUNK // LOOK_RG), 1)
    ).astype(jnp.float32)
    real_looks = jnp.dot(real_lines, pooling, precision=lax.Precision.HIGHEST, preferred_element_type=jnp.float32)
    imag_looks = jnp.dot(imag_lines, pooling, precision=lax.Precision.HIGHEST, preferred_element_type=jnp.float32)
    out_ref[0] = real_looks / (LOOK_AZ * LOOK_RG)
    out_ref[1] = imag_looks / (LOOK_AZ * LOOK_RG)


def looks(first, second):
    nlines = first.shape[1]
    width = first.shape[2]
    groups = nlines // LOOK_AZ
    spec = pl.BlockSpec((2, nlines, CHUNK), lambda j: (0, 0, j))
    return pl.pallas_call(
        looks_kernel,
        grid=(width // CHUNK,),
        in_specs=[spec, spec],
        out_specs=pl.BlockSpec((2, groups, CHUNK // LOOK_RG), lambda j: (0, 0, j)),
        out_shape=jax.ShapeDtypeStruct((2, groups, width // LOOK_RG), jnp.float32),
    )(first, second)


def look_order(image):
    nlines = image.shape[1]
    groups = nlines // LOOK_AZ
    return image.reshape(2, groups, LOOK_AZ, image.shape[2]).transpose(0, 2, 1, 3).reshape(image.shape)


def conj(block):
    return jnp.stack([block[0], -block[1]])


def shards(slc, az_offset, az_kernel, rg_offset, rg_kernel, partners):
    padded = padded_2(slc, (("az", 2),), OFFAZ + 4)
    own_left, own_right = resample_block(padded[0], az_offset[0], az_kernel[0], rg_offset[0], rg_kernel[0])
    date = lax.axis_index("date")
    even = date % 2 == 0

    left_2 = routed(own_left, "date", 2, lambda i, n: True)
    left_4 = routed(left_2, "date", 2, lambda i, n: i + 4 < n)
    left_1_even = routed(own_left, "date", 1, lambda i, n: i % 2 == 0)
    left_1_odd = routed(left_2, "date", -1, lambda i, n: i % 2 == 1 and i + 1 < n)
    left_3_even = routed(left_1_even, "date", 2, lambda i, n: i % 2 == 0 and i + 3 < n)
    left_3_odd = routed(left_1_odd, "date", 2, lambda i, n: i % 2 == 1 and i + 3 < n)
    left_1 = jnp.where(even, left_1_even, left_1_odd)
    left_3 = jnp.where(even, left_3_even, left_3_odd)
    right_2 = routed(own_right, "date", -2, lambda i, n: True)
    right_4 = routed(right_2, "date", -2, lambda i, n: i >= 4)
    right_1_odd = routed(own_right, "date", -1, lambda i, n: i % 2 == 1)
    right_1_even = routed(right_2, "date", 1, lambda i, n: i % 2 == 0 and i >= 1)
    right_3_odd = routed(right_1_odd, "date", -2, lambda i, n: i % 2 == 1 and i >= 3)
    right_3_even = routed(right_1_even, "date", -2, lambda i, n: i % 2 == 0 and i >= 3)
    right_1 = jnp.where(even, right_1_even, right_1_odd)
    right_3 = jnp.where(even, right_3_even, right_3_odd)

    ahead = {
        1: looks(own_left, left_1),
        2: looks(own_left, left_2),
        3: looks(own_left, left_3),
        4: looks(own_left, left_4),
    }
    behind = {
        1: looks(own_right, right_1),
        2: looks(own_right, right_2),
        3: looks(own_right, right_3),
        4: looks(own_right, right_4),
    }
    full = {}
    for s in range(1, GAP + 1):
        right_of_ahead = conj(shifted(behind[s], "date", s))
        left_of_behind = conj(shifted(ahead[s], "date", -s))
        full[s] = jnp.concatenate([ahead[s], right_of_ahead], axis=2)
        full[-s] = jnp.concatenate([left_of_behind, behind[s]], axis=2)

    listed = partners[0]
    outputs = []
    for slot in range(PARTNERS):
        value = jnp.zeros_like(full[1])
        for step, block in full.items():
            value = jnp.where(listed[slot] == date + step, block, value)
        outputs.append(value)
    return jnp.stack(outputs)[None]


def solution(mesh):
    in_specs = (
        P("date", None, "az", None),
        P("date"),
        P("date"),
        P("date", "az"),
        P("date", "az"),
        P("date", None),
    )
    out_specs = P("date", None, None, "az", None)
    return jax.shard_map(shards, mesh=mesh, in_specs=in_specs, out_specs=out_specs, check_vma=False)
```

```python
import jax
import jax.numpy as jnp
from jax import lax
from jax.sharding import PartitionSpec as P
from jax.experimental import pallas as pl
from jax.experimental.pallas import tpu as pltpu

PARTNERS = 4
GAP = 4
OFFAZ = 12
OFFRG = 12
NFRAC = 64
LOOK_AZ = 20
LOOK_RG = 4


def padded_2(cells, sides, width):
    for axis, dim in sides:
        count = lax.axis_size(axis)
        ends = count - 1
        head = lax.slice_in_dim(cells, 0, width, axis=dim)
        tail = lax.slice_in_dim(cells, cells.shape[dim] - width, cells.shape[dim], axis=dim)
        cells = jnp.concatenate(
            [
                lax.ppermute(tail, axis, [(i, (i + 1) % count) for i in range(ends)]),
                cells,
                lax.ppermute(head, axis, [((i + 1) % count, i) for i in range(ends)]),
            ],
            axis=dim,
        )
    return cells


def shifted(block, axis, distance):
    count = lax.axis_size(axis)
    route = [(i + distance, i) for i in range(count) if 0 <= i + distance < count]
    return lax.ppermute(block, axis, route)


def swapped(block, axis):
    count = lax.axis_size(axis)
    return lax.ppermute(block, axis, [(i, i ^ 1) for i in range(count)])


def kernel_table():
    frac = jnp.arange(NFRAC, dtype=jnp.float32)[:, None] / NFRAC
    taps = jnp.arange(8, dtype=jnp.float32)[None, :]
    place = taps - 3.0 - frac
    return jnp.sinc(place) * (0.5 + 0.5 * jnp.cos(jnp.pi * place / 4.5))


ROWS = 16
EDGE = 128


def resample_kernel(weights_ref, window_ref, coeff_ref, shift_ref, out_ref):
    step = pl.program_id(1)
    first = pl.multiple_of(step * ROWS, ROWS)
    window = window_ref[0, pl.ds(first, ROWS + 8), :]
    along = weights_ref[0] * window[0:ROWS, :]
    for tap in range(1, 8):
        along = along + weights_ref[tap] * window[tap : tap + ROWS, :]
    nrange = along.shape[1]
    zeros = jnp.zeros((ROWS, EDGE), jnp.float32)
    row = jnp.concatenate([zeros, along, zeros], axis=1)
    width = row.shape[1]
    shift = shift_ref[...]
    for bit in range(5):
        moved = pltpu.roll(row, width - (1 << bit), 1)
        row = jnp.where(((shift >> bit) & 1) == 1, moved, row)
    coeff = coeff_ref[...]
    result = None
    for tap in range(8):
        moved = pltpu.roll(row, width - (EDGE - 15 + tap), 1)[:, :nrange]
        term = coeff[:, tap : tap + 1] * moved
        result = term if result is None else result + term
    out_ref[0] = result.astype(out_ref.dtype)


def resample_block(padded, shift_lines, kern_lines, shift_range, kern_range):
    table = kernel_table()
    nlines = shift_range.shape[0]
    nrange = padded.shape[2]
    border = OFFAZ + 4
    start = border + shift_lines - 3
    window = lax.dynamic_slice_in_dim(padded, start, nlines + 7, 1).astype(jnp.float32)
    window = jnp.pad(window, ((0, 0), (0, 1), (0, 0)))
    weights = table[kern_lines]
    coeff = jnp.take(table, kern_range, axis=0)
    shift = (shift_range + OFFRG)[:, None]
    out = pl.pallas_call(
        resample_kernel,
        grid=(2, nlines // ROWS),
        in_specs=[
            pl.BlockSpec(memory_space=pltpu.SMEM),
            pl.BlockSpec((1, nlines + 8, nrange), lambda c, t: (c, 0, 0)),
            pl.BlockSpec((ROWS, 8), lambda c, t: (t, 0)),
            pl.BlockSpec((ROWS, 1), lambda c, t: (t, 0)),
        ],
        out_specs=pl.BlockSpec((1, ROWS, nrange), lambda c, t: (c, t, 0)),
        out_shape=jax.ShapeDtypeStruct((2, nlines, nrange), jnp.bfloat16),
    )(weights, window, coeff, shift)
    half = nrange // 2
    return look_order(out[:, :, :half]), look_order(out[:, :, half:])


CHUNK = 512


def looks_kernel(first_ref, second_ref, out_ref):
    first_re = first_ref[0].astype(jnp.float32)
    first_im = first_ref[1].astype(jnp.float32)
    second_re = second_ref[0].astype(jnp.float32)
    second_im = second_ref[1].astype(jnp.float32)
    real_part = first_re * second_re + first_im * second_im
    imag_part = first_im * second_re - first_re * second_im
    rows = real_part.shape[0]
    groups = rows // LOOK_AZ
    real_lines = real_part.reshape(LOOK_AZ, groups, CHUNK).sum(axis=0)
    imag_lines = imag_part.reshape(LOOK_AZ, groups, CHUNK).sum(axis=0)
    pooling = (
        lax.broadcasted_iota(jnp.int32, (CHUNK, CHUNK // LOOK_RG), 0) // LOOK_RG
        == lax.broadcasted_iota(jnp.int32, (CHUNK, CHUNK // LOOK_RG), 1)
    ).astype(jnp.float32)
    real_looks = jnp.dot(real_lines, pooling, precision=lax.Precision.HIGHEST, preferred_element_type=jnp.float32)
    imag_looks = jnp.dot(imag_lines, pooling, precision=lax.Precision.HIGHEST, preferred_element_type=jnp.float32)
    out_ref[0] = real_looks / (LOOK_AZ * LOOK_RG)
    out_ref[1] = imag_looks / (LOOK_AZ * LOOK_RG)


def looks(first, second):
    nlines = first.shape[1]
    width = first.shape[2]
    groups = nlines // LOOK_AZ
    spec = pl.BlockSpec((2, nlines, CHUNK), lambda j: (0, 0, j))
    return pl.pallas_call(
        looks_kernel,
        grid=(width // CHUNK,),
        in_specs=[spec, spec],
        out_specs=pl.BlockSpec((2, groups, CHUNK // LOOK_RG), lambda j: (0, 0, j)),
        out_shape=jax.ShapeDtypeStruct((2, groups, width // LOOK_RG), jnp.float32),
    )(first, second)


def look_order(image):
    nlines = image.shape[1]
    groups = nlines // LOOK_AZ
    return image.reshape(2, groups, LOOK_AZ, image.shape[2]).transpose(0, 2, 1, 3).reshape(image.shape)


def conj(block):
    return jnp.stack([block[0], -block[1]])


def shards(slc, az_offset, az_kernel, rg_offset, rg_kernel, partners):
    padded = padded_2(slc, (("az", 2),), OFFAZ + 4)
    own_left, own_right = resample_block(padded[0], az_offset[0], az_kernel[0], rg_offset[0], rg_kernel[0])
    date = lax.axis_index("date")
    even = date % 2 == 0

    left_2 = shifted(own_left, "date", 2)
    left_1 = swapped(jnp.where(even, left_2, own_left), "date")
    left_4 = shifted(left_2, "date", 2)
    left_3 = shifted(left_1, "date", 2)
    right_2 = shifted(own_right, "date", -2)
    right_1 = swapped(jnp.where(even, own_right, right_2), "date")
    right_4 = shifted(right_2, "date", -2)
    right_3 = shifted(right_1, "date", -2)

    ahead = {
        1: looks(own_left, left_1),
        2: looks(own_left, left_2),
        3: looks(own_left, left_3),
        4: looks(own_left, left_4),
    }
    behind = {
        1: looks(own_right, right_1),
        2: looks(own_right, right_2),
        3: looks(own_right, right_3),
        4: looks(own_right, right_4),
    }
    ahead, behind = lax.optimization_barrier((ahead, behind))
    full = {}
    for s in range(1, GAP + 1):
        right_of_ahead = conj(shifted(behind[s], "date", s))
        left_of_behind = conj(shifted(ahead[s], "date", -s))
        full[s] = jnp.concatenate([ahead[s], right_of_ahead], axis=2)
        full[-s] = jnp.concatenate([left_of_behind, behind[s]], axis=2)

    listed = partners[0]
    outputs = []
    for slot in range(PARTNERS):
        value = jnp.zeros_like(full[1])
        for step, block in full.items():
            value = jnp.where(listed[slot] == date + step, block, value)
        outputs.append(value)
    return jnp.stack(outputs)[None]


def solution(mesh):
    in_specs = (
        P("date", None, "az", None),
        P("date"),
        P("date"),
        P("date", "az"),
        P("date", "az"),
        P("date", None),
    )
    out_specs = P("date", None, None, "az", None)
    return jax.shard_map(shards, mesh=mesh, in_specs=in_specs, out_specs=out_specs, check_vma=False)
```

```python
import jax
import jax.numpy as jnp
from jax import lax
from jax.sharding import PartitionSpec as P
from jax.experimental import pallas as pl
from jax.experimental.pallas import tpu as pltpu

PARTNERS = 4
GAP = 4
OFFAZ = 12
OFFRG = 12
NFRAC = 64
LOOK_AZ = 20
LOOK_RG = 4


def padded_2(cells, sides, width):
    for axis, dim in sides:
        count = lax.axis_size(axis)
        ends = count - 1
        head = lax.slice_in_dim(cells, 0, width, axis=dim)
        tail = lax.slice_in_dim(cells, cells.shape[dim] - width, cells.shape[dim], axis=dim)
        cells = jnp.concatenate(
            [
                lax.ppermute(tail, axis, [(i, (i + 1) % count) for i in range(ends)]),
                cells,
                lax.ppermute(head, axis, [((i + 1) % count, i) for i in range(ends)]),
            ],
            axis=dim,
        )
    return cells


def shifted(block, axis, distance):
    count = lax.axis_size(axis)
    route = [(i + distance, i) for i in range(count) if 0 <= i + distance < count]
    return lax.ppermute(block, axis, route)


def swapped(block, axis):
    count = lax.axis_size(axis)
    return lax.ppermute(block, axis, [(i, i ^ 1) for i in range(count)])


def kernel_table():
    frac = jnp.arange(NFRAC, dtype=jnp.float32)[:, None] / NFRAC
    taps = jnp.arange(8, dtype=jnp.float32)[None, :]
    place = taps - 3.0 - frac
    return jnp.sinc(place) * (0.5 + 0.5 * jnp.cos(jnp.pi * place / 4.5))


ROWS = 32
EDGE = 128


def resample_kernel(weights_ref, window_ref, coeff_ref, shift_ref, out_ref):
    step = pl.program_id(1)
    first = pl.multiple_of(step * ROWS, ROWS)
    window = window_ref[0, pl.ds(first, ROWS + 8), :]
    along = weights_ref[0] * window[0:ROWS, :]
    for tap in range(1, 8):
        along = along + weights_ref[tap] * window[tap : tap + ROWS, :]
    nrange = along.shape[1]
    zeros = jnp.zeros((ROWS, EDGE), jnp.float32)
    row = jnp.concatenate([zeros, along, zeros], axis=1)
    width = row.shape[1]
    shift = shift_ref[...]
    for bit in range(5):
        moved = pltpu.roll(row, width - (1 << bit), 1)
        row = jnp.where(((shift >> bit) & 1) == 1, moved, row)
    coeff = coeff_ref[...]
    result = None
    for tap in range(8):
        moved = pltpu.roll(row, width - (EDGE - 15 + tap), 1)[:, :nrange]
        term = coeff[:, tap : tap + 1] * moved
        result = term if result is None else result + term
    out_ref[0] = result.astype(out_ref.dtype)


def resample_block(padded, shift_lines, kern_lines, shift_range, kern_range):
    table = kernel_table()
    nlines = shift_range.shape[0]
    nrange = padded.shape[2]
    border = OFFAZ + 4
    start = border + shift_lines - 3
    window = lax.dynamic_slice_in_dim(padded, start, nlines + 7, 1).astype(jnp.float32)
    window = jnp.pad(window, ((0, 0), (0, 1), (0, 0)))
    weights = table[kern_lines]
    coeff = jnp.take(table, kern_range, axis=0)
    shift = (shift_range + OFFRG)[:, None]
    out = pl.pallas_call(
        resample_kernel,
        grid=(2, nlines // ROWS),
        in_specs=[
            pl.BlockSpec(memory_space=pltpu.SMEM),
            pl.BlockSpec((1, nlines + 8, nrange), lambda c, t: (c, 0, 0)),
            pl.BlockSpec((ROWS, 8), lambda c, t: (t, 0)),
            pl.BlockSpec((ROWS, 1), lambda c, t: (t, 0)),
        ],
        out_specs=pl.BlockSpec((1, ROWS, nrange), lambda c, t: (c, t, 0)),
        out_shape=jax.ShapeDtypeStruct((2, nlines, nrange), jnp.bfloat16),
        cost_estimate=pl.CostEstimate(
            flops=2 * nlines * nrange * 60, transcendentals=0, bytes_accessed=2 * nlines * nrange * 6
        ),
    )(weights, window, coeff, shift)
    half = nrange // 2
    return look_order(out[:, :, :half]), look_order(out[:, :, half:])


CHUNK = 512


def looks_kernel(first_ref, second_ref, out_ref):
    first_re = first_ref[0].astype(jnp.float32)
    first_im = first_ref[1].astype(jnp.float32)
    second_re = second_ref[0].astype(jnp.float32)
    second_im = second_ref[1].astype(jnp.float32)
    real_part = first_re * second_re + first_im * second_im
    imag_part = first_im * second_re - first_re * second_im
    rows = real_part.shape[0]
    groups = rows // LOOK_AZ
    real_lines = real_part.reshape(LOOK_AZ, groups, CHUNK).sum(axis=0)
    imag_lines = imag_part.reshape(LOOK_AZ, groups, CHUNK).sum(axis=0)
    pooling = (
        lax.broadcasted_iota(jnp.int32, (CHUNK, CHUNK // LOOK_RG), 0) // LOOK_RG
        == lax.broadcasted_iota(jnp.int32, (CHUNK, CHUNK // LOOK_RG), 1)
    ).astype(jnp.float32)
    real_looks = jnp.dot(real_lines, pooling, precision=lax.Precision.HIGHEST, preferred_element_type=jnp.float32)
    imag_looks = jnp.dot(imag_lines, pooling, precision=lax.Precision.HIGHEST, preferred_element_type=jnp.float32)
    out_ref[0] = real_looks / (LOOK_AZ * LOOK_RG)
    out_ref[1] = imag_looks / (LOOK_AZ * LOOK_RG)


def looks(first, second):
    nlines = first.shape[1]
    width = first.shape[2]
    groups = nlines // LOOK_AZ
    spec = pl.BlockSpec((2, nlines, CHUNK), lambda j: (0, 0, j))
    return pl.pallas_call(
        looks_kernel,
        grid=(width // CHUNK,),
        in_specs=[spec, spec],
        out_specs=pl.BlockSpec((2, groups, CHUNK // LOOK_RG), lambda j: (0, 0, j)),
        out_shape=jax.ShapeDtypeStruct((2, groups, width // LOOK_RG), jnp.float32),
        cost_estimate=pl.CostEstimate(
            flops=nlines * width * 40, transcendentals=0, bytes_accessed=2 * 2 * nlines * width * 2
        ),
    )(first, second)


def look_order(image):
    nlines = image.shape[1]
    groups = nlines // LOOK_AZ
    return image.reshape(2, groups, LOOK_AZ, image.shape[2]).transpose(0, 2, 1, 3).reshape(image.shape)


def conj(block):
    return jnp.stack([block[0], -block[1]])


def shards(slc, az_offset, az_kernel, rg_offset, rg_kernel, partners):
    padded = padded_2(slc, (("az", 2),), OFFAZ + 4)
    own_left, own_right = resample_block(padded[0], az_offset[0], az_kernel[0], rg_offset[0], rg_kernel[0])
    date = lax.axis_index("date")
    even = date % 2 == 0

    left_2 = shifted(own_left, "date", 2)
    left_1 = swapped(jnp.where(even, left_2, own_left), "date")
    left_4 = shifted(left_2, "date", 2)
    left_3 = shifted(left_1, "date", 2)
    right_2 = shifted(own_right, "date", -2)
    right_1 = swapped(jnp.where(even, own_right, right_2), "date")
    right_4 = shifted(right_2, "date", -2)
    right_3 = shifted(right_1, "date", -2)

    ahead = {
        1: looks(own_left, left_1),
        2: looks(own_left, left_2),
        3: looks(own_left, left_3),
        4: looks(own_left, left_4),
    }
    behind = {
        1: looks(own_right, right_1),
        2: looks(own_right, right_2),
        3: looks(own_right, right_3),
        4: looks(own_right, right_4),
    }
    full = {}
    for s in range(1, GAP + 1):
        right_of_ahead = conj(shifted(behind[s], "date", s))
        left_of_behind = conj(shifted(ahead[s], "date", -s))
        full[s] = jnp.concatenate([ahead[s], right_of_ahead], axis=2)
        full[-s] = jnp.concatenate([left_of_behind, behind[s]], axis=2)

    listed = partners[0]
    outputs = []
    for slot in range(PARTNERS):
        value = jnp.zeros_like(full[1])
        for step, block in full.items():
            value = jnp.where(listed[slot] == date + step, block, value)
        outputs.append(value)
    return jnp.stack(outputs)[None]


def solution(mesh):
    in_specs = (
        P("date", None, "az", None),
        P("date"),
        P("date"),
        P("date", "az"),
        P("date", "az"),
        P("date", None),
    )
    out_specs = P("date", None, None, "az", None)
    return jax.shard_map(shards, mesh=mesh, in_specs=in_specs, out_specs=out_specs, check_vma=False)
```

```python
import jax
import jax.numpy as jnp
from jax import lax
from jax.sharding import PartitionSpec as P
from jax.experimental import pallas as pl
from jax.experimental.pallas import tpu as pltpu

PARTNERS = 4
GAP = 4
OFFAZ = 12
OFFRG = 12
NFRAC = 64
LOOK_AZ = 20
LOOK_RG = 4


def padded_2(cells, sides, width):
    for axis, dim in sides:
        count = lax.axis_size(axis)
        ends = count - 1
        head = lax.slice_in_dim(cells, 0, width, axis=dim)
        tail = lax.slice_in_dim(cells, cells.shape[dim] - width, cells.shape[dim], axis=dim)
        cells = jnp.concatenate(
            [
                lax.ppermute(tail, axis, [(i, (i + 1) % count) for i in range(ends)]),
                cells,
                lax.ppermute(head, axis, [((i + 1) % count, i) for i in range(ends)]),
            ],
            axis=dim,
        )
    return cells


def shifted(block, axis, distance):
    count = lax.axis_size(axis)
    route = [(i + distance, i) for i in range(count) if 0 <= i + distance < count]
    return lax.ppermute(block, axis, route)


def swapped(block, axis):
    count = lax.axis_size(axis)
    return lax.ppermute(block, axis, [(i, i ^ 1) for i in range(count)])


def kernel_table():
    frac = jnp.arange(NFRAC, dtype=jnp.float32)[:, None] / NFRAC
    taps = jnp.arange(8, dtype=jnp.float32)[None, :]
    place = taps - 3.0 - frac
    return jnp.sinc(place) * (0.5 + 0.5 * jnp.cos(jnp.pi * place / 4.5))


ROWS = 32
EDGE = 128


def resample_kernel(weights_ref, window_ref, coeff_ref, shift_ref, out_ref):
    step = pl.program_id(1)
    first = pl.multiple_of(step * ROWS, ROWS)
    window = window_ref[0, pl.ds(first, ROWS + 8), :]
    along = weights_ref[0] * window[0:ROWS, :]
    for tap in range(1, 8):
        along = along + weights_ref[tap] * window[tap : tap + ROWS, :]
    nrange = along.shape[1]
    zeros = jnp.zeros((ROWS, EDGE), jnp.float32)
    row = jnp.concatenate([zeros, along, zeros], axis=1)
    width = row.shape[1]
    shift = shift_ref[...]
    for bit in range(5):
        moved = pltpu.roll(row, width - (1 << bit), 1)
        row = jnp.where(((shift >> bit) & 1) == 1, moved, row)
    coeff = coeff_ref[...]
    result = None
    for tap in range(8):
        moved = pltpu.roll(row, width - (EDGE - 15 + tap), 1)[:, :nrange]
        term = coeff[:, tap : tap + 1] * moved
        result = term if result is None else result + term
    out_ref[0] = result.astype(out_ref.dtype)


def resample_block(padded, shift_lines, kern_lines, shift_range, kern_range):
    table = kernel_table()
    nlines = shift_range.shape[0]
    nrange = padded.shape[2]
    border = OFFAZ + 4
    start = border + shift_lines - 3
    window = lax.dynamic_slice_in_dim(padded, start, nlines + 7, 1).astype(jnp.float32)
    window = jnp.pad(window, ((0, 0), (0, 1), (0, 0)))
    weights = table[kern_lines]
    coeff = jnp.take(table, kern_range, axis=0)
    shift = (shift_range + OFFRG)[:, None]
    out = pl.pallas_call(
        resample_kernel,
        grid=(2, nlines // ROWS),
        in_specs=[
            pl.BlockSpec(memory_space=pltpu.SMEM),
            pl.BlockSpec((1, nlines + 8, nrange), lambda c, t: (c, 0, 0)),
            pl.BlockSpec((ROWS, 8), lambda c, t: (t, 0)),
            pl.BlockSpec((ROWS, 1), lambda c, t: (t, 0)),
        ],
        out_specs=pl.BlockSpec((1, ROWS, nrange), lambda c, t: (c, t, 0)),
        out_shape=jax.ShapeDtypeStruct((2, nlines, nrange), jnp.bfloat16),
        cost_estimate=pl.CostEstimate(
            flops=2 * nlines * nrange * 60, transcendentals=0, bytes_accessed=2 * nlines * nrange * 6
        ),
    )(weights, window, coeff, shift)
    half = nrange // 2
    return look_order(out[:, :, :half]), look_order(out[:, :, half:])


CHUNK = 512


def looks_kernel(first_ref, second_ref, out_ref):
    first_re = first_ref[0].astype(jnp.float32)
    first_im = first_ref[1].astype(jnp.float32)
    second_re = second_ref[0].astype(jnp.float32)
    second_im = second_ref[1].astype(jnp.float32)
    real_part = first_re * second_re + first_im * second_im
    imag_part = first_im * second_re - first_re * second_im
    rows = real_part.shape[0]
    groups = rows // LOOK_AZ
    real_lines = real_part.reshape(LOOK_AZ, groups, CHUNK).sum(axis=0)
    imag_lines = imag_part.reshape(LOOK_AZ, groups, CHUNK).sum(axis=0)
    pooling = (
        lax.broadcasted_iota(jnp.int32, (CHUNK, CHUNK // LOOK_RG), 0) // LOOK_RG
        == lax.broadcasted_iota(jnp.int32, (CHUNK, CHUNK // LOOK_RG), 1)
    ).astype(jnp.float32)
    real_looks = jnp.dot(real_lines, pooling, precision=lax.Precision.HIGHEST, preferred_element_type=jnp.float32)
    imag_looks = jnp.dot(imag_lines, pooling, precision=lax.Precision.HIGHEST, preferred_element_type=jnp.float32)
    out_ref[0] = real_looks / (LOOK_AZ * LOOK_RG)
    out_ref[1] = imag_looks / (LOOK_AZ * LOOK_RG)


def looks(first, second):
    nlines = first.shape[1]
    width = first.shape[2]
    groups = nlines // LOOK_AZ
    spec = pl.BlockSpec((2, nlines, CHUNK), lambda j: (0, 0, j))
    return pl.pallas_call(
        looks_kernel,
        grid=(width // CHUNK,),
        in_specs=[spec, spec],
        out_specs=pl.BlockSpec((2, groups, CHUNK // LOOK_RG), lambda j: (0, 0, j)),
        out_shape=jax.ShapeDtypeStruct((2, groups, width // LOOK_RG), jnp.float32),
        cost_estimate=pl.CostEstimate(
            flops=nlines * width * 40, transcendentals=0, bytes_accessed=2 * 2 * nlines * width * 2
        ),
    )(first, second)


def look_order(image):
    nlines = image.shape[1]
    groups = nlines // LOOK_AZ
    return image.reshape(2, groups, LOOK_AZ, image.shape[2]).transpose(0, 2, 1, 3).reshape(image.shape)


def conj(block):
    return jnp.stack([block[0], -block[1]])


def shards(slc, az_offset, az_kernel, rg_offset, rg_kernel, partners):
    padded = padded_2(slc, (("az", 2),), OFFAZ + 4)
    own_left, own_right = resample_block(padded[0], az_offset[0], az_kernel[0], rg_offset[0], rg_kernel[0])
    date = lax.axis_index("date")
    even = date % 2 == 0

    left_2 = shifted(own_left, "date", 2)
    left_1 = swapped(jnp.where(even, left_2, own_left), "date")
    left_4 = shifted(left_2, "date", 2)
    left_3 = shifted(left_1, "date", 2)
    right_2 = shifted(own_right, "date", -2)
    right_1 = swapped(jnp.where(even, own_right, right_2), "date")
    right_4 = shifted(right_2, "date", -2)
    right_3 = shifted(right_1, "date", -2)

    ahead = {s: looks(own_left, other) for s, other in ((2, left_2), (1, left_1), (4, left_4))}
    behind = {s: looks(own_right, other) for s, other in ((2, right_2), (1, right_1), (4, right_4))}
    ahead, behind, left_3, right_3 = lax.optimization_barrier((ahead, behind, left_3, right_3))
    ahead[3] = looks(own_left, left_3)
    behind[3] = looks(own_right, right_3)
    full = {}
    for s in range(1, GAP + 1):
        right_of_ahead = conj(shifted(behind[s], "date", s))
        left_of_behind = conj(shifted(ahead[s], "date", -s))
        full[s] = jnp.concatenate([ahead[s], right_of_ahead], axis=2)
        full[-s] = jnp.concatenate([left_of_behind, behind[s]], axis=2)

    listed = partners[0]
    outputs = []
    for slot in range(PARTNERS):
        value = jnp.zeros_like(full[1])
        for step, block in full.items():
            value = jnp.where(listed[slot] == date + step, block, value)
        outputs.append(value)
    return jnp.stack(outputs)[None]


def solution(mesh):
    in_specs = (
        P("date", None, "az", None),
        P("date"),
        P("date"),
        P("date", "az"),
        P("date", "az"),
        P("date", None),
    )
    out_specs = P("date", None, None, "az", None)
    return jax.shard_map(shards, mesh=mesh, in_specs=in_specs, out_specs=out_specs, check_vma=False)
```

```python
import jax
import jax.numpy as jnp
from jax import lax
from jax.sharding import PartitionSpec as P
from jax.experimental import pallas as pl
from jax.experimental.pallas import tpu as pltpu

PARTNERS = 4
GAP = 4
OFFAZ = 12
OFFRG = 12
NFRAC = 64
LOOK_AZ = 20
LOOK_RG = 4


def padded_2(cells, sides, width):
    for axis, dim in sides:
        count = lax.axis_size(axis)
        ends = count - 1
        head = lax.slice_in_dim(cells, 0, width, axis=dim)
        tail = lax.slice_in_dim(cells, cells.shape[dim] - width, cells.shape[dim], axis=dim)
        cells = jnp.concatenate(
            [
                lax.ppermute(tail, axis, [(i, (i + 1) % count) for i in range(ends)]),
                cells,
                lax.ppermute(head, axis, [((i + 1) % count, i) for i in range(ends)]),
            ],
            axis=dim,
        )
    return cells


def shifted(block, axis, distance):
    count = lax.axis_size(axis)
    route = [(i + distance, i) for i in range(count) if 0 <= i + distance < count]
    return lax.ppermute(block, axis, route)


def swapped(block, axis):
    count = lax.axis_size(axis)
    return lax.ppermute(block, axis, [(i, i ^ 1) for i in range(count)])


def kernel_table():
    frac = jnp.arange(NFRAC, dtype=jnp.float32)[:, None] / NFRAC
    taps = jnp.arange(8, dtype=jnp.float32)[None, :]
    place = taps - 3.0 - frac
    return jnp.sinc(place) * (0.5 + 0.5 * jnp.cos(jnp.pi * place / 4.5))


ROWS = 32
EDGE = 128


def resample_kernel(weights_ref, window_ref, coeff_ref, shift_ref, out_ref):
    step = pl.program_id(1)
    first = pl.multiple_of(step * ROWS, ROWS)
    window = window_ref[0, pl.ds(first, ROWS + 8), :]
    along = weights_ref[0] * window[0:ROWS, :]
    for tap in range(1, 8):
        along = along + weights_ref[tap] * window[tap : tap + ROWS, :]
    nrange = along.shape[1]
    zeros = jnp.zeros((ROWS, EDGE), jnp.float32)
    row = jnp.concatenate([zeros, along, zeros], axis=1)
    width = row.shape[1]
    shift = shift_ref[...]
    for bit in range(5):
        moved = pltpu.roll(row, width - (1 << bit), 1)
        row = jnp.where(((shift >> bit) & 1) == 1, moved, row)
    coeff = coeff_ref[...]
    result = None
    for tap in range(8):
        moved = pltpu.roll(row, width - (EDGE - 15 + tap), 1)[:, :nrange]
        term = coeff[:, tap : tap + 1] * moved
        result = term if result is None else result + term
    out_ref[0] = result.astype(out_ref.dtype)


def resample_block(padded, shift_lines, kern_lines, shift_range, kern_range):
    table = kernel_table()
    nlines = shift_range.shape[0]
    nrange = padded.shape[2]
    border = OFFAZ + 4
    start = border + shift_lines - 3
    window = lax.dynamic_slice_in_dim(padded, start, nlines + 7, 1).astype(jnp.float32)
    window = jnp.pad(window, ((0, 0), (0, 1), (0, 0)))
    weights = table[kern_lines]
    coeff = jnp.take(table, kern_range, axis=0)
    shift = (shift_range + OFFRG)[:, None]
    out = pl.pallas_call(
        resample_kernel,
        grid=(2, nlines // ROWS),
        in_specs=[
            pl.BlockSpec(memory_space=pltpu.SMEM),
            pl.BlockSpec((1, nlines + 8, nrange), lambda c, t: (c, 0, 0)),
            pl.BlockSpec((ROWS, 8), lambda c, t: (t, 0)),
            pl.BlockSpec((ROWS, 1), lambda c, t: (t, 0)),
        ],
        out_specs=pl.BlockSpec((1, ROWS, nrange), lambda c, t: (c, t, 0)),
        out_shape=jax.ShapeDtypeStruct((2, nlines, nrange), jnp.bfloat16),
        cost_estimate=pl.CostEstimate(
            flops=2 * nlines * nrange * 60, transcendentals=0, bytes_accessed=2 * nlines * nrange * 6
        ),
    )(weights, window, coeff, shift)
    half = nrange // 2
    return look_order(out[:, :, :half]), look_order(out[:, :, half:])


CHUNK = 512


def looks_kernel(first_ref, second_ref, out_ref):
    first_re = first_ref[0].astype(jnp.float32)
    first_im = first_ref[1].astype(jnp.float32)
    second_re = second_ref[0].astype(jnp.float32)
    second_im = second_ref[1].astype(jnp.float32)
    real_part = first_re * second_re + first_im * second_im
    imag_part = first_im * second_re - first_re * second_im
    rows = real_part.shape[0]
    groups = rows // LOOK_AZ
    real_lines = real_part.reshape(LOOK_AZ, groups, CHUNK).sum(axis=0)
    imag_lines = imag_part.reshape(LOOK_AZ, groups, CHUNK).sum(axis=0)
    pooling = (
        lax.broadcasted_iota(jnp.int32, (CHUNK, CHUNK // LOOK_RG), 0) // LOOK_RG
        == lax.broadcasted_iota(jnp.int32, (CHUNK, CHUNK // LOOK_RG), 1)
    ).astype(jnp.float32)
    real_looks = jnp.dot(real_lines, pooling, precision=lax.Precision.HIGHEST, preferred_element_type=jnp.float32)
    imag_looks = jnp.dot(imag_lines, pooling, precision=lax.Precision.HIGHEST, preferred_element_type=jnp.float32)
    out_ref[0] = real_looks / (LOOK_AZ * LOOK_RG)
    out_ref[1] = imag_looks / (LOOK_AZ * LOOK_RG)


def looks(first, second):
    nlines = first.shape[1]
    width = first.shape[2]
    groups = nlines // LOOK_AZ
    spec = pl.BlockSpec((2, nlines, CHUNK), lambda j: (0, 0, j))
    return pl.pallas_call(
        looks_kernel,
        grid=(width // CHUNK,),
        in_specs=[spec, spec],
        out_specs=pl.BlockSpec((2, groups, CHUNK // LOOK_RG), lambda j: (0, 0, j)),
        out_shape=jax.ShapeDtypeStruct((2, groups, width // LOOK_RG), jnp.float32),
        cost_estimate=pl.CostEstimate(
            flops=nlines * width * 40, transcendentals=0, bytes_accessed=2 * 2 * nlines * width * 2
        ),
    )(first, second)


def look_order(image):
    nlines = image.shape[1]
    groups = nlines // LOOK_AZ
    return image.reshape(2, groups, LOOK_AZ, image.shape[2]).transpose(0, 2, 1, 3).reshape(image.shape)


def conj(block):
    return jnp.stack([block[0], -block[1]])


def shards(slc, az_offset, az_kernel, rg_offset, rg_kernel, partners):
    padded = padded_2(slc, (("az", 2),), OFFAZ + 4)
    own_left, own_right = resample_block(padded[0], az_offset[0], az_kernel[0], rg_offset[0], rg_kernel[0])
    date = lax.axis_index("date")
    even = date % 2 == 0

    left_2 = shifted(own_left, "date", 2)
    left_1 = swapped(jnp.where(even, left_2, own_left), "date")
    left_4 = shifted(left_2, "date", 2)
    left_3 = shifted(left_1, "date", 2)
    right_2 = shifted(own_right, "date", -2)
    right_1 = swapped(jnp.where(even, own_right, right_2), "date")
    right_4 = shifted(right_2, "date", -2)
    right_3 = shifted(right_1, "date", -2)

    ahead = {
        1: looks(own_left, left_1),
        2: looks(own_left, left_2),
        3: looks(own_left, left_3),
        4: looks(own_left, left_4),
    }
    behind = {
        1: looks(own_right, right_1),
        2: looks(own_right, right_2),
        3: looks(own_right, right_3),
        4: looks(own_right, right_4),
    }
    count = lax.axis_size("date")
    target = lax.broadcasted_iota(jnp.int32, (count, 1, 1, 1), 0) - date
    sent = jnp.zeros((count,) + ahead[1].shape, jnp.float32)
    for s in range(1, GAP + 1):
        sent = jnp.where(target == s, ahead[s][None], sent)
        sent = jnp.where(target == -s, behind[s][None], sent)
    got = lax.all_to_all(sent, "date", 0, 0, tiled=True)
    full = {}
    for s in range(1, GAP + 1):
        right_of_ahead = conj(lax.dynamic_index_in_dim(got, jnp.minimum(date + s, count - 1), 0, keepdims=False))
        left_of_behind = conj(lax.dynamic_index_in_dim(got, jnp.maximum(date - s, 0), 0, keepdims=False))
        full[s] = jnp.concatenate([ahead[s], right_of_ahead], axis=2)
        full[-s] = jnp.concatenate([left_of_behind, behind[s]], axis=2)

    listed = partners[0]
    outputs = []
    for slot in range(PARTNERS):
        value = jnp.zeros_like(full[1])
        for step, block in full.items():
            value = jnp.where(listed[slot] == date + step, block, value)
        outputs.append(value)
    return jnp.stack(outputs)[None]


def solution(mesh):
    in_specs = (
        P("date", None, "az", None),
        P("date"),
        P("date"),
        P("date", "az"),
        P("date", "az"),
        P("date", None),
    )
    out_specs = P("date", None, None, "az", None)
    return jax.shard_map(shards, mesh=mesh, in_specs=in_specs, out_specs=out_specs, check_vma=False)
```

```python
import jax
import jax.numpy as jnp
from jax import lax
from jax.sharding import PartitionSpec as P
from jax.experimental import pallas as pl
from jax.experimental.pallas import tpu as pltpu

PARTNERS = 4
GAP = 4
OFFAZ = 12
OFFRG = 12
NFRAC = 64
LOOK_AZ = 20
LOOK_RG = 4


def padded_2(cells, sides, width):
    for axis, dim in sides:
        count = lax.axis_size(axis)
        ends = count - 1
        head = lax.slice_in_dim(cells, 0, width, axis=dim)
        tail = lax.slice_in_dim(cells, cells.shape[dim] - width, cells.shape[dim], axis=dim)
        cells = jnp.concatenate(
            [
                lax.ppermute(tail, axis, [(i, (i + 1) % count) for i in range(ends)]),
                cells,
                lax.ppermute(head, axis, [((i + 1) % count, i) for i in range(ends)]),
            ],
            axis=dim,
        )
    return cells


def shifted(block, axis, distance):
    count = lax.axis_size(axis)
    route = [(i + distance, i) for i in range(count) if 0 <= i + distance < count]
    return lax.ppermute(block, axis, route)


def swapped(block, axis):
    count = lax.axis_size(axis)
    return lax.ppermute(block, axis, [(i, i ^ 1) for i in range(count)])


def kernel_table():
    frac = jnp.arange(NFRAC, dtype=jnp.float32)[:, None] / NFRAC
    taps = jnp.arange(8, dtype=jnp.float32)[None, :]
    place = taps - 3.0 - frac
    return jnp.sinc(place) * (0.5 + 0.5 * jnp.cos(jnp.pi * place / 4.5))


ROWS = 32
EDGE = 128


def resample_kernel(weights_ref, window_ref, coeff_ref, shift_ref, out_ref):
    step = pl.program_id(1)
    first = pl.multiple_of(step * ROWS, ROWS)
    window = window_ref[0, pl.ds(first, ROWS + 8), :]
    along = weights_ref[0] * window[0:ROWS, :]
    for tap in range(1, 8):
        along = along + weights_ref[tap] * window[tap : tap + ROWS, :]
    nrange = along.shape[1]
    zeros = jnp.zeros((ROWS, EDGE), jnp.float32)
    row = jnp.concatenate([zeros, along, zeros], axis=1)
    width = row.shape[1]
    shift = shift_ref[...]
    for bit in range(5):
        moved = pltpu.roll(row, width - (1 << bit), 1)
        row = jnp.where(((shift >> bit) & 1) == 1, moved, row)
    coeff = coeff_ref[...]
    result = None
    for tap in range(8):
        moved = pltpu.roll(row, width - (EDGE - 15 + tap), 1)[:, :nrange]
        term = coeff[:, tap : tap + 1] * moved
        result = term if result is None else result + term
    out_ref[0] = result.astype(out_ref.dtype)


def resample_block(padded, shift_lines, kern_lines, shift_range, kern_range):
    table = kernel_table()
    nlines = shift_range.shape[0]
    nrange = padded.shape[2]
    border = OFFAZ + 4
    start = border + shift_lines - 3
    window = lax.dynamic_slice_in_dim(padded, start, nlines + 7, 1).astype(jnp.float32)
    window = jnp.pad(window, ((0, 0), (0, 1), (0, 0)))
    weights = table[kern_lines]
    coeff = jnp.take(table, kern_range, axis=0)
    shift = (shift_range + OFFRG)[:, None]
    out = pl.pallas_call(
        resample_kernel,
        grid=(2, nlines // ROWS),
        in_specs=[
            pl.BlockSpec(memory_space=pltpu.SMEM),
            pl.BlockSpec((1, nlines + 8, nrange), lambda c, t: (c, 0, 0)),
            pl.BlockSpec((ROWS, 8), lambda c, t: (t, 0)),
            pl.BlockSpec((ROWS, 1), lambda c, t: (t, 0)),
        ],
        out_specs=pl.BlockSpec((1, ROWS, nrange), lambda c, t: (c, t, 0)),
        out_shape=jax.ShapeDtypeStruct((2, nlines, nrange), jnp.bfloat16),
        cost_estimate=pl.CostEstimate(
            flops=2 * nlines * nrange * 60, transcendentals=0, bytes_accessed=2 * nlines * nrange * 6
        ),
    )(weights, window, coeff, shift)
    half = nrange // 2
    return look_order(out[:, :, :half]), look_order(out[:, :, half:])


CHUNK = 512


def looks_kernel(first_ref, *refs):
    count = len(refs) // 2
    first_re = first_ref[0].astype(jnp.float32)
    first_im = first_ref[1].astype(jnp.float32)
    rows = first_re.shape[0]
    groups = rows // LOOK_AZ
    pooling = (
        lax.broadcasted_iota(jnp.int32, (CHUNK, CHUNK // LOOK_RG), 0) // LOOK_RG
        == lax.broadcasted_iota(jnp.int32, (CHUNK, CHUNK // LOOK_RG), 1)
    ).astype(jnp.float32)
    for second_ref, out_ref in zip(refs[:count], refs[count:]):
        second_re = second_ref[0].astype(jnp.float32)
        second_im = second_ref[1].astype(jnp.float32)
        real_part = first_re * second_re + first_im * second_im
        imag_part = first_im * second_re - first_re * second_im
        real_lines = real_part.reshape(LOOK_AZ, groups, CHUNK).sum(axis=0)
        imag_lines = imag_part.reshape(LOOK_AZ, groups, CHUNK).sum(axis=0)
        real_looks = jnp.dot(real_lines, pooling, precision=lax.Precision.HIGHEST, preferred_element_type=jnp.float32)
        imag_looks = jnp.dot(imag_lines, pooling, precision=lax.Precision.HIGHEST, preferred_element_type=jnp.float32)
        out_ref[0] = real_looks / (LOOK_AZ * LOOK_RG)
        out_ref[1] = imag_looks / (LOOK_AZ * LOOK_RG)


def looks(first, others):
    nlines = first.shape[1]
    width = first.shape[2]
    groups = nlines // LOOK_AZ
    spec = pl.BlockSpec((2, nlines, CHUNK), lambda j: (0, 0, j))
    out_spec = pl.BlockSpec((2, groups, CHUNK // LOOK_RG), lambda j: (0, 0, j))
    shape = jax.ShapeDtypeStruct((2, groups, width // LOOK_RG), jnp.float32)
    count = len(others)
    return pl.pallas_call(
        looks_kernel,
        grid=(width // CHUNK,),
        in_specs=[spec] * (count + 1),
        out_specs=[out_spec] * count,
        out_shape=[shape] * count,
        cost_estimate=pl.CostEstimate(
            flops=count * nlines * width * 40, transcendentals=0, bytes_accessed=(count + 1) * 2 * nlines * width * 2
        ),
    )(first, *others)


def look_order(image):
    nlines = image.shape[1]
    groups = nlines // LOOK_AZ
    return image.reshape(2, groups, LOOK_AZ, image.shape[2]).transpose(0, 2, 1, 3).reshape(image.shape)


def conj(block):
    return jnp.stack([block[0], -block[1]])


def shards(slc, az_offset, az_kernel, rg_offset, rg_kernel, partners):
    padded = padded_2(slc, (("az", 2),), OFFAZ + 4)
    own_left, own_right = resample_block(padded[0], az_offset[0], az_kernel[0], rg_offset[0], rg_kernel[0])
    date = lax.axis_index("date")
    even = date % 2 == 0

    left_2 = shifted(own_left, "date", 2)
    left_1 = swapped(jnp.where(even, left_2, own_left), "date")
    left_4 = shifted(left_2, "date", 2)
    left_3 = shifted(left_1, "date", 2)
    right_2 = shifted(own_right, "date", -2)
    right_1 = swapped(jnp.where(even, own_right, right_2), "date")
    right_4 = shifted(right_2, "date", -2)
    right_3 = shifted(right_1, "date", -2)

    ahead = dict(zip((1, 2, 3, 4), looks(own_left, [left_1, left_2, left_3, left_4])))
    behind = dict(zip((1, 2, 3, 4), looks(own_right, [right_1, right_2, right_3, right_4])))
    count = lax.axis_size("date")
    target = lax.broadcasted_iota(jnp.int32, (count, 1, 1, 1), 0) - date
    sent = jnp.zeros((count,) + ahead[1].shape, jnp.float32)
    for s in range(1, GAP + 1):
        sent = jnp.where(target == s, ahead[s][None], sent)
        sent = jnp.where(target == -s, behind[s][None], sent)
    got = lax.all_to_all(sent, "date", 0, 0, tiled=True)
    full = {}
    for s in range(1, GAP + 1):
        right_of_ahead = conj(lax.dynamic_index_in_dim(got, jnp.minimum(date + s, count - 1), 0, keepdims=False))
        left_of_behind = conj(lax.dynamic_index_in_dim(got, jnp.maximum(date - s, 0), 0, keepdims=False))
        full[s] = jnp.concatenate([ahead[s], right_of_ahead], axis=2)
        full[-s] = jnp.concatenate([left_of_behind, behind[s]], axis=2)

    listed = partners[0]
    outputs = []
    for slot in range(PARTNERS):
        value = jnp.zeros_like(full[1])
        for step, block in full.items():
            value = jnp.where(listed[slot] == date + step, block, value)
        outputs.append(value)
    return jnp.stack(outputs)[None]


def solution(mesh):
    in_specs = (
        P("date", None, "az", None),
        P("date"),
        P("date"),
        P("date", "az"),
        P("date", "az"),
        P("date", None),
    )
    out_specs = P("date", None, None, "az", None)
    return jax.shard_map(shards, mesh=mesh, in_specs=in_specs, out_specs=out_specs, check_vma=False)
```

```python
import jax
import jax.numpy as jnp
from jax import lax
from jax.sharding import PartitionSpec as P
from jax.experimental import pallas as pl
from jax.experimental.pallas import tpu as pltpu

PARTNERS = 4
GAP = 4
OFFAZ = 12
OFFRG = 12
NFRAC = 64
LOOK_AZ = 20
LOOK_RG = 4


def padded_2(cells, sides, width):
    for axis, dim in sides:
        count = lax.axis_size(axis)
        ends = count - 1
        head = lax.slice_in_dim(cells, 0, width, axis=dim)
        tail = lax.slice_in_dim(cells, cells.shape[dim] - width, cells.shape[dim], axis=dim)
        cells = jnp.concatenate(
            [
                lax.ppermute(tail, axis, [(i, (i + 1) % count) for i in range(ends)]),
                cells,
                lax.ppermute(head, axis, [((i + 1) % count, i) for i in range(ends)]),
            ],
            axis=dim,
        )
    return cells


def routed(block, axis, distance, keep):
    count = lax.axis_size(axis)
    route = [(i + distance, i) for i in range(count) if 0 <= i + distance < count and keep(i, count)]
    return lax.ppermute(block, axis, route)


def kernel_table():
    frac = jnp.arange(NFRAC, dtype=jnp.float32)[:, None] / NFRAC
    taps = jnp.arange(8, dtype=jnp.float32)[None, :]
    place = taps - 3.0 - frac
    return jnp.sinc(place) * (0.5 + 0.5 * jnp.cos(jnp.pi * place / 4.5))


ROWS = 32
EDGE = 128


def resample_kernel(weights_ref, window_ref, coeff_ref, shift_ref, out_ref):
    step = pl.program_id(1)
    first = pl.multiple_of(step * ROWS, ROWS)
    window = window_ref[0, pl.ds(first, ROWS + 8), :]
    along = weights_ref[0] * window[0:ROWS, :]
    for tap in range(1, 8):
        along = along + weights_ref[tap] * window[tap : tap + ROWS, :]
    nrange = along.shape[1]
    zeros = jnp.zeros((ROWS, EDGE), jnp.float32)
    row = jnp.concatenate([zeros, along, zeros], axis=1)
    width = row.shape[1]
    shift = shift_ref[...]
    for bit in range(5):
        moved = pltpu.roll(row, width - (1 << bit), 1)
        row = jnp.where(((shift >> bit) & 1) == 1, moved, row)
    coeff = coeff_ref[...]
    result = None
    for tap in range(8):
        moved = pltpu.roll(row, width - (EDGE - 15 + tap), 1)[:, :nrange]
        term = coeff[:, tap : tap + 1] * moved
        result = term if result is None else result + term
    out_ref[0] = result.astype(out_ref.dtype)


def resample_block(padded, shift_lines, kern_lines, shift_range, kern_range):
    table = kernel_table()
    nlines = shift_range.shape[0]
    nrange = padded.shape[2]
    border = OFFAZ + 4
    start = border + shift_lines - 3
    window = lax.dynamic_slice_in_dim(padded, start, nlines + 7, 1).astype(jnp.float32)
    window = jnp.pad(window, ((0, 0), (0, 1), (0, 0)))
    weights = table[kern_lines]
    coeff = jnp.take(table, kern_range, axis=0)
    shift = (shift_range + OFFRG)[:, None]
    out = pl.pallas_call(
        resample_kernel,
        grid=(2, nlines // ROWS),
        in_specs=[
            pl.BlockSpec(memory_space=pltpu.SMEM),
            pl.BlockSpec((1, nlines + 8, nrange), lambda c, t: (c, 0, 0)),
            pl.BlockSpec((ROWS, 8), lambda c, t: (t, 0)),
            pl.BlockSpec((ROWS, 1), lambda c, t: (t, 0)),
        ],
        out_specs=pl.BlockSpec((1, ROWS, nrange), lambda c, t: (c, t, 0)),
        out_shape=jax.ShapeDtypeStruct((2, nlines, nrange), jnp.bfloat16),
        cost_estimate=pl.CostEstimate(
            flops=2 * nlines * nrange * 60, transcendentals=0, bytes_accessed=2 * nlines * nrange * 6
        ),
    )(weights, window, coeff, shift)
    half = nrange // 2
    return look_order(out[:, :, :half]), look_order(out[:, :, half:])


CHUNK = 512


def looks_kernel(first_ref, *refs):
    count = len(refs) // 2
    first_re = first_ref[0].astype(jnp.float32)
    first_im = first_ref[1].astype(jnp.float32)
    rows = first_re.shape[0]
    groups = rows // LOOK_AZ
    pooling = (
        lax.broadcasted_iota(jnp.int32, (CHUNK, CHUNK // LOOK_RG), 0) // LOOK_RG
        == lax.broadcasted_iota(jnp.int32, (CHUNK, CHUNK // LOOK_RG), 1)
    ).astype(jnp.float32)
    for second_ref, out_ref in zip(refs[:count], refs[count:]):
        second_re = second_ref[0].astype(jnp.float32)
        second_im = second_ref[1].astype(jnp.float32)
        real_part = first_re * second_re + first_im * second_im
        imag_part = first_im * second_re - first_re * second_im
        real_lines = real_part.reshape(LOOK_AZ, groups, CHUNK).sum(axis=0)
        imag_lines = imag_part.reshape(LOOK_AZ, groups, CHUNK).sum(axis=0)
        real_looks = jnp.dot(real_lines, pooling, precision=lax.Precision.HIGHEST, preferred_element_type=jnp.float32)
        imag_looks = jnp.dot(imag_lines, pooling, precision=lax.Precision.HIGHEST, preferred_element_type=jnp.float32)
        out_ref[0] = real_looks / (LOOK_AZ * LOOK_RG)
        out_ref[1] = imag_looks / (LOOK_AZ * LOOK_RG)


def looks(first, others):
    nlines = first.shape[1]
    width = first.shape[2]
    groups = nlines // LOOK_AZ
    spec = pl.BlockSpec((2, nlines, CHUNK), lambda j: (0, 0, j))
    out_spec = pl.BlockSpec((2, groups, CHUNK // LOOK_RG), lambda j: (0, 0, j))
    shape = jax.ShapeDtypeStruct((2, groups, width // LOOK_RG), jnp.float32)
    count = len(others)
    return pl.pallas_call(
        looks_kernel,
        grid=(width // CHUNK,),
        in_specs=[spec] * (count + 1),
        out_specs=[out_spec] * count,
        out_shape=[shape] * count,
        cost_estimate=pl.CostEstimate(
            flops=count * nlines * width * 40, transcendentals=0, bytes_accessed=(count + 1) * 2 * nlines * width * 2
        ),
    )(first, *others)


def look_order(image):
    nlines = image.shape[1]
    groups = nlines // LOOK_AZ
    return image.reshape(2, groups, LOOK_AZ, image.shape[2]).transpose(0, 2, 1, 3).reshape(image.shape)


def conj(block):
    return jnp.stack([block[0], -block[1]])


def shards(slc, az_offset, az_kernel, rg_offset, rg_kernel, partners):
    padded = padded_2(slc, (("az", 2),), OFFAZ + 4)
    own_left, own_right = resample_block(padded[0], az_offset[0], az_kernel[0], rg_offset[0], rg_kernel[0])
    date = lax.axis_index("date")
    even = date % 2 == 0

    left_2 = routed(own_left, "date", 2, lambda i, n: True)
    left_1_even = routed(own_left, "date", 1, lambda i, n: i % 2 == 0)
    left_4 = routed(left_2, "date", 2, lambda i, n: i + 4 < n)
    left_1_odd = routed(left_2, "date", -1, lambda i, n: i % 2 == 1 and i + 1 < n)
    left_3_even = routed(left_1_even, "date", 2, lambda i, n: i % 2 == 0 and i + 3 < n)
    left_3_odd = routed(left_1_odd, "date", 2, lambda i, n: i % 2 == 1 and i + 3 < n)
    left_1 = jnp.where(even, left_1_even, left_1_odd)
    left_3 = jnp.where(even, left_3_even, left_3_odd)
    right_2 = routed(own_right, "date", -2, lambda i, n: True)
    right_1_odd = routed(own_right, "date", -1, lambda i, n: i % 2 == 1)
    right_4 = routed(right_2, "date", -2, lambda i, n: i >= 4)
    right_1_even = routed(right_2, "date", 1, lambda i, n: i % 2 == 0 and i >= 1)
    right_3_odd = routed(right_1_odd, "date", -2, lambda i, n: i % 2 == 1 and i >= 3)
    right_3_even = routed(right_1_even, "date", -2, lambda i, n: i % 2 == 0 and i >= 3)
    right_1 = jnp.where(even, right_1_even, right_1_odd)
    right_3 = jnp.where(even, right_3_even, right_3_odd)

    ahead = dict(zip((1, 2, 3, 4), looks(own_left, [left_1, left_2, left_3, left_4])))
    behind = dict(zip((1, 2, 3, 4), looks(own_right, [right_1, right_2, right_3, right_4])))
    count = lax.axis_size("date")
    target = lax.broadcasted_iota(jnp.int32, (count, 1, 1, 1), 0) - date
    sent = jnp.zeros((count,) + ahead[1].shape, jnp.float32)
    for s in range(1, GAP + 1):
        sent = jnp.where(target == s, ahead[s][None], sent)
        sent = jnp.where(target == -s, behind[s][None], sent)
    got = lax.all_to_all(sent, "date", 0, 0, tiled=True)
    full = {}
    for s in range(1, GAP + 1):
        right_of_ahead = conj(lax.dynamic_index_in_dim(got, jnp.minimum(date + s, count - 1), 0, keepdims=False))
        left_of_behind = conj(lax.dynamic_index_in_dim(got, jnp.maximum(date - s, 0), 0, keepdims=False))
        full[s] = jnp.concatenate([ahead[s], right_of_ahead], axis=2)
        full[-s] = jnp.concatenate([left_of_behind, behind[s]], axis=2)

    listed = partners[0]
    outputs = []
    for slot in range(PARTNERS):
        value = jnp.zeros_like(full[1])
        for step, block in full.items():
            value = jnp.where(listed[slot] == date + step, block, value)
        outputs.append(value)
    return jnp.stack(outputs)[None]


def solution(mesh):
    in_specs = (
        P("date", None, "az", None),
        P("date"),
        P("date"),
        P("date", "az"),
        P("date", "az"),
        P("date", None),
    )
    out_specs = P("date", None, None, "az", None)
    return jax.shard_map(shards, mesh=mesh, in_specs=in_specs, out_specs=out_specs, check_vma=False)
```

```python
import jax
import jax.numpy as jnp
from jax import lax
from jax.sharding import PartitionSpec as P
from jax.experimental import pallas as pl
from jax.experimental.pallas import tpu as pltpu

PARTNERS = 4
GAP = 4
OFFAZ = 12
OFFRG = 12
NFRAC = 64
LOOK_AZ = 20
LOOK_RG = 4


def padded_2(cells, sides, width):
    for axis, dim in sides:
        count = lax.axis_size(axis)
        ends = count - 1
        head = lax.slice_in_dim(cells, 0, width, axis=dim)
        tail = lax.slice_in_dim(cells, cells.shape[dim] - width, cells.shape[dim], axis=dim)
        cells = jnp.concatenate(
            [
                lax.ppermute(tail, axis, [(i, (i + 1) % count) for i in range(ends)]),
                cells,
                lax.ppermute(head, axis, [((i + 1) % count, i) for i in range(ends)]),
            ],
            axis=dim,
        )
    return cells


def gathered(block, axis, source):
    count = lax.axis_size(axis)
    route = [(source(i, count), i) for i in range(count) if source(i, count) is not None]
    return lax.ppermute(block, axis, route)


def within(i, n):
    return i if 0 <= i < n else None


def kernel_table():
    frac = jnp.arange(NFRAC, dtype=jnp.float32)[:, None] / NFRAC
    taps = jnp.arange(8, dtype=jnp.float32)[None, :]
    place = taps - 3.0 - frac
    return jnp.sinc(place) * (0.5 + 0.5 * jnp.cos(jnp.pi * place / 4.5))


ROWS = 32
EDGE = 128


def resample_kernel(weights_ref, window_ref, coeff_ref, shift_ref, out_ref):
    step = pl.program_id(1)
    first = pl.multiple_of(step * ROWS, ROWS)
    window = window_ref[0, pl.ds(first, ROWS + 8), :]
    along = weights_ref[0] * window[0:ROWS, :]
    for tap in range(1, 8):
        along = along + weights_ref[tap] * window[tap : tap + ROWS, :]
    nrange = along.shape[1]
    zeros = jnp.zeros((ROWS, EDGE), jnp.float32)
    row = jnp.concatenate([zeros, along, zeros], axis=1)
    width = row.shape[1]
    shift = shift_ref[...]
    for bit in range(5):
        moved = pltpu.roll(row, width - (1 << bit), 1)
        row = jnp.where(((shift >> bit) & 1) == 1, moved, row)
    coeff = coeff_ref[...]
    result = None
    for tap in range(8):
        moved = pltpu.roll(row, width - (EDGE - 15 + tap), 1)[:, :nrange]
        term = coeff[:, tap : tap + 1] * moved
        result = term if result is None else result + term
    out_ref[0] = result.astype(out_ref.dtype)


def resample_block(padded, shift_lines, kern_lines, shift_range, kern_range):
    table = kernel_table()
    nlines = shift_range.shape[0]
    nrange = padded.shape[2]
    border = OFFAZ + 4
    start = border + shift_lines - 3
    window = lax.dynamic_slice_in_dim(padded, start, nlines + 7, 1).astype(jnp.float32)
    window = jnp.pad(window, ((0, 0), (0, 1), (0, 0)))
    weights = table[kern_lines]
    coeff = jnp.take(table, kern_range, axis=0)
    shift = (shift_range + OFFRG)[:, None]
    out = pl.pallas_call(
        resample_kernel,
        grid=(2, nlines // ROWS),
        in_specs=[
            pl.BlockSpec(memory_space=pltpu.SMEM),
            pl.BlockSpec((1, nlines + 8, nrange), lambda c, t: (c, 0, 0)),
            pl.BlockSpec((ROWS, 8), lambda c, t: (t, 0)),
            pl.BlockSpec((ROWS, 1), lambda c, t: (t, 0)),
        ],
        out_specs=pl.BlockSpec((1, ROWS, nrange), lambda c, t: (c, t, 0)),
        out_shape=jax.ShapeDtypeStruct((2, nlines, nrange), jnp.bfloat16),
        cost_estimate=pl.CostEstimate(
            flops=2 * nlines * nrange * 60, transcendentals=0, bytes_accessed=2 * nlines * nrange * 6
        ),
    )(weights, window, coeff, shift)
    half = nrange // 2
    return look_order(out[:, :, :half]), look_order(out[:, :, half:])


CHUNK = 512


def looks_kernel(first_ref, *refs):
    count = len(refs) // 2
    first_re = first_ref[0].astype(jnp.float32)
    first_im = first_ref[1].astype(jnp.float32)
    rows = first_re.shape[0]
    groups = rows // LOOK_AZ
    pooling = (
        lax.broadcasted_iota(jnp.int32, (CHUNK, CHUNK // LOOK_RG), 0) // LOOK_RG
        == lax.broadcasted_iota(jnp.int32, (CHUNK, CHUNK // LOOK_RG), 1)
    ).astype(jnp.float32)
    for second_ref, out_ref in zip(refs[:count], refs[count:]):
        second_re = second_ref[0].astype(jnp.float32)
        second_im = second_ref[1].astype(jnp.float32)
        real_part = first_re * second_re + first_im * second_im
        imag_part = first_im * second_re - first_re * second_im
        real_lines = real_part.reshape(LOOK_AZ, groups, CHUNK).sum(axis=0)
        imag_lines = imag_part.reshape(LOOK_AZ, groups, CHUNK).sum(axis=0)
        real_looks = jnp.dot(real_lines, pooling, precision=lax.Precision.HIGHEST, preferred_element_type=jnp.float32)
        imag_looks = jnp.dot(imag_lines, pooling, precision=lax.Precision.HIGHEST, preferred_element_type=jnp.float32)
        out_ref[0] = real_looks / (LOOK_AZ * LOOK_RG)
        out_ref[1] = imag_looks / (LOOK_AZ * LOOK_RG)


def looks(first, others):
    nlines = first.shape[1]
    width = first.shape[2]
    groups = nlines // LOOK_AZ
    spec = pl.BlockSpec((2, nlines, CHUNK), lambda j: (0, 0, j))
    out_spec = pl.BlockSpec((2, groups, CHUNK // LOOK_RG), lambda j: (0, 0, j))
    shape = jax.ShapeDtypeStruct((2, groups, width // LOOK_RG), jnp.float32)
    count = len(others)
    return pl.pallas_call(
        looks_kernel,
        grid=(width // CHUNK,),
        in_specs=[spec] * (count + 1),
        out_specs=[out_spec] * count,
        out_shape=[shape] * count,
        cost_estimate=pl.CostEstimate(
            flops=count * nlines * width * 40, transcendentals=0, bytes_accessed=(count + 1) * 2 * nlines * width * 2
        ),
    )(first, *others)


def look_order(image):
    nlines = image.shape[1]
    groups = nlines // LOOK_AZ
    return image.reshape(2, groups, LOOK_AZ, image.shape[2]).transpose(0, 2, 1, 3).reshape(image.shape)


def conj(block):
    return jnp.stack([block[0], -block[1]])


def shards(slc, az_offset, az_kernel, rg_offset, rg_kernel, partners):
    padded = padded_2(slc, (("az", 2),), OFFAZ + 4)
    own_left, own_right = resample_block(padded[0], az_offset[0], az_kernel[0], rg_offset[0], rg_kernel[0])
    date = lax.axis_index("date")
    even = date % 2 == 0

    left_2 = gathered(own_left, "date", lambda i, n: within(i + 2, n))
    right_2 = gathered(own_right, "date", lambda i, n: within(i - 2, n))
    pair_own = gathered(jnp.where(even, own_right, own_left), "date", lambda i, n: i ^ 1)
    left_4 = gathered(left_2, "date", lambda i, n: within(i + 2, n) if i + 4 < n else None)
    right_4 = gathered(right_2, "date", lambda i, n: within(i - 2, n) if i >= 4 else None)
    pair_relay = gathered(jnp.where(even, left_2, right_2), "date", lambda i, n: i ^ 1)
    third_own = gathered(
        pair_own, "date", lambda i, n: (i + 2 if i + 3 < n else None) if i % 2 == 0 else (i - 2 if i >= 3 else None)
    )
    third_relay = gathered(
        pair_relay, "date", lambda i, n: (i + 2 if i + 3 < n else None) if i % 2 == 1 else (i - 2 if i >= 3 else None)
    )
    left_1 = jnp.where(even, pair_own, pair_relay)
    right_1 = jnp.where(even, pair_relay, pair_own)
    left_3 = jnp.where(even, third_own, third_relay)
    right_3 = jnp.where(even, third_relay, third_own)

    ahead = dict(zip((1, 2, 3, 4), looks(own_left, [left_1, left_2, left_3, left_4])))
    behind = dict(zip((1, 2, 3, 4), looks(own_right, [right_1, right_2, right_3, right_4])))
    count = lax.axis_size("date")
    target = lax.broadcasted_iota(jnp.int32, (count, 1, 1, 1), 0) - date
    sent = jnp.zeros((count,) + ahead[1].shape, jnp.float32)
    for s in range(1, GAP + 1):
        sent = jnp.where(target == s, ahead[s][None], sent)
        sent = jnp.where(target == -s, behind[s][None], sent)
    got = lax.all_to_all(sent, "date", 0, 0, tiled=True)
    full = {}
    for s in range(1, GAP + 1):
        right_of_ahead = conj(lax.dynamic_index_in_dim(got, jnp.minimum(date + s, count - 1), 0, keepdims=False))
        left_of_behind = conj(lax.dynamic_index_in_dim(got, jnp.maximum(date - s, 0), 0, keepdims=False))
        full[s] = jnp.concatenate([ahead[s], right_of_ahead], axis=2)
        full[-s] = jnp.concatenate([left_of_behind, behind[s]], axis=2)

    listed = partners[0]
    outputs = []
    for slot in range(PARTNERS):
        value = jnp.zeros_like(full[1])
        for step, block in full.items():
            value = jnp.where(listed[slot] == date + step, block, value)
        outputs.append(value)
    return jnp.stack(outputs)[None]


def solution(mesh):
    in_specs = (
        P("date", None, "az", None),
        P("date"),
        P("date"),
        P("date", "az"),
        P("date", "az"),
        P("date", None),
    )
    out_specs = P("date", None, None, "az", None)
    return jax.shard_map(shards, mesh=mesh, in_specs=in_specs, out_specs=out_specs, check_vma=False)
```

```python
import functools

import jax
import jax.numpy as jnp
from jax import lax
from jax.sharding import PartitionSpec as P
from jax.experimental import pallas as pl
from jax.experimental.pallas import tpu as pltpu

PARTNERS = 4
GAP = 4
OFFAZ = 12
OFFRG = 12
NFRAC = 64
LOOK_AZ = 20
LOOK_RG = 4


def padded_2(cells, sides, width):
    for axis, dim in sides:
        count = lax.axis_size(axis)
        ends = count - 1
        head = lax.slice_in_dim(cells, 0, width, axis=dim)
        tail = lax.slice_in_dim(cells, cells.shape[dim] - width, cells.shape[dim], axis=dim)
        cells = jnp.concatenate(
            [
                lax.ppermute(tail, axis, [(i, (i + 1) % count) for i in range(ends)]),
                cells,
                lax.ppermute(head, axis, [((i + 1) % count, i) for i in range(ends)]),
            ],
            axis=dim,
        )
    return cells


def shifted(block, axis, distance):
    count = lax.axis_size(axis)
    route = [(i + distance, i) for i in range(count) if 0 <= i + distance < count]
    return lax.ppermute(block, axis, route)


def swapped(block, axis):
    count = lax.axis_size(axis)
    return lax.ppermute(block, axis, [(i, i ^ 1) for i in range(count)])


def kernel_table():
    frac = jnp.arange(NFRAC, dtype=jnp.float32)[:, None] / NFRAC
    taps = jnp.arange(8, dtype=jnp.float32)[None, :]
    place = taps - 3.0 - frac
    return jnp.sinc(place) * (0.5 + 0.5 * jnp.cos(jnp.pi * place / 4.5))


ROWS = 32
EDGE = 128


def resample_kernel(side, weights_ref, window_ref, coeff_ref, shift_ref, out_ref):
    step = pl.program_id(1)
    first = pl.multiple_of(step * ROWS, ROWS)
    half = out_ref.shape[2]
    low = max(side * half - EDGE, 0)
    high = min(side * half + half + EDGE, window_ref.shape[2])
    window = window_ref[0, pl.ds(first, ROWS + 8), low:high]
    along = weights_ref[0] * window[0:ROWS, :]
    for tap in range(1, 8):
        along = along + weights_ref[tap] * window[tap : tap + ROWS, :]
    zeros = jnp.zeros((ROWS, EDGE), jnp.float32)
    row = jnp.concatenate([zeros, along] if side == 0 else [along, zeros], axis=1)
    width = row.shape[1]
    shift = shift_ref[...]
    for bit in range(5):
        moved = pltpu.roll(row, width - (1 << bit), 1)
        row = jnp.where(((shift >> bit) & 1) == 1, moved, row)
    coeff = coeff_ref[...]
    result = None
    for tap in range(8):
        moved = pltpu.roll(row, width - (EDGE - 15 + tap), 1)[:, :half]
        term = coeff[:, tap : tap + 1] * moved
        result = term if result is None else result + term
    out_ref[0] = result.astype(out_ref.dtype)


def resample_half(side, weights, window, coeff, shift):
    nlines = coeff.shape[0]
    half = window.shape[2] // 2
    return pl.pallas_call(
        functools.partial(resample_kernel, side),
        grid=(2, nlines // ROWS),
        in_specs=[
            pl.BlockSpec(memory_space=pltpu.SMEM),
            pl.BlockSpec((1,) + window.shape[1:], lambda c, t: (c, 0, 0)),
            pl.BlockSpec((ROWS, 8), lambda c, t: (t, 0)),
            pl.BlockSpec((ROWS, 1), lambda c, t: (t, 0)),
        ],
        out_specs=pl.BlockSpec((1, ROWS, half), lambda c, t: (c, t, 0)),
        out_shape=jax.ShapeDtypeStruct((2, nlines, half), jnp.bfloat16),
        cost_estimate=pl.CostEstimate(
            flops=2 * nlines * half * 60, transcendentals=0, bytes_accessed=2 * nlines * half * 6
        ),
    )(weights, window, coeff, shift)


def resample_block(padded, shift_lines, kern_lines, shift_range, kern_range):
    table = kernel_table()
    nlines = shift_range.shape[0]
    border = OFFAZ + 4
    start = border + shift_lines - 3
    window = lax.dynamic_slice_in_dim(padded, start, nlines + 7, 1).astype(jnp.float32)
    window = jnp.pad(window, ((0, 0), (0, 1), (0, 0)))
    weights = table[kern_lines]
    coeff = jnp.take(table, kern_range, axis=0)
    shift = (shift_range + OFFRG)[:, None]
    left = look_order(resample_half(0, weights, window, coeff, shift))
    right = look_order(resample_half(1, weights, window, coeff, shift))
    return left, right


CHUNK = 512


def looks_kernel(first_ref, second_ref, out_ref):
    first_re = first_ref[0].astype(jnp.float32)
    first_im = first_ref[1].astype(jnp.float32)
    second_re = second_ref[0].astype(jnp.float32)
    second_im = second_ref[1].astype(jnp.float32)
    real_part = first_re * second_re + first_im * second_im
    imag_part = first_im * second_re - first_re * second_im
    rows = real_part.shape[0]
    groups = rows // LOOK_AZ
    real_lines = real_part.reshape(LOOK_AZ, groups, CHUNK).sum(axis=0)
    imag_lines = imag_part.reshape(LOOK_AZ, groups, CHUNK).sum(axis=0)
    pooling = (
        lax.broadcasted_iota(jnp.int32, (CHUNK, CHUNK // LOOK_RG), 0) // LOOK_RG
        == lax.broadcasted_iota(jnp.int32, (CHUNK, CHUNK // LOOK_RG), 1)
    ).astype(jnp.float32)
    real_looks = jnp.dot(real_lines, pooling, precision=lax.Precision.HIGHEST, preferred_element_type=jnp.float32)
    imag_looks = jnp.dot(imag_lines, pooling, precision=lax.Precision.HIGHEST, preferred_element_type=jnp.float32)
    out_ref[0] = real_looks / (LOOK_AZ * LOOK_RG)
    out_ref[1] = imag_looks / (LOOK_AZ * LOOK_RG)


def looks(first, second):
    nlines = first.shape[1]
    width = first.shape[2]
    groups = nlines // LOOK_AZ
    spec = pl.BlockSpec((2, nlines, CHUNK), lambda j: (0, 0, j))
    return pl.pallas_call(
        looks_kernel,
        grid=(width // CHUNK,),
        in_specs=[spec, spec],
        out_specs=pl.BlockSpec((2, groups, CHUNK // LOOK_RG), lambda j: (0, 0, j)),
        out_shape=jax.ShapeDtypeStruct((2, groups, width // LOOK_RG), jnp.float32),
        cost_estimate=pl.CostEstimate(
            flops=nlines * width * 40, transcendentals=0, bytes_accessed=2 * 2 * nlines * width * 2
        ),
    )(first, second)


def look_order(image):
    nlines = image.shape[1]
    groups = nlines // LOOK_AZ
    return image.reshape(2, groups, LOOK_AZ, image.shape[2]).transpose(0, 2, 1, 3).reshape(image.shape)


def conj(block):
    return jnp.stack([block[0], -block[1]])


def shards(slc, az_offset, az_kernel, rg_offset, rg_kernel, partners):
    padded = padded_2(slc, (("az", 2),), OFFAZ + 4)
    own_left, own_right = resample_block(padded[0], az_offset[0], az_kernel[0], rg_offset[0], rg_kernel[0])
    date = lax.axis_index("date")
    even = date % 2 == 0

    left_2 = shifted(own_left, "date", 2)
    left_1 = swapped(jnp.where(even, left_2, own_left), "date")
    left_4 = shifted(left_2, "date", 2)
    left_3 = shifted(left_1, "date", 2)
    right_2 = shifted(own_right, "date", -2)
    right_1 = swapped(jnp.where(even, own_right, right_2), "date")
    right_4 = shifted(right_2, "date", -2)
    right_3 = shifted(right_1, "date", -2)

    ahead = {
        1: looks(own_left, left_1),
        2: looks(own_left, left_2),
        3: looks(own_left, left_3),
        4: looks(own_left, left_4),
    }
    behind = {
        1: looks(own_right, right_1),
        2: looks(own_right, right_2),
        3: looks(own_right, right_3),
        4: looks(own_right, right_4),
    }
    count = lax.axis_size("date")
    target = lax.broadcasted_iota(jnp.int32, (count, 1, 1, 1), 0) - date
    sent = jnp.zeros((count,) + ahead[1].shape, jnp.float32)
    for s in range(1, GAP + 1):
        sent = jnp.where(target == s, ahead[s][None], sent)
        sent = jnp.where(target == -s, behind[s][None], sent)
    got = lax.all_to_all(sent, "date", 0, 0, tiled=True)
    full = {}
    for s in range(1, GAP + 1):
        right_of_ahead = conj(lax.dynamic_index_in_dim(got, jnp.minimum(date + s, count - 1), 0, keepdims=False))
        left_of_behind = conj(lax.dynamic_index_in_dim(got, jnp.maximum(date - s, 0), 0, keepdims=False))
        full[s] = jnp.concatenate([ahead[s], right_of_ahead], axis=2)
        full[-s] = jnp.concatenate([left_of_behind, behind[s]], axis=2)

    listed = partners[0]
    outputs = []
    for slot in range(PARTNERS):
        value = jnp.zeros_like(full[1])
        for step, block in full.items():
            value = jnp.where(listed[slot] == date + step, block, value)
        outputs.append(value)
    return jnp.stack(outputs)[None]


def solution(mesh):
    in_specs = (
        P("date", None, "az", None),
        P("date"),
        P("date"),
        P("date", "az"),
        P("date", "az"),
        P("date", None),
    )
    out_specs = P("date", None, None, "az", None)
    return jax.shard_map(shards, mesh=mesh, in_specs=in_specs, out_specs=out_specs, check_vma=False)
```

```python
import functools

import jax
import jax.numpy as jnp
from jax import lax
from jax.sharding import PartitionSpec as P
from jax.experimental import pallas as pl
from jax.experimental.pallas import tpu as pltpu

PARTNERS = 4
GAP = 4
OFFAZ = 12
OFFRG = 12
NFRAC = 64
LOOK_AZ = 20
LOOK_RG = 4


def padded_2(cells, sides, width):
    for axis, dim in sides:
        count = lax.axis_size(axis)
        ends = count - 1
        head = lax.slice_in_dim(cells, 0, width, axis=dim)
        tail = lax.slice_in_dim(cells, cells.shape[dim] - width, cells.shape[dim], axis=dim)
        cells = jnp.concatenate(
            [
                lax.ppermute(tail, axis, [(i, (i + 1) % count) for i in range(ends)]),
                cells,
                lax.ppermute(head, axis, [((i + 1) % count, i) for i in range(ends)]),
            ],
            axis=dim,
        )
    return cells


def shifted(block, axis, distance):
    count = lax.axis_size(axis)
    route = [(i + distance, i) for i in range(count) if 0 <= i + distance < count]
    return lax.ppermute(block, axis, route)


def swapped(block, axis):
    count = lax.axis_size(axis)
    return lax.ppermute(block, axis, [(i, i ^ 1) for i in range(count)])


def kernel_table():
    frac = jnp.arange(NFRAC, dtype=jnp.float32)[:, None] / NFRAC
    taps = jnp.arange(8, dtype=jnp.float32)[None, :]
    place = taps - 3.0 - frac
    return jnp.sinc(place) * (0.5 + 0.5 * jnp.cos(jnp.pi * place / 4.5))


ROWS = 32
EDGE = 128


def resample_kernel(side, weights_ref, window_ref, coeff_ref, shift_ref, out_ref):
    step = pl.program_id(1)
    first = pl.multiple_of(step * ROWS, ROWS)
    half = out_ref.shape[2]
    low = max(side * half - EDGE, 0)
    high = min(side * half + half + EDGE, window_ref.shape[2])
    window = window_ref[0, pl.ds(first, ROWS + 8), low:high]
    along = weights_ref[0] * window[0:ROWS, :]
    for tap in range(1, 8):
        along = along + weights_ref[tap] * window[tap : tap + ROWS, :]
    zeros = jnp.zeros((ROWS, EDGE), jnp.float32)
    row = jnp.concatenate([zeros, along] if side == 0 else [along, zeros], axis=1)
    width = row.shape[1]
    shift = shift_ref[...]
    for bit in range(5):
        moved = pltpu.roll(row, width - (1 << bit), 1)
        row = jnp.where(((shift >> bit) & 1) == 1, moved, row)
    coeff = coeff_ref[...]
    result = None
    for tap in range(8):
        moved = pltpu.roll(row, width - (EDGE - 15 + tap), 1)[:, :half]
        term = coeff[:, tap : tap + 1] * moved
        result = term if result is None else result + term
    out_ref[0] = result.astype(out_ref.dtype)


def resample_half(side, weights, window, coeff, shift):
    nlines = coeff.shape[0]
    half = window.shape[2] // 2
    return pl.pallas_call(
        functools.partial(resample_kernel, side),
        grid=(2, nlines // ROWS),
        in_specs=[
            pl.BlockSpec(memory_space=pltpu.SMEM),
            pl.BlockSpec((1,) + window.shape[1:], lambda c, t: (c, 0, 0)),
            pl.BlockSpec((ROWS, 8), lambda c, t: (t, 0)),
            pl.BlockSpec((ROWS, 1), lambda c, t: (t, 0)),
        ],
        out_specs=pl.BlockSpec((1, ROWS, half), lambda c, t: (c, t, 0)),
        out_shape=jax.ShapeDtypeStruct((2, nlines, half), jnp.bfloat16),
        cost_estimate=pl.CostEstimate(
            flops=2 * nlines * half * 60, transcendentals=0, bytes_accessed=2 * nlines * half * 6
        ),
    )(weights, window, coeff, shift)


def resample_block(padded, shift_lines, kern_lines, shift_range, kern_range):
    table = kernel_table()
    nlines = shift_range.shape[0]
    border = OFFAZ + 4
    start = border + shift_lines - 3
    window = lax.dynamic_slice_in_dim(padded, start, nlines + 7, 1).astype(jnp.float32)
    window = jnp.pad(window, ((0, 0), (0, 1), (0, 0)))
    weights = table[kern_lines]
    coeff = jnp.take(table, kern_range, axis=0)
    shift = (shift_range + OFFRG)[:, None]
    left = look_order(resample_half(0, weights, window, coeff, shift))
    right = look_order(resample_half(1, weights, window, coeff, shift))
    return left, right


CHUNK = 512


def looks_kernel(first_ref, second_ref, out_ref):
    first_re = first_ref[0].astype(jnp.float32)
    first_im = first_ref[1].astype(jnp.float32)
    second_re = second_ref[0].astype(jnp.float32)
    second_im = second_ref[1].astype(jnp.float32)
    real_part = first_re * second_re + first_im * second_im
    imag_part = first_im * second_re - first_re * second_im
    rows = real_part.shape[0]
    groups = rows // LOOK_AZ
    real_lines = real_part.reshape(LOOK_AZ, groups, CHUNK).sum(axis=0)
    imag_lines = imag_part.reshape(LOOK_AZ, groups, CHUNK).sum(axis=0)
    pooling = (
        lax.broadcasted_iota(jnp.int32, (CHUNK, CHUNK // LOOK_RG), 0) // LOOK_RG
        == lax.broadcasted_iota(jnp.int32, (CHUNK, CHUNK // LOOK_RG), 1)
    ).astype(jnp.float32)
    real_looks = jnp.dot(real_lines, pooling, precision=lax.Precision.HIGHEST, preferred_element_type=jnp.float32)
    imag_looks = jnp.dot(imag_lines, pooling, precision=lax.Precision.HIGHEST, preferred_element_type=jnp.float32)
    out_ref[0] = real_looks / (LOOK_AZ * LOOK_RG)
    out_ref[1] = imag_looks / (LOOK_AZ * LOOK_RG)


def looks(first, second):
    nlines = first.shape[1]
    width = first.shape[2]
    groups = nlines // LOOK_AZ
    spec = pl.BlockSpec((2, nlines, CHUNK), lambda j: (0, 0, j))
    return pl.pallas_call(
        looks_kernel,
        grid=(width // CHUNK,),
        in_specs=[spec, spec],
        out_specs=pl.BlockSpec((2, groups, CHUNK // LOOK_RG), lambda j: (0, 0, j)),
        out_shape=jax.ShapeDtypeStruct((2, groups, width // LOOK_RG), jnp.float32),
        cost_estimate=pl.CostEstimate(
            flops=nlines * width * 40, transcendentals=0, bytes_accessed=2 * 2 * nlines * width * 2
        ),
    )(first, second)


def look_order(image):
    nlines = image.shape[1]
    groups = nlines // LOOK_AZ
    return image.reshape(2, groups, LOOK_AZ, image.shape[2]).transpose(0, 2, 1, 3).reshape(image.shape)


def conj(block):
    return jnp.stack([block[0], -block[1]])


def shards(slc, az_offset, az_kernel, rg_offset, rg_kernel, partners):
    padded = padded_2(slc, (("az", 2),), OFFAZ + 4)
    own_left, own_right = resample_block(padded[0], az_offset[0], az_kernel[0], rg_offset[0], rg_kernel[0])
    date = lax.axis_index("date")
    even = date % 2 == 0

    left_2 = shifted(own_left, "date", 2)
    left_1 = swapped(jnp.where(even, left_2, own_left), "date")
    left_4 = shifted(left_2, "date", 2)
    right_2 = shifted(own_right, "date", -2)
    right_1 = swapped(jnp.where(even, own_right, right_2), "date")
    right_4 = shifted(right_2, "date", -2)
    ahead = {2: looks(own_left, left_2)}
    behind = {2: looks(own_right, right_2)}
    left_1, ahead[2] = lax.optimization_barrier((left_1, ahead[2]))
    right_1, behind[2] = lax.optimization_barrier((right_1, behind[2]))
    left_3 = shifted(left_1, "date", 2)
    right_3 = shifted(right_1, "date", -2)
    for s, other in ((1, left_1), (4, left_4), (3, left_3)):
        ahead[s] = looks(own_left, other)
    for s, other in ((1, right_1), (4, right_4), (3, right_3)):
        behind[s] = looks(own_right, other)
    count = lax.axis_size("date")
    target = lax.broadcasted_iota(jnp.int32, (count, 1, 1, 1), 0) - date
    sent = jnp.zeros((count,) + ahead[1].shape, jnp.float32)
    for s in range(1, GAP + 1):
        sent = jnp.where(target == s, ahead[s][None], sent)
        sent = jnp.where(target == -s, behind[s][None], sent)
    got = lax.all_to_all(sent, "date", 0, 0, tiled=True)
    full = {}
    for s in range(1, GAP + 1):
        right_of_ahead = conj(lax.dynamic_index_in_dim(got, jnp.minimum(date + s, count - 1), 0, keepdims=False))
        left_of_behind = conj(lax.dynamic_index_in_dim(got, jnp.maximum(date - s, 0), 0, keepdims=False))
        full[s] = jnp.concatenate([ahead[s], right_of_ahead], axis=2)
        full[-s] = jnp.concatenate([left_of_behind, behind[s]], axis=2)

    listed = partners[0]
    outputs = []
    for slot in range(PARTNERS):
        value = jnp.zeros_like(full[1])
        for step, block in full.items():
            value = jnp.where(listed[slot] == date + step, block, value)
        outputs.append(value)
    return jnp.stack(outputs)[None]


def solution(mesh):
    in_specs = (
        P("date", None, "az", None),
        P("date"),
        P("date"),
        P("date", "az"),
        P("date", "az"),
        P("date", None),
    )
    out_specs = P("date", None, None, "az", None)
    return jax.shard_map(shards, mesh=mesh, in_specs=in_specs, out_specs=out_specs, check_vma=False)
```

```python
import functools

import jax
import jax.numpy as jnp
from jax import lax
from jax.sharding import PartitionSpec as P
from jax.experimental import pallas as pl
from jax.experimental.pallas import tpu as pltpu

PARTNERS = 4
GAP = 4
OFFAZ = 12
OFFRG = 12
NFRAC = 64
LOOK_AZ = 20
LOOK_RG = 4


def padded_2(cells, sides, width):
    for axis, dim in sides:
        count = lax.axis_size(axis)
        ends = count - 1
        head = lax.slice_in_dim(cells, 0, width, axis=dim)
        tail = lax.slice_in_dim(cells, cells.shape[dim] - width, cells.shape[dim], axis=dim)
        cells = jnp.concatenate(
            [
                lax.ppermute(tail, axis, [(i, (i + 1) % count) for i in range(ends)]),
                cells,
                lax.ppermute(head, axis, [((i + 1) % count, i) for i in range(ends)]),
            ],
            axis=dim,
        )
    return cells


def shifted(block, axis, distance):
    count = lax.axis_size(axis)
    route = [(i + distance, i) for i in range(count) if 0 <= i + distance < count]
    return lax.ppermute(block, axis, route)


def swapped(block, axis):
    count = lax.axis_size(axis)
    return lax.ppermute(block, axis, [(i, i ^ 1) for i in range(count)])


def kernel_table():
    frac = jnp.arange(NFRAC, dtype=jnp.float32)[:, None] / NFRAC
    taps = jnp.arange(8, dtype=jnp.float32)[None, :]
    place = taps - 3.0 - frac
    return jnp.sinc(place) * (0.5 + 0.5 * jnp.cos(jnp.pi * place / 4.5))


ROWS = 32
EDGE = 128


def resample_kernel(side, weights_ref, window_ref, coeff_ref, shift_ref, out_ref):
    step = pl.program_id(1)
    first = pl.multiple_of(step * ROWS, ROWS)
    half = out_ref.shape[2]
    low = max(side * half - EDGE, 0)
    high = min(side * half + half + EDGE, window_ref.shape[2])
    window = window_ref[0, pl.ds(first, ROWS + 8), low:high]
    along = weights_ref[0] * window[0:ROWS, :]
    for tap in range(1, 8):
        along = along + weights_ref[tap] * window[tap : tap + ROWS, :]
    zeros = jnp.zeros((ROWS, EDGE), jnp.float32)
    row = jnp.concatenate([zeros, along] if side == 0 else [along, zeros], axis=1)
    width = row.shape[1]
    shift = shift_ref[...]
    for bit in range(5):
        moved = pltpu.roll(row, width - (1 << bit), 1)
        row = jnp.where(((shift >> bit) & 1) == 1, moved, row)
    coeff = coeff_ref[...]
    result = None
    for tap in range(8):
        moved = pltpu.roll(row, width - (EDGE - 15 + tap), 1)[:, :half]
        term = coeff[:, tap : tap + 1] * moved
        result = term if result is None else result + term
    out_ref[0] = result.astype(out_ref.dtype)


def resample_half(side, weights, window, coeff, shift):
    nlines = coeff.shape[0]
    half = window.shape[2] // 2
    return pl.pallas_call(
        functools.partial(resample_kernel, side),
        grid=(2, nlines // ROWS),
        in_specs=[
            pl.BlockSpec(memory_space=pltpu.SMEM),
            pl.BlockSpec((1,) + window.shape[1:], lambda c, t: (c, 0, 0)),
            pl.BlockSpec((ROWS, 8), lambda c, t: (t, 0)),
            pl.BlockSpec((ROWS, 1), lambda c, t: (t, 0)),
        ],
        out_specs=pl.BlockSpec((1, ROWS, half), lambda c, t: (c, t, 0)),
        out_shape=jax.ShapeDtypeStruct((2, nlines, half), jnp.bfloat16),
        cost_estimate=pl.CostEstimate(
            flops=2 * nlines * half * 60, transcendentals=0, bytes_accessed=2 * nlines * half * 6
        ),
    )(weights, window, coeff, shift)


def resample_block(padded, shift_lines, kern_lines, shift_range, kern_range):
    table = kernel_table()
    nlines = shift_range.shape[0]
    border = OFFAZ + 4
    start = border + shift_lines - 3
    window = lax.dynamic_slice_in_dim(padded, start, nlines + 7, 1).astype(jnp.float32)
    window = jnp.pad(window, ((0, 0), (0, 1), (0, 0)))
    weights = table[kern_lines]
    coeff = jnp.take(table, kern_range, axis=0)
    shift = (shift_range + OFFRG)[:, None]
    left = look_order(resample_half(0, weights, window, coeff, shift))
    right = look_order(resample_half(1, weights, window, coeff, shift))
    return left, right


CHUNK = 512


def looks_kernel(first_ref, second_ref, out_ref):
    first_re = first_ref[0].astype(jnp.float32)
    first_im = first_ref[1].astype(jnp.float32)
    second_re = second_ref[0].astype(jnp.float32)
    second_im = second_ref[1].astype(jnp.float32)
    real_part = first_re * second_re + first_im * second_im
    imag_part = first_im * second_re - first_re * second_im
    rows = real_part.shape[0]
    groups = rows // LOOK_AZ
    real_lines = real_part.reshape(LOOK_AZ, groups, CHUNK).sum(axis=0)
    imag_lines = imag_part.reshape(LOOK_AZ, groups, CHUNK).sum(axis=0)
    pooling = (
        lax.broadcasted_iota(jnp.int32, (CHUNK, CHUNK // LOOK_RG), 0) // LOOK_RG
        == lax.broadcasted_iota(jnp.int32, (CHUNK, CHUNK // LOOK_RG), 1)
    ).astype(jnp.float32)
    real_looks = jnp.dot(real_lines, pooling, precision=lax.Precision.HIGHEST, preferred_element_type=jnp.float32)
    imag_looks = jnp.dot(imag_lines, pooling, precision=lax.Precision.HIGHEST, preferred_element_type=jnp.float32)
    out_ref[0] = real_looks / (LOOK_AZ * LOOK_RG)
    out_ref[1] = imag_looks / (LOOK_AZ * LOOK_RG)


def looks(first, second):
    nlines = first.shape[1]
    width = first.shape[2]
    groups = nlines // LOOK_AZ
    spec = pl.BlockSpec((2, nlines, CHUNK), lambda j: (0, 0, j))
    return pl.pallas_call(
        looks_kernel,
        grid=(width // CHUNK,),
        in_specs=[spec, spec],
        out_specs=pl.BlockSpec((2, groups, CHUNK // LOOK_RG), lambda j: (0, 0, j)),
        out_shape=jax.ShapeDtypeStruct((2, groups, width // LOOK_RG), jnp.float32),
        cost_estimate=pl.CostEstimate(
            flops=nlines * width * 40, transcendentals=0, bytes_accessed=2 * 2 * nlines * width * 2
        ),
    )(first, second)


def look_order(image):
    nlines = image.shape[1]
    groups = nlines // LOOK_AZ
    return image.reshape(2, groups, LOOK_AZ, image.shape[2]).transpose(0, 2, 1, 3).reshape(image.shape)


def conj(block):
    return jnp.stack([block[0], -block[1]])


def shards(slc, az_offset, az_kernel, rg_offset, rg_kernel, partners):
    padded = padded_2(slc, (("az", 2),), OFFAZ + 4)
    own_left, own_right = resample_block(padded[0], az_offset[0], az_kernel[0], rg_offset[0], rg_kernel[0])
    date = lax.axis_index("date")
    even = date % 2 == 0

    left_2 = shifted(own_left, "date", 2)
    left_1 = swapped(jnp.where(even, left_2, own_left), "date")
    left_4 = shifted(left_2, "date", 2)
    right_2 = shifted(own_right, "date", -2)
    right_1 = swapped(jnp.where(even, own_right, right_2), "date")
    right_4 = shifted(right_2, "date", -2)
    ahead = {2: looks(own_left, left_2)}
    behind = {2: looks(own_right, right_2)}
    left_1, ahead[2] = lax.optimization_barrier((left_1, ahead[2]))
    right_1, behind[2] = lax.optimization_barrier((right_1, behind[2]))
    left_3 = shifted(left_1, "date", 2)
    right_3 = shifted(right_1, "date", -2)
    for s, other in ((1, left_1), (4, left_4), (3, left_3)):
        ahead[s] = looks(own_left, other)
    for s, other in ((1, right_1), (4, right_4), (3, right_3)):
        behind[s] = looks(own_right, other)
    count = lax.axis_size("date")
    target = lax.broadcasted_iota(jnp.int32, (count, 1, 1, 1), 0) - date
    sent = jnp.zeros((count,) + ahead[1].shape, jnp.float32)
    for s in (1, 2, 4):
        sent = jnp.where(target == s, ahead[s][None], sent)
        sent = jnp.where(target == -s, behind[s][None], sent)
    got = lax.all_to_all(sent, "date", 0, 0, tiled=True)
    full = {}
    for s in range(1, GAP + 1):
        if s == 3:
            right_of_ahead = conj(shifted(behind[s], "date", s))
            left_of_behind = conj(shifted(ahead[s], "date", -s))
        else:
            right_of_ahead = conj(lax.dynamic_index_in_dim(got, jnp.minimum(date + s, count - 1), 0, keepdims=False))
            left_of_behind = conj(lax.dynamic_index_in_dim(got, jnp.maximum(date - s, 0), 0, keepdims=False))
        full[s] = jnp.concatenate([ahead[s], right_of_ahead], axis=2)
        full[-s] = jnp.concatenate([left_of_behind, behind[s]], axis=2)

    listed = partners[0]
    outputs = []
    for slot in range(PARTNERS):
        value = jnp.zeros_like(full[1])
        for step, block in full.items():
            value = jnp.where(listed[slot] == date + step, block, value)
        outputs.append(value)
    return jnp.stack(outputs)[None]


def solution(mesh):
    in_specs = (
        P("date", None, "az", None),
        P("date"),
        P("date"),
        P("date", "az"),
        P("date", "az"),
        P("date", None),
    )
    out_specs = P("date", None, None, "az", None)
    return jax.shard_map(shards, mesh=mesh, in_specs=in_specs, out_specs=out_specs, check_vma=False)
```

```python
import functools

import jax
import jax.numpy as jnp
from jax import lax
from jax.sharding import PartitionSpec as P
from jax.experimental import pallas as pl
from jax.experimental.pallas import tpu as pltpu

PARTNERS = 4
GAP = 4
OFFAZ = 12
OFFRG = 12
NFRAC = 64
LOOK_AZ = 20
LOOK_RG = 4


def padded_2(cells, sides, width):
    for axis, dim in sides:
        count = lax.axis_size(axis)
        ends = count - 1
        head = lax.slice_in_dim(cells, 0, width, axis=dim)
        tail = lax.slice_in_dim(cells, cells.shape[dim] - width, cells.shape[dim], axis=dim)
        cells = jnp.concatenate(
            [
                lax.ppermute(tail, axis, [(i, (i + 1) % count) for i in range(ends)]),
                cells,
                lax.ppermute(head, axis, [((i + 1) % count, i) for i in range(ends)]),
            ],
            axis=dim,
        )
    return cells


def shifted(block, axis, distance):
    count = lax.axis_size(axis)
    route = [(i + distance, i) for i in range(count) if 0 <= i + distance < count]
    return lax.ppermute(block, axis, route)


def swapped(block, axis):
    count = lax.axis_size(axis)
    return lax.ppermute(block, axis, [(i, i ^ 1) for i in range(count)])


def kernel_table():
    frac = jnp.arange(NFRAC, dtype=jnp.float32)[:, None] / NFRAC
    taps = jnp.arange(8, dtype=jnp.float32)[None, :]
    place = taps - 3.0 - frac
    return jnp.sinc(place) * (0.5 + 0.5 * jnp.cos(jnp.pi * place / 4.5))


ROWS = 32
EDGE = 128


def resample_kernel(side, weights_ref, window_ref, coeff_ref, shift_ref, out_ref):
    step = pl.program_id(1)
    first = pl.multiple_of(step * ROWS, ROWS)
    half = out_ref.shape[2]
    low = max(side * half - EDGE, 0)
    high = min(side * half + half + EDGE, window_ref.shape[2])
    window = window_ref[0, pl.ds(first, ROWS + 16), low:high].astype(jnp.float32)
    along = weights_ref[0] * window[0:ROWS, :]
    for tap in range(1, 8):
        along = along + weights_ref[tap] * window[tap : tap + ROWS, :]
    zeros = jnp.zeros((ROWS, EDGE), jnp.float32)
    row = jnp.concatenate([zeros, along] if side == 0 else [along, zeros], axis=1)
    width = row.shape[1]
    shift = shift_ref[...]
    for bit in range(5):
        moved = pltpu.roll(row, width - (1 << bit), 1)
        row = jnp.where(((shift >> bit) & 1) == 1, moved, row)
    coeff = coeff_ref[...]
    result = None
    for tap in range(8):
        moved = pltpu.roll(row, width - (EDGE - 15 + tap), 1)[:, :half]
        term = coeff[:, tap : tap + 1] * moved
        result = term if result is None else result + term
    out_ref[0] = result.astype(out_ref.dtype)


def resample_half(side, weights, window, coeff, shift):
    nlines = coeff.shape[0]
    half = window.shape[2] // 2
    return pl.pallas_call(
        functools.partial(resample_kernel, side),
        grid=(2, nlines // ROWS),
        in_specs=[
            pl.BlockSpec(memory_space=pltpu.SMEM),
            pl.BlockSpec((1,) + window.shape[1:], lambda c, t: (c, 0, 0)),
            pl.BlockSpec((ROWS, 8), lambda c, t: (t, 0)),
            pl.BlockSpec((ROWS, 1), lambda c, t: (t, 0)),
        ],
        out_specs=pl.BlockSpec((1, ROWS, half), lambda c, t: (c, t, 0)),
        out_shape=jax.ShapeDtypeStruct((2, nlines, half), jnp.bfloat16),
        cost_estimate=pl.CostEstimate(
            flops=2 * nlines * half * 60, transcendentals=0, bytes_accessed=2 * nlines * half * 6
        ),
    )(weights, window, coeff, shift)


def resample_block(padded, shift_lines, kern_lines, shift_range, kern_range):
    table = kernel_table()
    nlines = shift_range.shape[0]
    border = OFFAZ + 4
    start = border + shift_lines - 3
    window = lax.dynamic_slice_in_dim(padded, start, nlines + 7, 1)
    window = jnp.pad(window, ((0, 0), (0, 9), (0, 0)))
    weights = table[kern_lines]
    coeff = jnp.take(table, kern_range, axis=0)
    shift = (shift_range + OFFRG)[:, None]
    left = look_order(resample_half(0, weights, window, coeff, shift))
    right = look_order(resample_half(1, weights, window, coeff, shift))
    return left, right


CHUNK = 512


def looks_kernel(first_ref, second_ref, out_ref):
    first_re = first_ref[0].astype(jnp.float32)
    first_im = first_ref[1].astype(jnp.float32)
    second_re = second_ref[0].astype(jnp.float32)
    second_im = second_ref[1].astype(jnp.float32)
    real_part = first_re * second_re + first_im * second_im
    imag_part = first_im * second_re - first_re * second_im
    rows = real_part.shape[0]
    groups = rows // LOOK_AZ
    real_lines = real_part.reshape(LOOK_AZ, groups, CHUNK).sum(axis=0)
    imag_lines = imag_part.reshape(LOOK_AZ, groups, CHUNK).sum(axis=0)
    pooling = (
        lax.broadcasted_iota(jnp.int32, (CHUNK, CHUNK // LOOK_RG), 0) // LOOK_RG
        == lax.broadcasted_iota(jnp.int32, (CHUNK, CHUNK // LOOK_RG), 1)
    ).astype(jnp.float32)
    real_looks = jnp.dot(real_lines, pooling, precision=lax.Precision.HIGHEST, preferred_element_type=jnp.float32)
    imag_looks = jnp.dot(imag_lines, pooling, precision=lax.Precision.HIGHEST, preferred_element_type=jnp.float32)
    out_ref[0] = real_looks / (LOOK_AZ * LOOK_RG)
    out_ref[1] = imag_looks / (LOOK_AZ * LOOK_RG)


def looks(first, second):
    nlines = first.shape[1]
    width = first.shape[2]
    groups = nlines // LOOK_AZ
    spec = pl.BlockSpec((2, nlines, CHUNK), lambda j: (0, 0, j))
    return pl.pallas_call(
        looks_kernel,
        grid=(width // CHUNK,),
        in_specs=[spec, spec],
        out_specs=pl.BlockSpec((2, groups, CHUNK // LOOK_RG), lambda j: (0, 0, j)),
        out_shape=jax.ShapeDtypeStruct((2, groups, width // LOOK_RG), jnp.float32),
        cost_estimate=pl.CostEstimate(
            flops=nlines * width * 40, transcendentals=0, bytes_accessed=2 * 2 * nlines * width * 2
        ),
    )(first, second)


def look_order(image):
    nlines = image.shape[1]
    groups = nlines // LOOK_AZ
    return image.reshape(2, groups, LOOK_AZ, image.shape[2]).transpose(0, 2, 1, 3).reshape(image.shape)


def conj(block):
    return jnp.stack([block[0], -block[1]])


def shards(slc, az_offset, az_kernel, rg_offset, rg_kernel, partners):
    padded = padded_2(slc, (("az", 2),), OFFAZ + 4)
    own_left, own_right = resample_block(padded[0], az_offset[0], az_kernel[0], rg_offset[0], rg_kernel[0])
    date = lax.axis_index("date")
    even = date % 2 == 0

    left_2 = shifted(own_left, "date", 2)
    left_1 = swapped(jnp.where(even, left_2, own_left), "date")
    left_4 = shifted(left_2, "date", 2)
    right_2 = shifted(own_right, "date", -2)
    right_1 = swapped(jnp.where(even, own_right, right_2), "date")
    right_4 = shifted(right_2, "date", -2)
    ahead = {2: looks(own_left, left_2)}
    behind = {2: looks(own_right, right_2)}
    left_1, ahead[2] = lax.optimization_barrier((left_1, ahead[2]))
    right_1, behind[2] = lax.optimization_barrier((right_1, behind[2]))
    left_3 = shifted(left_1, "date", 2)
    right_3 = shifted(right_1, "date", -2)
    for s, other in ((1, left_1), (4, left_4), (3, left_3)):
        ahead[s] = looks(own_left, other)
    for s, other in ((1, right_1), (4, right_4), (3, right_3)):
        behind[s] = looks(own_right, other)
    count = lax.axis_size("date")
    target = lax.broadcasted_iota(jnp.int32, (count, 1, 1, 1), 0) - date
    sent = jnp.zeros((count,) + ahead[1].shape, jnp.float32)
    for s in range(1, GAP + 1):
        sent = jnp.where(target == s, ahead[s][None], sent)
        sent = jnp.where(target == -s, behind[s][None], sent)
    got = lax.all_to_all(sent, "date", 0, 0, tiled=True)
    full = {}
    for s in range(1, GAP + 1):
        right_of_ahead = conj(lax.dynamic_index_in_dim(got, jnp.minimum(date + s, count - 1), 0, keepdims=False))
        left_of_behind = conj(lax.dynamic_index_in_dim(got, jnp.maximum(date - s, 0), 0, keepdims=False))
        full[s] = jnp.concatenate([ahead[s], right_of_ahead], axis=2)
        full[-s] = jnp.concatenate([left_of_behind, behind[s]], axis=2)

    listed = partners[0]
    outputs = []
    for slot in range(PARTNERS):
        value = jnp.zeros_like(full[1])
        for step, block in full.items():
            value = jnp.where(listed[slot] == date + step, block, value)
        outputs.append(value)
    return jnp.stack(outputs)[None]


def solution(mesh):
    in_specs = (
        P("date", None, "az", None),
        P("date"),
        P("date"),
        P("date", "az"),
        P("date", "az"),
        P("date", None),
    )
    out_specs = P("date", None, None, "az", None)
    return jax.shard_map(shards, mesh=mesh, in_specs=in_specs, out_specs=out_specs, check_vma=False)
```

```python
import functools

import jax
import jax.numpy as jnp
from jax import lax
from jax.sharding import PartitionSpec as P
from jax.experimental import pallas as pl
from jax.experimental.pallas import tpu as pltpu

PARTNERS = 4
GAP = 4
OFFAZ = 12
OFFRG = 12
NFRAC = 64
LOOK_AZ = 20
LOOK_RG = 4


def padded_2(cells, sides, width, extra):
    for axis, dim in sides:
        count = lax.axis_size(axis)
        ends = count - 1
        head = lax.slice_in_dim(cells, 0, width + extra, axis=dim)
        tail = lax.slice_in_dim(cells, cells.shape[dim] - width, cells.shape[dim], axis=dim)
        cells = jnp.concatenate(
            [
                lax.ppermute(tail, axis, [(i, (i + 1) % count) for i in range(ends)]),
                cells,
                lax.ppermute(head, axis, [((i + 1) % count, i) for i in range(ends)]),
            ],
            axis=dim,
        )
    return cells


def shifted(block, axis, distance):
    count = lax.axis_size(axis)
    route = [(i + distance, i) for i in range(count) if 0 <= i + distance < count]
    return lax.ppermute(block, axis, route)


def swapped(block, axis):
    count = lax.axis_size(axis)
    return lax.ppermute(block, axis, [(i, i ^ 1) for i in range(count)])


def kernel_table():
    frac = jnp.arange(NFRAC, dtype=jnp.float32)[:, None] / NFRAC
    taps = jnp.arange(8, dtype=jnp.float32)[None, :]
    place = taps - 3.0 - frac
    return jnp.sinc(place) * (0.5 + 0.5 * jnp.cos(jnp.pi * place / 4.5))


ROWS = 32
EDGE = 128


def resample_kernel(side, weights_ref, window_ref, coeff_ref, shift_ref, out_ref):
    step = pl.program_id(1)
    first = pl.multiple_of(step * ROWS, ROWS)
    half = out_ref.shape[2]
    low = max(side * half - EDGE, 0)
    high = min(side * half + half + EDGE, window_ref.shape[2])
    window = window_ref[0, pl.ds(first, ROWS + 16), low:high].astype(jnp.float32)
    along = weights_ref[0] * window[0:ROWS, :]
    for tap in range(1, 8):
        along = along + weights_ref[tap] * window[tap : tap + ROWS, :]
    zeros = jnp.zeros((ROWS, EDGE), jnp.float32)
    row = jnp.concatenate([zeros, along] if side == 0 else [along, zeros], axis=1)
    width = row.shape[1]
    shift = shift_ref[...]
    for bit in range(5):
        moved = pltpu.roll(row, width - (1 << bit), 1)
        row = jnp.where(((shift >> bit) & 1) == 1, moved, row)
    coeff = coeff_ref[...]
    result = None
    for tap in range(8):
        moved = pltpu.roll(row, width - (EDGE - 15 + tap), 1)[:, :half]
        term = coeff[:, tap : tap + 1] * moved
        result = term if result is None else result + term
    out_ref[0] = result.astype(out_ref.dtype)


def resample_half(side, weights, window, coeff, shift):
    nlines = coeff.shape[0]
    half = window.shape[2] // 2
    return pl.pallas_call(
        functools.partial(resample_kernel, side),
        grid=(2, nlines // ROWS),
        in_specs=[
            pl.BlockSpec(memory_space=pltpu.SMEM),
            pl.BlockSpec((1,) + window.shape[1:], lambda c, t: (c, 0, 0)),
            pl.BlockSpec((ROWS, 8), lambda c, t: (t, 0)),
            pl.BlockSpec((ROWS, 1), lambda c, t: (t, 0)),
        ],
        out_specs=pl.BlockSpec((1, ROWS, half), lambda c, t: (c, t, 0)),
        out_shape=jax.ShapeDtypeStruct((2, nlines, half), jnp.bfloat16),
        cost_estimate=pl.CostEstimate(
            flops=2 * nlines * half * 60, transcendentals=0, bytes_accessed=2 * nlines * half * 6
        ),
    )(weights, window, coeff, shift)


def resample_block(padded, shift_lines, kern_lines, shift_range, kern_range):
    table = kernel_table()
    nlines = shift_range.shape[0]
    border = OFFAZ + 4
    start = border + shift_lines - 3
    window = lax.dynamic_slice_in_dim(padded, start, nlines + 16, 1)
    weights = table[kern_lines]
    coeff = jnp.take(table, kern_range, axis=0)
    shift = (shift_range + OFFRG)[:, None]
    left = look_order(resample_half(0, weights, window, coeff, shift))
    right = look_order(resample_half(1, weights, window, coeff, shift))
    return left, right


CHUNK = 512


def looks_kernel(first_ref, second_ref, out_ref):
    first_re = first_ref[0].astype(jnp.float32)
    first_im = first_ref[1].astype(jnp.float32)
    second_re = second_ref[0].astype(jnp.float32)
    second_im = second_ref[1].astype(jnp.float32)
    real_part = first_re * second_re + first_im * second_im
    imag_part = first_im * second_re - first_re * second_im
    rows = real_part.shape[0]
    groups = rows // LOOK_AZ
    real_lines = real_part.reshape(LOOK_AZ, groups, CHUNK).sum(axis=0)
    imag_lines = imag_part.reshape(LOOK_AZ, groups, CHUNK).sum(axis=0)
    pooling = (
        lax.broadcasted_iota(jnp.int32, (CHUNK, CHUNK // LOOK_RG), 0) // LOOK_RG
        == lax.broadcasted_iota(jnp.int32, (CHUNK, CHUNK // LOOK_RG), 1)
    ).astype(jnp.float32)
    real_looks = jnp.dot(real_lines, pooling, precision=lax.Precision.HIGHEST, preferred_element_type=jnp.float32)
    imag_looks = jnp.dot(imag_lines, pooling, precision=lax.Precision.HIGHEST, preferred_element_type=jnp.float32)
    out_ref[0] = real_looks / (LOOK_AZ * LOOK_RG)
    out_ref[1] = imag_looks / (LOOK_AZ * LOOK_RG)


def looks(first, second):
    nlines = first.shape[1]
    width = first.shape[2]
    groups = nlines // LOOK_AZ
    spec = pl.BlockSpec((2, nlines, CHUNK), lambda j: (0, 0, j))
    return pl.pallas_call(
        looks_kernel,
        grid=(width // CHUNK,),
        in_specs=[spec, spec],
        out_specs=pl.BlockSpec((2, groups, CHUNK // LOOK_RG), lambda j: (0, 0, j)),
        out_shape=jax.ShapeDtypeStruct((2, groups, width // LOOK_RG), jnp.float32),
        cost_estimate=pl.CostEstimate(
            flops=nlines * width * 40, transcendentals=0, bytes_accessed=2 * 2 * nlines * width * 2
        ),
    )(first, second)


def look_order(image):
    nlines = image.shape[1]
    groups = nlines // LOOK_AZ
    return image.reshape(2, groups, LOOK_AZ, image.shape[2]).transpose(0, 2, 1, 3).reshape(image.shape)


def conj(block):
    return jnp.stack([block[0], -block[1]])


def shards(slc, az_offset, az_kernel, rg_offset, rg_kernel, partners):
    padded = padded_2(slc, (("az", 2),), OFFAZ + 4, 9)
    own_left, own_right = resample_block(padded[0], az_offset[0], az_kernel[0], rg_offset[0], rg_kernel[0])
    date = lax.axis_index("date")
    even = date % 2 == 0

    left_2 = shifted(own_left, "date", 2)
    left_1 = swapped(jnp.where(even, left_2, own_left), "date")
    left_4 = shifted(left_2, "date", 2)
    right_2 = shifted(own_right, "date", -2)
    right_1 = swapped(jnp.where(even, own_right, right_2), "date")
    right_4 = shifted(right_2, "date", -2)
    ahead = {2: looks(own_left, left_2)}
    behind = {2: looks(own_right, right_2)}
    left_1, ahead[2] = lax.optimization_barrier((left_1, ahead[2]))
    right_1, behind[2] = lax.optimization_barrier((right_1, behind[2]))
    left_3 = shifted(left_1, "date", 2)
    right_3 = shifted(right_1, "date", -2)
    for s, other in ((1, left_1), (4, left_4), (3, left_3)):
        ahead[s] = looks(own_left, other)
    for s, other in ((1, right_1), (4, right_4), (3, right_3)):
        behind[s] = looks(own_right, other)
    count = lax.axis_size("date")
    target = lax.broadcasted_iota(jnp.int32, (count, 1, 1, 1), 0) - date
    sent = jnp.zeros((count,) + ahead[1].shape, jnp.float32)
    for s in range(1, GAP + 1):
        sent = jnp.where(target == s, ahead[s][None], sent)
        sent = jnp.where(target == -s, behind[s][None], sent)
    got = lax.all_to_all(sent, "date", 0, 0, tiled=True)
    full = {}
    for s in range(1, GAP + 1):
        right_of_ahead = conj(lax.dynamic_index_in_dim(got, jnp.minimum(date + s, count - 1), 0, keepdims=False))
        left_of_behind = conj(lax.dynamic_index_in_dim(got, jnp.maximum(date - s, 0), 0, keepdims=False))
        full[s] = jnp.concatenate([ahead[s], right_of_ahead], axis=2)
        full[-s] = jnp.concatenate([left_of_behind, behind[s]], axis=2)

    listed = partners[0]
    outputs = []
    for slot in range(PARTNERS):
        value = jnp.zeros_like(full[1])
        for step, block in full.items():
            value = jnp.where(listed[slot] == date + step, block, value)
        outputs.append(value)
    return jnp.stack(outputs)[None]


def solution(mesh):
    in_specs = (
        P("date", None, "az", None),
        P("date"),
        P("date"),
        P("date", "az"),
        P("date", "az"),
        P("date", None),
    )
    out_specs = P("date", None, None, "az", None)
    return jax.shard_map(shards, mesh=mesh, in_specs=in_specs, out_specs=out_specs, check_vma=False)
```

```python
import functools

import jax
import jax.numpy as jnp
from jax import lax
from jax.sharding import PartitionSpec as P
from jax.experimental import pallas as pl
from jax.experimental.pallas import tpu as pltpu

PARTNERS = 4
GAP = 4
OFFAZ = 12
OFFRG = 12
NFRAC = 64
LOOK_AZ = 20
LOOK_RG = 4


def padded_2(cells, sides, width, extra):
    for axis, dim in sides:
        count = lax.axis_size(axis)
        ends = count - 1
        head = lax.slice_in_dim(cells, 0, width + extra, axis=dim)
        tail = lax.slice_in_dim(cells, cells.shape[dim] - width, cells.shape[dim], axis=dim)
        cells = jnp.concatenate(
            [
                lax.ppermute(tail, axis, [(i, (i + 1) % count) for i in range(ends)]),
                cells,
                lax.ppermute(head, axis, [((i + 1) % count, i) for i in range(ends)]),
            ],
            axis=dim,
        )
    return cells


def shifted(block, axis, distance):
    count = lax.axis_size(axis)
    route = [(i + distance, i) for i in range(count) if 0 <= i + distance < count]
    return lax.ppermute(block, axis, route)


def swapped(block, axis):
    count = lax.axis_size(axis)
    return lax.ppermute(block, axis, [(i, i ^ 1) for i in range(count)])


def kernel_table():
    frac = jnp.arange(NFRAC, dtype=jnp.float32)[:, None] / NFRAC
    taps = jnp.arange(8, dtype=jnp.float32)[None, :]
    place = taps - 3.0 - frac
    return jnp.sinc(place) * (0.5 + 0.5 * jnp.cos(jnp.pi * place / 4.5))


ROWS = 80
EDGE = 128


def resample_kernel(side, weights_ref, window_ref, coeff_ref, shift_ref, out_ref):
    step = pl.program_id(1)
    first = pl.multiple_of(step * ROWS, ROWS)
    half = out_ref.shape[2]
    low = max(side * half - EDGE, 0)
    high = min(side * half + half + EDGE, window_ref.shape[2])
    window = window_ref[0, pl.ds(first, ROWS + 16), low:high].astype(jnp.float32)
    along = weights_ref[0] * window[0:ROWS, :]
    for tap in range(1, 8):
        along = along + weights_ref[tap] * window[tap : tap + ROWS, :]
    zeros = jnp.zeros((ROWS, EDGE), jnp.float32)
    row = jnp.concatenate([zeros, along] if side == 0 else [along, zeros], axis=1)
    width = row.shape[1]
    shift = shift_ref[...]
    for bit in range(5):
        moved = pltpu.roll(row, width - (1 << bit), 1)
        row = jnp.where(((shift >> bit) & 1) == 1, moved, row)
    coeff = coeff_ref[...]
    result = None
    for tap in range(8):
        moved = pltpu.roll(row, width - (EDGE - 15 + tap), 1)[:, :half]
        term = coeff[:, tap : tap + 1] * moved
        result = term if result is None else result + term
    out_ref[0] = result.astype(out_ref.dtype)


def resample_half(side, weights, window, coeff, shift):
    nlines = coeff.shape[0]
    half = window.shape[2] // 2
    return pl.pallas_call(
        functools.partial(resample_kernel, side),
        grid=(2, nlines // ROWS),
        in_specs=[
            pl.BlockSpec(memory_space=pltpu.SMEM),
            pl.BlockSpec((1,) + window.shape[1:], lambda c, t: (c, 0, 0)),
            pl.BlockSpec((ROWS, 8), lambda c, t: (t, 0)),
            pl.BlockSpec((ROWS, 1), lambda c, t: (t, 0)),
        ],
        out_specs=pl.BlockSpec((1, ROWS, half), lambda c, t: (c, t, 0)),
        out_shape=jax.ShapeDtypeStruct((2, nlines, half), jnp.bfloat16),
        cost_estimate=pl.CostEstimate(
            flops=2 * nlines * half * 60, transcendentals=0, bytes_accessed=2 * nlines * half * 6
        ),
    )(weights, window, coeff, shift)


def resample_block(padded, shift_lines, kern_lines, shift_range, kern_range):
    table = kernel_table()
    nlines = shift_range.shape[0]
    border = OFFAZ + 4
    start = border + shift_lines - 3
    window = lax.dynamic_slice_in_dim(padded, start, nlines + 16, 1)
    weights = table[kern_lines]
    coeff = jnp.take(table, kern_range, axis=0)
    shift = (shift_range + OFFRG)[:, None]
    left = look_order(resample_half(0, weights, window, coeff, shift))
    right = look_order(resample_half(1, weights, window, coeff, shift))
    return left, right


CHUNK = 512


def looks_kernel(first_ref, second_ref, out_ref):
    first_re = first_ref[0].astype(jnp.float32)
    first_im = first_ref[1].astype(jnp.float32)
    second_re = second_ref[0].astype(jnp.float32)
    second_im = second_ref[1].astype(jnp.float32)
    real_part = first_re * second_re + first_im * second_im
    imag_part = first_im * second_re - first_re * second_im
    rows = real_part.shape[0]
    groups = rows // LOOK_AZ
    real_lines = real_part.reshape(LOOK_AZ, groups, CHUNK).sum(axis=0)
    imag_lines = imag_part.reshape(LOOK_AZ, groups, CHUNK).sum(axis=0)
    pooling = (
        lax.broadcasted_iota(jnp.int32, (CHUNK, CHUNK // LOOK_RG), 0) // LOOK_RG
        == lax.broadcasted_iota(jnp.int32, (CHUNK, CHUNK // LOOK_RG), 1)
    ).astype(jnp.float32)
    real_looks = jnp.dot(real_lines, pooling, precision=lax.Precision.HIGHEST, preferred_element_type=jnp.float32)
    imag_looks = jnp.dot(imag_lines, pooling, precision=lax.Precision.HIGHEST, preferred_element_type=jnp.float32)
    out_ref[0] = real_looks / (LOOK_AZ * LOOK_RG)
    out_ref[1] = imag_looks / (LOOK_AZ * LOOK_RG)


def looks(first, second):
    nlines = first.shape[1]
    width = first.shape[2]
    groups = nlines // LOOK_AZ
    spec = pl.BlockSpec((2, nlines, CHUNK), lambda j: (0, 0, j))
    return pl.pallas_call(
        looks_kernel,
        grid=(width // CHUNK,),
        in_specs=[spec, spec],
        out_specs=pl.BlockSpec((2, groups, CHUNK // LOOK_RG), lambda j: (0, 0, j)),
        out_shape=jax.ShapeDtypeStruct((2, groups, width // LOOK_RG), jnp.float32),
        cost_estimate=pl.CostEstimate(
            flops=nlines * width * 40, transcendentals=0, bytes_accessed=2 * 2 * nlines * width * 2
        ),
    )(first, second)


def look_order(image):
    nlines = image.shape[1]
    groups = nlines // LOOK_AZ
    return image.reshape(2, groups, LOOK_AZ, image.shape[2]).transpose(0, 2, 1, 3).reshape(image.shape)


def conj(block):
    return jnp.stack([block[0], -block[1]])


def shards(slc, az_offset, az_kernel, rg_offset, rg_kernel, partners):
    padded = padded_2(slc, (("az", 2),), OFFAZ + 4, 9)
    own_left, own_right = resample_block(padded[0], az_offset[0], az_kernel[0], rg_offset[0], rg_kernel[0])
    date = lax.axis_index("date")
    even = date % 2 == 0

    left_2 = shifted(own_left, "date", 2)
    left_1 = swapped(jnp.where(even, left_2, own_left), "date")
    left_4 = shifted(left_2, "date", 2)
    right_2 = shifted(own_right, "date", -2)
    right_1 = swapped(jnp.where(even, own_right, right_2), "date")
    right_4 = shifted(right_2, "date", -2)
    ahead = {2: looks(own_left, left_2)}
    behind = {2: looks(own_right, right_2)}
    left_1, ahead[2] = lax.optimization_barrier((left_1, ahead[2]))
    right_1, behind[2] = lax.optimization_barrier((right_1, behind[2]))
    left_3 = shifted(left_1, "date", 2)
    right_3 = shifted(right_1, "date", -2)
    for s, other in ((1, left_1), (4, left_4), (3, left_3)):
        ahead[s] = looks(own_left, other)
    for s, other in ((1, right_1), (4, right_4), (3, right_3)):
        behind[s] = looks(own_right, other)
    count = lax.axis_size("date")
    target = lax.broadcasted_iota(jnp.int32, (count, 1, 1, 1), 0) - date
    sent = jnp.zeros((count,) + ahead[1].shape, jnp.float32)
    for s in range(1, GAP + 1):
        sent = jnp.where(target == s, ahead[s][None], sent)
        sent = jnp.where(target == -s, behind[s][None], sent)
    got = lax.all_to_all(sent, "date", 0, 0, tiled=True)
    full = {}
    for s in range(1, GAP + 1):
        right_of_ahead = conj(lax.dynamic_index_in_dim(got, jnp.minimum(date + s, count - 1), 0, keepdims=False))
        left_of_behind = conj(lax.dynamic_index_in_dim(got, jnp.maximum(date - s, 0), 0, keepdims=False))
        full[s] = jnp.concatenate([ahead[s], right_of_ahead], axis=2)
        full[-s] = jnp.concatenate([left_of_behind, behind[s]], axis=2)

    listed = partners[0]
    outputs = []
    for slot in range(PARTNERS):
        value = jnp.zeros_like(full[1])
        for step, block in full.items():
            value = jnp.where(listed[slot] == date + step, block, value)
        outputs.append(value)
    return jnp.stack(outputs)[None]


def solution(mesh):
    in_specs = (
        P("date", None, "az", None),
        P("date"),
        P("date"),
        P("date", "az"),
        P("date", "az"),
        P("date", None),
    )
    out_specs = P("date", None, None, "az", None)
    return jax.shard_map(shards, mesh=mesh, in_specs=in_specs, out_specs=out_specs, check_vma=False)
```

```python
import functools

import jax
import jax.numpy as jnp
from jax import lax
from jax.sharding import PartitionSpec as P
from jax.experimental import pallas as pl
from jax.experimental.pallas import tpu as pltpu

PARTNERS = 4
GAP = 4
OFFAZ = 12
OFFRG = 12
NFRAC = 64
LOOK_AZ = 20
LOOK_RG = 4


def padded_2(cells, sides, width, extra):
    for axis, dim in sides:
        count = lax.axis_size(axis)
        ends = count - 1
        head = lax.slice_in_dim(cells, 0, width + extra, axis=dim)
        tail = lax.slice_in_dim(cells, cells.shape[dim] - width, cells.shape[dim], axis=dim)
        cells = jnp.concatenate(
            [
                lax.ppermute(tail, axis, [(i, (i + 1) % count) for i in range(ends)]),
                cells,
                lax.ppermute(head, axis, [((i + 1) % count, i) for i in range(ends)]),
            ],
            axis=dim,
        )
    return cells


def shifted(block, axis, distance):
    count = lax.axis_size(axis)
    route = [(i + distance, i) for i in range(count) if 0 <= i + distance < count]
    return lax.ppermute(block, axis, route)


def swapped(block, axis):
    count = lax.axis_size(axis)
    return lax.ppermute(block, axis, [(i, i ^ 1) for i in range(count)])


def kernel_table():
    frac = jnp.arange(NFRAC, dtype=jnp.float32)[:, None] / NFRAC
    taps = jnp.arange(8, dtype=jnp.float32)[None, :]
    place = taps - 3.0 - frac
    return jnp.sinc(place) * (0.5 + 0.5 * jnp.cos(jnp.pi * place / 4.5))


ROWS = 160
EDGE = 128


def resample_kernel(side, weights_ref, window_ref, coeff_ref, shift_ref, out_ref):
    step = pl.program_id(1)
    first = pl.multiple_of(step * ROWS, ROWS)
    half = out_ref.shape[2]
    low = max(side * half - EDGE, 0)
    high = min(side * half + half + EDGE, window_ref.shape[2])
    window = window_ref[0, pl.ds(first, ROWS + 16), low:high].astype(jnp.float32)
    along = weights_ref[0] * window[0:ROWS, :]
    for tap in range(1, 8):
        along = along + weights_ref[tap] * window[tap : tap + ROWS, :]
    zeros = jnp.zeros((ROWS, EDGE), jnp.float32)
    row = jnp.concatenate([zeros, along] if side == 0 else [along, zeros], axis=1)
    width = row.shape[1]
    shift = shift_ref[...]
    for bit in range(5):
        moved = pltpu.roll(row, width - (1 << bit), 1)
        row = jnp.where(((shift >> bit) & 1) == 1, moved, row)
    coeff = coeff_ref[...]
    result = None
    for tap in range(8):
        moved = pltpu.roll(row, width - (EDGE - 15 + tap), 1)[:, :half]
        term = coeff[:, tap : tap + 1] * moved
        result = term if result is None else result + term
    out_ref[0] = result.astype(out_ref.dtype)


def resample_half(side, weights, window, coeff, shift):
    nlines = coeff.shape[0]
    half = window.shape[2] // 2
    return pl.pallas_call(
        functools.partial(resample_kernel, side),
        grid=(2, nlines // ROWS),
        in_specs=[
            pl.BlockSpec(memory_space=pltpu.SMEM),
            pl.BlockSpec((1,) + window.shape[1:], lambda c, t: (c, 0, 0)),
            pl.BlockSpec((ROWS, 8), lambda c, t: (t, 0)),
            pl.BlockSpec((ROWS, 1), lambda c, t: (t, 0)),
        ],
        out_specs=pl.BlockSpec((1, ROWS, half), lambda c, t: (c, t, 0)),
        out_shape=jax.ShapeDtypeStruct((2, nlines, half), jnp.bfloat16),
        cost_estimate=pl.CostEstimate(
            flops=2 * nlines * half * 60, transcendentals=0, bytes_accessed=2 * nlines * half * 6
        ),
    )(weights, window, coeff, shift)


def resample_block(padded, shift_lines, kern_lines, shift_range, kern_range):
    table = kernel_table()
    nlines = shift_range.shape[0]
    border = OFFAZ + 4
    start = border + shift_lines - 3
    window = lax.dynamic_slice_in_dim(padded, start, nlines + 16, 1)
    weights = table[kern_lines]
    coeff = jnp.take(table, kern_range, axis=0)
    shift = (shift_range + OFFRG)[:, None]
    left = look_order(resample_half(0, weights, window, coeff, shift))
    right = look_order(resample_half(1, weights, window, coeff, shift))
    return left, right


CHUNK = 512


def looks_kernel(first_ref, second_ref, out_ref):
    first_re = first_ref[0].astype(jnp.float32)
    first_im = first_ref[1].astype(jnp.float32)
    second_re = second_ref[0].astype(jnp.float32)
    second_im = second_ref[1].astype(jnp.float32)
    real_part = first_re * second_re + first_im * second_im
    imag_part = first_im * second_re - first_re * second_im
    rows = real_part.shape[0]
    groups = rows // LOOK_AZ
    real_lines = real_part.reshape(LOOK_AZ, groups, CHUNK).sum(axis=0)
    imag_lines = imag_part.reshape(LOOK_AZ, groups, CHUNK).sum(axis=0)
    pooling = (
        lax.broadcasted_iota(jnp.int32, (CHUNK, CHUNK // LOOK_RG), 0) // LOOK_RG
        == lax.broadcasted_iota(jnp.int32, (CHUNK, CHUNK // LOOK_RG), 1)
    ).astype(jnp.float32)
    real_looks = jnp.dot(real_lines, pooling, precision=lax.Precision.HIGHEST, preferred_element_type=jnp.float32)
    imag_looks = jnp.dot(imag_lines, pooling, precision=lax.Precision.HIGHEST, preferred_element_type=jnp.float32)
    out_ref[0] = real_looks / (LOOK_AZ * LOOK_RG)
    out_ref[1] = imag_looks / (LOOK_AZ * LOOK_RG)


def looks(first, second):
    nlines = first.shape[1]
    width = first.shape[2]
    groups = nlines // LOOK_AZ
    spec = pl.BlockSpec((2, nlines, CHUNK), lambda j: (0, 0, j))
    return pl.pallas_call(
        looks_kernel,
        grid=(width // CHUNK,),
        in_specs=[spec, spec],
        out_specs=pl.BlockSpec((2, groups, CHUNK // LOOK_RG), lambda j: (0, 0, j)),
        out_shape=jax.ShapeDtypeStruct((2, groups, width // LOOK_RG), jnp.float32),
        cost_estimate=pl.CostEstimate(
            flops=nlines * width * 40, transcendentals=0, bytes_accessed=2 * 2 * nlines * width * 2
        ),
    )(first, second)


def look_order(image):
    nlines = image.shape[1]
    groups = nlines // LOOK_AZ
    return image.reshape(2, groups, LOOK_AZ, image.shape[2]).transpose(0, 2, 1, 3).reshape(image.shape)


def conj(block):
    return jnp.stack([block[0], -block[1]])


def shards(slc, az_offset, az_kernel, rg_offset, rg_kernel, partners):
    padded = padded_2(slc, (("az", 2),), OFFAZ + 4, 9)
    own_left, own_right = resample_block(padded[0], az_offset[0], az_kernel[0], rg_offset[0], rg_kernel[0])
    date = lax.axis_index("date")
    even = date % 2 == 0

    left_2 = shifted(own_left, "date", 2)
    left_1 = swapped(jnp.where(even, left_2, own_left), "date")
    left_4 = shifted(left_2, "date", 2)
    right_2 = shifted(own_right, "date", -2)
    right_1 = swapped(jnp.where(even, own_right, right_2), "date")
    right_4 = shifted(right_2, "date", -2)
    ahead = {2: looks(own_left, left_2)}
    behind = {2: looks(own_right, right_2)}
    left_1, ahead[2] = lax.optimization_barrier((left_1, ahead[2]))
    right_1, behind[2] = lax.optimization_barrier((right_1, behind[2]))
    left_3 = shifted(left_1, "date", 2)
    right_3 = shifted(right_1, "date", -2)
    for s, other in ((1, left_1), (4, left_4), (3, left_3)):
        ahead[s] = looks(own_left, other)
    for s, other in ((1, right_1), (4, right_4), (3, right_3)):
        behind[s] = looks(own_right, other)
    count = lax.axis_size("date")
    target = lax.broadcasted_iota(jnp.int32, (count, 1, 1, 1), 0) - date
    sent = jnp.zeros((count,) + ahead[1].shape, jnp.float32)
    for s in range(1, GAP + 1):
        sent = jnp.where(target == s, ahead[s][None], sent)
        sent = jnp.where(target == -s, behind[s][None], sent)
    got = lax.all_to_all(sent, "date", 0, 0, tiled=True)
    full = {}
    for s in range(1, GAP + 1):
        right_of_ahead = conj(lax.dynamic_index_in_dim(got, jnp.minimum(date + s, count - 1), 0, keepdims=False))
        left_of_behind = conj(lax.dynamic_index_in_dim(got, jnp.maximum(date - s, 0), 0, keepdims=False))
        full[s] = jnp.concatenate([ahead[s], right_of_ahead], axis=2)
        full[-s] = jnp.concatenate([left_of_behind, behind[s]], axis=2)

    listed = partners[0]
    outputs = []
    for slot in range(PARTNERS):
        value = jnp.zeros_like(full[1])
        for step, block in full.items():
            value = jnp.where(listed[slot] == date + step, block, value)
        outputs.append(value)
    return jnp.stack(outputs)[None]


def solution(mesh):
    in_specs = (
        P("date", None, "az", None),
        P("date"),
        P("date"),
        P("date", "az"),
        P("date", "az"),
        P("date", None),
    )
    out_specs = P("date", None, None, "az", None)
    return jax.shard_map(shards, mesh=mesh, in_specs=in_specs, out_specs=out_specs, check_vma=False)
```

```python
import functools

import jax
import jax.numpy as jnp
from jax import lax
from jax.sharding import PartitionSpec as P
from jax.experimental import pallas as pl
from jax.experimental.pallas import tpu as pltpu

PARTNERS = 4
GAP = 4
OFFAZ = 12
OFFRG = 12
NFRAC = 64
LOOK_AZ = 20
LOOK_RG = 4


def padded_2(cells, sides, width, extra):
    for axis, dim in sides:
        count = lax.axis_size(axis)
        ends = count - 1
        head = lax.slice_in_dim(cells, 0, width + extra, axis=dim)
        tail = lax.slice_in_dim(cells, cells.shape[dim] - width, cells.shape[dim], axis=dim)
        cells = jnp.concatenate(
            [
                lax.ppermute(tail, axis, [(i, (i + 1) % count) for i in range(ends)]),
                cells,
                lax.ppermute(head, axis, [((i + 1) % count, i) for i in range(ends)]),
            ],
            axis=dim,
        )
    return cells


def shifted(block, axis, distance):
    count = lax.axis_size(axis)
    route = [(i + distance, i) for i in range(count) if 0 <= i + distance < count]
    return lax.ppermute(block, axis, route)


def swapped(block, axis):
    count = lax.axis_size(axis)
    return lax.ppermute(block, axis, [(i, i ^ 1) for i in range(count)])


def kernel_table():
    frac = jnp.arange(NFRAC, dtype=jnp.float32)[:, None] / NFRAC
    taps = jnp.arange(8, dtype=jnp.float32)[None, :]
    place = taps - 3.0 - frac
    return jnp.sinc(place) * (0.5 + 0.5 * jnp.cos(jnp.pi * place / 4.5))


ROWS = 160
EDGE = 128


def resample_kernel(side, weights_ref, window_ref, coeff_ref, shift_ref, out_ref):
    step = pl.program_id(1)
    first = pl.multiple_of(step * ROWS, ROWS)
    half = out_ref.shape[2]
    low = max(side * half - EDGE, 0)
    high = min(side * half + half + EDGE, window_ref.shape[2])
    window = window_ref[0, :, low:high].astype(jnp.float32)
    groups = ROWS // LOOK_AZ
    place = lax.broadcasted_iota(jnp.int32, (ROWS, window.shape[0]), 0)
    line = LOOK_AZ * (place % groups) + place // groups
    offset = lax.broadcasted_iota(jnp.int32, (ROWS, window.shape[0]), 1) - line
    taps = jnp.zeros((ROWS, window.shape[0]), jnp.float32)
    for tap in range(8):
        taps = jnp.where(offset == tap, weights_ref[tap], taps)
    along = jnp.dot(taps, window, precision=lax.Precision.HIGHEST, preferred_element_type=jnp.float32)
    zeros = jnp.zeros((ROWS, EDGE), jnp.float32)
    row = jnp.concatenate([zeros, along] if side == 0 else [along, zeros], axis=1)
    width = row.shape[1]
    shift = shift_ref[...]
    for bit in range(5):
        moved = pltpu.roll(row, width - (1 << bit), 1)
        row = jnp.where(((shift >> bit) & 1) == 1, moved, row)
    coeff = coeff_ref[...]
    result = None
    for tap in range(8):
        moved = pltpu.roll(row, width - (EDGE - 15 + tap), 1)[:, :half]
        term = coeff[:, tap : tap + 1] * moved
        result = term if result is None else result + term
    out_ref[0] = result.astype(out_ref.dtype)


def resample_half(side, weights, window, coeff, shift):
    nlines = coeff.shape[0]
    half = window.shape[2] // 2
    return pl.pallas_call(
        functools.partial(resample_kernel, side),
        grid=(2, nlines // ROWS),
        in_specs=[
            pl.BlockSpec(memory_space=pltpu.SMEM),
            pl.BlockSpec((1,) + window.shape[1:], lambda c, t: (c, 0, 0)),
            pl.BlockSpec((ROWS, 8), lambda c, t: (t, 0)),
            pl.BlockSpec((ROWS, 1), lambda c, t: (t, 0)),
        ],
        out_specs=pl.BlockSpec((1, ROWS, half), lambda c, t: (c, t, 0)),
        out_shape=jax.ShapeDtypeStruct((2, nlines, half), jnp.bfloat16),
        cost_estimate=pl.CostEstimate(
            flops=2 * nlines * half * 60, transcendentals=0, bytes_accessed=2 * nlines * half * 6
        ),
    )(weights, window, coeff, shift)


def resample_block(padded, shift_lines, kern_lines, shift_range, kern_range):
    table = kernel_table()
    nlines = shift_range.shape[0]
    border = OFFAZ + 4
    start = border + shift_lines - 3
    window = lax.dynamic_slice_in_dim(padded, start, nlines + 16, 1)
    weights = table[kern_lines]
    coeff = lines_in_look_order(jnp.take(table, kern_range, axis=0))
    shift = lines_in_look_order((shift_range + OFFRG)[:, None])
    left = resample_half(0, weights, window, coeff, shift)
    right = resample_half(1, weights, window, coeff, shift)
    return left, right


def lines_in_look_order(values):
    nlines = values.shape[0]
    return values.reshape(nlines // LOOK_AZ, LOOK_AZ, -1).transpose(1, 0, 2).reshape(nlines, -1)


CHUNK = 512


def looks_kernel(first_ref, second_ref, out_ref):
    first_re = first_ref[0].astype(jnp.float32)
    first_im = first_ref[1].astype(jnp.float32)
    second_re = second_ref[0].astype(jnp.float32)
    second_im = second_ref[1].astype(jnp.float32)
    real_part = first_re * second_re + first_im * second_im
    imag_part = first_im * second_re - first_re * second_im
    rows = real_part.shape[0]
    groups = rows // LOOK_AZ
    real_lines = real_part.reshape(LOOK_AZ, groups, CHUNK).sum(axis=0)
    imag_lines = imag_part.reshape(LOOK_AZ, groups, CHUNK).sum(axis=0)
    pooling = (
        lax.broadcasted_iota(jnp.int32, (CHUNK, CHUNK // LOOK_RG), 0) // LOOK_RG
        == lax.broadcasted_iota(jnp.int32, (CHUNK, CHUNK // LOOK_RG), 1)
    ).astype(jnp.float32)
    real_looks = jnp.dot(real_lines, pooling, precision=lax.Precision.HIGHEST, preferred_element_type=jnp.float32)
    imag_looks = jnp.dot(imag_lines, pooling, precision=lax.Precision.HIGHEST, preferred_element_type=jnp.float32)
    out_ref[0] = real_looks / (LOOK_AZ * LOOK_RG)
    out_ref[1] = imag_looks / (LOOK_AZ * LOOK_RG)


def looks(first, second):
    nlines = first.shape[1]
    width = first.shape[2]
    groups = nlines // LOOK_AZ
    spec = pl.BlockSpec((2, nlines, CHUNK), lambda j: (0, 0, j))
    return pl.pallas_call(
        looks_kernel,
        grid=(width // CHUNK,),
        in_specs=[spec, spec],
        out_specs=pl.BlockSpec((2, groups, CHUNK // LOOK_RG), lambda j: (0, 0, j)),
        out_shape=jax.ShapeDtypeStruct((2, groups, width // LOOK_RG), jnp.float32),
        cost_estimate=pl.CostEstimate(
            flops=nlines * width * 40, transcendentals=0, bytes_accessed=2 * 2 * nlines * width * 2
        ),
    )(first, second)


def look_order(image):
    nlines = image.shape[1]
    groups = nlines // LOOK_AZ
    return image.reshape(2, groups, LOOK_AZ, image.shape[2]).transpose(0, 2, 1, 3).reshape(image.shape)


def conj(block):
    return jnp.stack([block[0], -block[1]])


def shards(slc, az_offset, az_kernel, rg_offset, rg_kernel, partners):
    padded = padded_2(slc, (("az", 2),), OFFAZ + 4, 9)
    own_left, own_right = resample_block(padded[0], az_offset[0], az_kernel[0], rg_offset[0], rg_kernel[0])
    date = lax.axis_index("date")
    even = date % 2 == 0

    left_2 = shifted(own_left, "date", 2)
    left_1 = swapped(jnp.where(even, left_2, own_left), "date")
    left_4 = shifted(left_2, "date", 2)
    right_2 = shifted(own_right, "date", -2)
    right_1 = swapped(jnp.where(even, own_right, right_2), "date")
    right_4 = shifted(right_2, "date", -2)
    ahead = {2: looks(own_left, left_2)}
    behind = {2: looks(own_right, right_2)}
    left_1, ahead[2] = lax.optimization_barrier((left_1, ahead[2]))
    right_1, behind[2] = lax.optimization_barrier((right_1, behind[2]))
    left_3 = shifted(left_1, "date", 2)
    right_3 = shifted(right_1, "date", -2)
    for s, other in ((1, left_1), (4, left_4), (3, left_3)):
        ahead[s] = looks(own_left, other)
    for s, other in ((1, right_1), (4, right_4), (3, right_3)):
        behind[s] = looks(own_right, other)
    count = lax.axis_size("date")
    target = lax.broadcasted_iota(jnp.int32, (count, 1, 1, 1), 0) - date
    sent = jnp.zeros((count,) + ahead[1].shape, jnp.float32)
    for s in range(1, GAP + 1):
        sent = jnp.where(target == s, ahead[s][None], sent)
        sent = jnp.where(target == -s, behind[s][None], sent)
    got = lax.all_to_all(sent, "date", 0, 0, tiled=True)
    full = {}
    for s in range(1, GAP + 1):
        right_of_ahead = conj(lax.dynamic_index_in_dim(got, jnp.minimum(date + s, count - 1), 0, keepdims=False))
        left_of_behind = conj(lax.dynamic_index_in_dim(got, jnp.maximum(date - s, 0), 0, keepdims=False))
        full[s] = jnp.concatenate([ahead[s], right_of_ahead], axis=2)
        full[-s] = jnp.concatenate([left_of_behind, behind[s]], axis=2)

    listed = partners[0]
    outputs = []
    for slot in range(PARTNERS):
        value = jnp.zeros_like(full[1])
        for step, block in full.items():
            value = jnp.where(listed[slot] == date + step, block, value)
        outputs.append(value)
    return jnp.stack(outputs)[None]


def solution(mesh):
    in_specs = (
        P("date", None, "az", None),
        P("date"),
        P("date"),
        P("date", "az"),
        P("date", "az"),
        P("date", None),
    )
    out_specs = P("date", None, None, "az", None)
    return jax.shard_map(shards, mesh=mesh, in_specs=in_specs, out_specs=out_specs, check_vma=False)
```

```python
import functools

import jax
import jax.numpy as jnp
from jax import lax
from jax.sharding import PartitionSpec as P
from jax.experimental import pallas as pl
from jax.experimental.pallas import tpu as pltpu

PARTNERS = 4
GAP = 4
OFFAZ = 12
OFFRG = 12
NFRAC = 64
LOOK_AZ = 20
LOOK_RG = 4


def padded_2(cells, sides, width, extra):
    for axis, dim in sides:
        count = lax.axis_size(axis)
        ends = count - 1
        head = lax.slice_in_dim(cells, 0, width + extra, axis=dim)
        tail = lax.slice_in_dim(cells, cells.shape[dim] - width, cells.shape[dim], axis=dim)
        cells = jnp.concatenate(
            [
                lax.ppermute(tail, axis, [(i, (i + 1) % count) for i in range(ends)]),
                cells,
                lax.ppermute(head, axis, [((i + 1) % count, i) for i in range(ends)]),
            ],
            axis=dim,
        )
    return cells


def shifted(block, axis, distance):
    count = lax.axis_size(axis)
    route = [(i + distance, i) for i in range(count) if 0 <= i + distance < count]
    return lax.ppermute(block, axis, route)


def swapped(block, axis):
    count = lax.axis_size(axis)
    return lax.ppermute(block, axis, [(i, i ^ 1) for i in range(count)])


def kernel_table():
    frac = jnp.arange(NFRAC, dtype=jnp.float32)[:, None] / NFRAC
    taps = jnp.arange(8, dtype=jnp.float32)[None, :]
    place = taps - 3.0 - frac
    return jnp.sinc(place) * (0.5 + 0.5 * jnp.cos(jnp.pi * place / 4.5))


ROWS = 160
EDGE = 128


def resample_kernel(side, weights_ref, window_ref, coeff_ref, shift_ref, out_ref):
    step = pl.program_id(1)
    first = pl.multiple_of(step * ROWS, ROWS)
    half = out_ref.shape[2]
    low = max(side * half - EDGE, 0)
    high = min(side * half + half + EDGE, window_ref.shape[2])
    window = window_ref[0, :, low:high].astype(jnp.float32)
    groups = ROWS // LOOK_AZ
    place = lax.broadcasted_iota(jnp.int32, (ROWS, window.shape[0]), 0)
    line = LOOK_AZ * (place % groups) + place // groups
    offset = lax.broadcasted_iota(jnp.int32, (ROWS, window.shape[0]), 1) - line
    taps = jnp.zeros((ROWS, window.shape[0]), jnp.float32)
    for tap in range(8):
        taps = jnp.where(offset == tap, weights_ref[tap], taps)
    along = jnp.dot(taps, window, precision=lax.Precision.HIGHEST, preferred_element_type=jnp.float32)
    zeros = jnp.zeros((ROWS, EDGE), jnp.float32)
    row = jnp.concatenate([zeros, along] if side == 0 else [along, zeros], axis=1)
    width = row.shape[1]
    shift = shift_ref[...]
    for bit in range(5):
        moved = pltpu.roll(row, width - (1 << bit), 1)
        row = jnp.where(((shift >> bit) & 1) == 1, moved, row)
    coeff = coeff_ref[...]
    result = None
    for tap in range(8):
        moved = pltpu.roll(row, width - (EDGE - 15 + tap), 1)[:, :half]
        term = coeff[:, tap : tap + 1] * moved
        result = term if result is None else result + term
    out_ref[0] = result.astype(out_ref.dtype)


def resample_half(side, weights, window, coeff, shift):
    nlines = coeff.shape[0]
    half = window.shape[2] // 2
    return pl.pallas_call(
        functools.partial(resample_kernel, side),
        grid=(2, nlines // ROWS),
        in_specs=[
            pl.BlockSpec(memory_space=pltpu.SMEM),
            pl.BlockSpec((1,) + window.shape[1:], lambda c, t: (c, 0, 0)),
            pl.BlockSpec((ROWS, 8), lambda c, t: (t, 0)),
            pl.BlockSpec((ROWS, 1), lambda c, t: (t, 0)),
        ],
        out_specs=pl.BlockSpec((1, ROWS, half), lambda c, t: (c, t, 0)),
        out_shape=jax.ShapeDtypeStruct((2, nlines, half), jnp.bfloat16),
        cost_estimate=pl.CostEstimate(
            flops=2 * nlines * half * 60, transcendentals=0, bytes_accessed=2 * nlines * half * 6
        ),
    )(weights, window, coeff, shift)


def resample_block(padded, shift_lines, kern_lines, shift_range, kern_range):
    table = kernel_table()
    nlines = shift_range.shape[0]
    border = OFFAZ + 4
    start = border + shift_lines - 3
    window = lax.dynamic_slice_in_dim(padded, start, nlines + 16, 1)
    weights = table[kern_lines]
    coeff = lines_in_look_order(jnp.take(table, kern_range, axis=0))
    shift = lines_in_look_order((shift_range + OFFRG)[:, None])
    left = resample_half(0, weights, window, coeff, shift)
    right = resample_half(1, weights, window, coeff, shift)
    return left, right


def lines_in_look_order(values):
    nlines = values.shape[0]
    return values.reshape(nlines // LOOK_AZ, LOOK_AZ, -1).transpose(1, 0, 2).reshape(nlines, -1)


CHUNK = 512


BLOCK = 1024


def looks_kernel(first_ref, second_ref, out_ref):
    rows = first_ref.shape[1]
    groups = rows // LOOK_AZ
    pooling = (
        lax.broadcasted_iota(jnp.int32, (CHUNK, CHUNK // LOOK_RG), 0) // LOOK_RG
        == lax.broadcasted_iota(jnp.int32, (CHUNK, CHUNK // LOOK_RG), 1)
    ).astype(jnp.float32)
    for low in range(0, first_ref.shape[2], CHUNK):
        first_re = first_ref[0, :, low : low + CHUNK].astype(jnp.float32)
        first_im = first_ref[1, :, low : low + CHUNK].astype(jnp.float32)
        second_re = second_ref[0, :, low : low + CHUNK].astype(jnp.float32)
        second_im = second_ref[1, :, low : low + CHUNK].astype(jnp.float32)
        real_part = first_re * second_re + first_im * second_im
        imag_part = first_im * second_re - first_re * second_im
        real_lines = real_part.reshape(LOOK_AZ, groups, CHUNK).sum(axis=0)
        imag_lines = imag_part.reshape(LOOK_AZ, groups, CHUNK).sum(axis=0)
        real_looks = jnp.dot(real_lines, pooling, precision=lax.Precision.HIGHEST, preferred_element_type=jnp.float32)
        imag_looks = jnp.dot(imag_lines, pooling, precision=lax.Precision.HIGHEST, preferred_element_type=jnp.float32)
        out = slice(low // LOOK_RG, (low + CHUNK) // LOOK_RG)
        out_ref[0, :, out] = real_looks / (LOOK_AZ * LOOK_RG)
        out_ref[1, :, out] = imag_looks / (LOOK_AZ * LOOK_RG)


def looks(first, second):
    nlines = first.shape[1]
    width = first.shape[2]
    groups = nlines // LOOK_AZ
    spec = pl.BlockSpec((2, nlines, BLOCK), lambda j: (0, 0, j))
    return pl.pallas_call(
        looks_kernel,
        grid=(width // BLOCK,),
        in_specs=[spec, spec],
        out_specs=pl.BlockSpec((2, groups, BLOCK // LOOK_RG), lambda j: (0, 0, j)),
        out_shape=jax.ShapeDtypeStruct((2, groups, width // LOOK_RG), jnp.float32),
        cost_estimate=pl.CostEstimate(
            flops=nlines * width * 40, transcendentals=0, bytes_accessed=2 * 2 * nlines * width * 2
        ),
    )(first, second)


def look_order(image):
    nlines = image.shape[1]
    groups = nlines // LOOK_AZ
    return image.reshape(2, groups, LOOK_AZ, image.shape[2]).transpose(0, 2, 1, 3).reshape(image.shape)


def conj(block):
    return jnp.stack([block[0], -block[1]])


def shards(slc, az_offset, az_kernel, rg_offset, rg_kernel, partners):
    padded = padded_2(slc, (("az", 2),), OFFAZ + 4, 9)
    own_left, own_right = resample_block(padded[0], az_offset[0], az_kernel[0], rg_offset[0], rg_kernel[0])
    date = lax.axis_index("date")
    even = date % 2 == 0

    left_2 = shifted(own_left, "date", 2)
    left_1 = swapped(jnp.where(even, left_2, own_left), "date")
    left_4 = shifted(left_2, "date", 2)
    right_2 = shifted(own_right, "date", -2)
    right_1 = swapped(jnp.where(even, own_right, right_2), "date")
    right_4 = shifted(right_2, "date", -2)
    ahead = {2: looks(own_left, left_2)}
    behind = {2: looks(own_right, right_2)}
    left_1, ahead[2] = lax.optimization_barrier((left_1, ahead[2]))
    right_1, behind[2] = lax.optimization_barrier((right_1, behind[2]))
    left_3 = shifted(left_1, "date", 2)
    right_3 = shifted(right_1, "date", -2)
    for s, other in ((1, left_1), (4, left_4), (3, left_3)):
        ahead[s] = looks(own_left, other)
    for s, other in ((1, right_1), (4, right_4), (3, right_3)):
        behind[s] = looks(own_right, other)
    count = lax.axis_size("date")
    target = lax.broadcasted_iota(jnp.int32, (count, 1, 1, 1), 0) - date
    sent = jnp.zeros((count,) + ahead[1].shape, jnp.float32)
    for s in range(1, GAP + 1):
        sent = jnp.where(target == s, ahead[s][None], sent)
        sent = jnp.where(target == -s, behind[s][None], sent)
    got = lax.all_to_all(sent, "date", 0, 0, tiled=True)
    full = {}
    for s in range(1, GAP + 1):
        right_of_ahead = conj(lax.dynamic_index_in_dim(got, jnp.minimum(date + s, count - 1), 0, keepdims=False))
        left_of_behind = conj(lax.dynamic_index_in_dim(got, jnp.maximum(date - s, 0), 0, keepdims=False))
        full[s] = jnp.concatenate([ahead[s], right_of_ahead], axis=2)
        full[-s] = jnp.concatenate([left_of_behind, behind[s]], axis=2)

    listed = partners[0]
    outputs = []
    for slot in range(PARTNERS):
        value = jnp.zeros_like(full[1])
        for step, block in full.items():
            value = jnp.where(listed[slot] == date + step, block, value)
        outputs.append(value)
    return jnp.stack(outputs)[None]


def solution(mesh):
    in_specs = (
        P("date", None, "az", None),
        P("date"),
        P("date"),
        P("date", "az"),
        P("date", "az"),
        P("date", None),
    )
    out_specs = P("date", None, None, "az", None)
    return jax.shard_map(shards, mesh=mesh, in_specs=in_specs, out_specs=out_specs, check_vma=False)
```

```python
import functools

import jax
import jax.numpy as jnp
from jax import lax
from jax.sharding import PartitionSpec as P
from jax.experimental import pallas as pl
from jax.experimental.pallas import tpu as pltpu

PARTNERS = 4
GAP = 4
OFFAZ = 12
OFFRG = 12
NFRAC = 64
LOOK_AZ = 20
LOOK_RG = 4


def padded_2(cells, sides, width, extra):
    for axis, dim in sides:
        count = lax.axis_size(axis)
        ends = count - 1
        head = lax.slice_in_dim(cells, 0, width + extra, axis=dim)
        tail = lax.slice_in_dim(cells, cells.shape[dim] - width, cells.shape[dim], axis=dim)
        cells = jnp.concatenate(
            [
                lax.ppermute(tail, axis, [(i, (i + 1) % count) for i in range(ends)]),
                cells,
                lax.ppermute(head, axis, [((i + 1) % count, i) for i in range(ends)]),
            ],
            axis=dim,
        )
    return cells


def shifted(block, axis, distance):
    count = lax.axis_size(axis)
    route = [(i + distance, i) for i in range(count) if 0 <= i + distance < count]
    return lax.ppermute(block, axis, route)


def swapped(block, axis):
    count = lax.axis_size(axis)
    return lax.ppermute(block, axis, [(i, i ^ 1) for i in range(count)])


def kernel_table():
    frac = jnp.arange(NFRAC, dtype=jnp.float32)[:, None] / NFRAC
    taps = jnp.arange(8, dtype=jnp.float32)[None, :]
    place = taps - 3.0 - frac
    return jnp.sinc(place) * (0.5 + 0.5 * jnp.cos(jnp.pi * place / 4.5))


ROWS = 160
EDGE = 128


def resample_kernel(side, weights_ref, window_ref, coeff_ref, shift_ref, out_ref):
    step = pl.program_id(1)
    first = pl.multiple_of(step * ROWS, ROWS)
    half = out_ref.shape[2]
    low = max(side * half - EDGE, 0)
    high = min(side * half + half + EDGE, window_ref.shape[2])
    window = window_ref[0, :, low:high].astype(jnp.float32)
    groups = ROWS // LOOK_AZ
    place = lax.broadcasted_iota(jnp.int32, (ROWS, window.shape[0]), 0)
    line = LOOK_AZ * (place % groups) + place // groups
    offset = lax.broadcasted_iota(jnp.int32, (ROWS, window.shape[0]), 1) - line
    taps = jnp.zeros((ROWS, window.shape[0]), jnp.float32)
    for tap in range(8):
        taps = jnp.where(offset == tap, weights_ref[tap], taps)
    along = jnp.dot(taps, window, precision=lax.Precision.HIGHEST, preferred_element_type=jnp.float32)
    zeros = jnp.zeros((ROWS, EDGE), jnp.float32)
    row = jnp.concatenate([zeros, along] if side == 0 else [along, zeros], axis=1)
    width = row.shape[1]
    shift = shift_ref[...]
    for bit in range(5):
        moved = pltpu.roll(row, width - (1 << bit), 1)
        row = jnp.where(((shift >> bit) & 1) == 1, moved, row)
    coeff = coeff_ref[...]
    result = None
    for tap in range(8):
        moved = pltpu.roll(row, width - (EDGE - 15 + tap), 1)[:, :half]
        term = coeff[:, tap : tap + 1] * moved
        result = term if result is None else result + term
    out_ref[0] = result.astype(out_ref.dtype)


def resample_half(side, weights, window, coeff, shift):
    nlines = coeff.shape[0]
    half = window.shape[2] // 2
    return pl.pallas_call(
        functools.partial(resample_kernel, side),
        grid=(2, nlines // ROWS),
        in_specs=[
            pl.BlockSpec(memory_space=pltpu.SMEM),
            pl.BlockSpec((1,) + window.shape[1:], lambda c, t: (c, 0, 0)),
            pl.BlockSpec((ROWS, 8), lambda c, t: (t, 0)),
            pl.BlockSpec((ROWS, 1), lambda c, t: (t, 0)),
        ],
        out_specs=pl.BlockSpec((1, ROWS, half), lambda c, t: (c, t, 0)),
        out_shape=jax.ShapeDtypeStruct((2, nlines, half), jnp.bfloat16),
        cost_estimate=pl.CostEstimate(
            flops=2 * nlines * half * 60, transcendentals=0, bytes_accessed=2 * nlines * half * 6
        ),
    )(weights, window, coeff, shift)


def resample_block(padded, shift_lines, kern_lines, shift_range, kern_range):
    table = kernel_table()
    nlines = shift_range.shape[0]
    border = OFFAZ + 4
    start = border + shift_lines - 3
    window = lax.dynamic_slice_in_dim(padded, start, nlines + 16, 1)
    weights = table[kern_lines]
    coeff = lines_in_look_order(jnp.take(table, kern_range, axis=0))
    shift = lines_in_look_order((shift_range + OFFRG)[:, None])
    left = resample_half(0, weights, window, coeff, shift)
    right = resample_half(1, weights, window, coeff, shift)
    return left, right


def lines_in_look_order(values):
    nlines = values.shape[0]
    return values.reshape(nlines // LOOK_AZ, LOOK_AZ, -1).transpose(1, 0, 2).reshape(nlines, -1)


CHUNK = 512


BLOCK = 2048


def looks_kernel(first_ref, second_ref, out_ref):
    rows = first_ref.shape[1]
    groups = rows // LOOK_AZ
    pooling = (
        lax.broadcasted_iota(jnp.int32, (CHUNK, CHUNK // LOOK_RG), 0) // LOOK_RG
        == lax.broadcasted_iota(jnp.int32, (CHUNK, CHUNK // LOOK_RG), 1)
    ).astype(jnp.float32)
    for low in range(0, first_ref.shape[2], CHUNK):
        first_re = first_ref[0, :, low : low + CHUNK].astype(jnp.float32)
        first_im = first_ref[1, :, low : low + CHUNK].astype(jnp.float32)
        second_re = second_ref[0, :, low : low + CHUNK].astype(jnp.float32)
        second_im = second_ref[1, :, low : low + CHUNK].astype(jnp.float32)
        real_part = first_re * second_re + first_im * second_im
        imag_part = first_im * second_re - first_re * second_im
        real_lines = real_part.reshape(LOOK_AZ, groups, CHUNK).sum(axis=0)
        imag_lines = imag_part.reshape(LOOK_AZ, groups, CHUNK).sum(axis=0)
        real_looks = jnp.dot(real_lines, pooling, precision=lax.Precision.HIGHEST, preferred_element_type=jnp.float32)
        imag_looks = jnp.dot(imag_lines, pooling, precision=lax.Precision.HIGHEST, preferred_element_type=jnp.float32)
        out = slice(low // LOOK_RG, (low + CHUNK) // LOOK_RG)
        out_ref[0, :, out] = real_looks / (LOOK_AZ * LOOK_RG)
        out_ref[1, :, out] = imag_looks / (LOOK_AZ * LOOK_RG)


def looks(first, second):
    nlines = first.shape[1]
    width = first.shape[2]
    groups = nlines // LOOK_AZ
    spec = pl.BlockSpec((2, nlines, BLOCK), lambda j: (0, 0, j))
    return pl.pallas_call(
        looks_kernel,
        grid=(width // BLOCK,),
        in_specs=[spec, spec],
        out_specs=pl.BlockSpec((2, groups, BLOCK // LOOK_RG), lambda j: (0, 0, j)),
        out_shape=jax.ShapeDtypeStruct((2, groups, width // LOOK_RG), jnp.float32),
        cost_estimate=pl.CostEstimate(
            flops=nlines * width * 40, transcendentals=0, bytes_accessed=2 * 2 * nlines * width * 2
        ),
    )(first, second)


def look_order(image):
    nlines = image.shape[1]
    groups = nlines // LOOK_AZ
    return image.reshape(2, groups, LOOK_AZ, image.shape[2]).transpose(0, 2, 1, 3).reshape(image.shape)


def conj(block):
    return jnp.stack([block[0], -block[1]])


def shards(slc, az_offset, az_kernel, rg_offset, rg_kernel, partners):
    padded = padded_2(slc, (("az", 2),), OFFAZ + 4, 9)
    own_left, own_right = resample_block(padded[0], az_offset[0], az_kernel[0], rg_offset[0], rg_kernel[0])
    date = lax.axis_index("date")
    even = date % 2 == 0

    left_2 = shifted(own_left, "date", 2)
    left_1 = swapped(jnp.where(even, left_2, own_left), "date")
    left_4 = shifted(left_2, "date", 2)
    right_2 = shifted(own_right, "date", -2)
    right_1 = swapped(jnp.where(even, own_right, right_2), "date")
    right_4 = shifted(right_2, "date", -2)
    ahead = {2: looks(own_left, left_2)}
    behind = {2: looks(own_right, right_2)}
    left_1, ahead[2] = lax.optimization_barrier((left_1, ahead[2]))
    right_1, behind[2] = lax.optimization_barrier((right_1, behind[2]))
    left_3 = shifted(left_1, "date", 2)
    right_3 = shifted(right_1, "date", -2)
    for s, other in ((1, left_1), (4, left_4), (3, left_3)):
        ahead[s] = looks(own_left, other)
    for s, other in ((1, right_1), (4, right_4), (3, right_3)):
        behind[s] = looks(own_right, other)
    count = lax.axis_size("date")
    target = lax.broadcasted_iota(jnp.int32, (count, 1, 1, 1), 0) - date
    sent = jnp.zeros((count,) + ahead[1].shape, jnp.float32)
    for s in range(1, GAP + 1):
        sent = jnp.where(target == s, ahead[s][None], sent)
        sent = jnp.where(target == -s, behind[s][None], sent)
    got = lax.all_to_all(sent, "date", 0, 0, tiled=True)
    full = {}
    for s in range(1, GAP + 1):
        right_of_ahead = conj(lax.dynamic_index_in_dim(got, jnp.minimum(date + s, count - 1), 0, keepdims=False))
        left_of_behind = conj(lax.dynamic_index_in_dim(got, jnp.maximum(date - s, 0), 0, keepdims=False))
        full[s] = jnp.concatenate([ahead[s], right_of_ahead], axis=2)
        full[-s] = jnp.concatenate([left_of_behind, behind[s]], axis=2)

    listed = partners[0]
    outputs = []
    for slot in range(PARTNERS):
        value = jnp.zeros_like(full[1])
        for step, block in full.items():
            value = jnp.where(listed[slot] == date + step, block, value)
        outputs.append(value)
    return jnp.stack(outputs)[None]


def solution(mesh):
    in_specs = (
        P("date", None, "az", None),
        P("date"),
        P("date"),
        P("date", "az"),
        P("date", "az"),
        P("date", None),
    )
    out_specs = P("date", None, None, "az", None)
    return jax.shard_map(shards, mesh=mesh, in_specs=in_specs, out_specs=out_specs, check_vma=False)
```

```python
import functools

import jax
import jax.numpy as jnp
from jax import lax
from jax.sharding import PartitionSpec as P
from jax.experimental import pallas as pl
from jax.experimental.pallas import tpu as pltpu

PARTNERS = 4
GAP = 4
OFFAZ = 12
OFFRG = 12
NFRAC = 64
LOOK_AZ = 20
LOOK_RG = 4


def padded_2(cells, sides, width, extra):
    for axis, dim in sides:
        count = lax.axis_size(axis)
        ends = count - 1
        head = lax.slice_in_dim(cells, 0, width + extra, axis=dim)
        tail = lax.slice_in_dim(cells, cells.shape[dim] - width, cells.shape[dim], axis=dim)
        cells = jnp.concatenate(
            [
                lax.ppermute(tail, axis, [(i, (i + 1) % count) for i in range(ends)]),
                cells,
                lax.ppermute(head, axis, [((i + 1) % count, i) for i in range(ends)]),
            ],
            axis=dim,
        )
    return cells


def shifted(block, axis, distance):
    count = lax.axis_size(axis)
    route = [(i + distance, i) for i in range(count) if 0 <= i + distance < count]
    return lax.ppermute(block, axis, route)


def swapped(block, axis):
    count = lax.axis_size(axis)
    return lax.ppermute(block, axis, [(i, i ^ 1) for i in range(count)])


def kernel_table():
    frac = jnp.arange(NFRAC, dtype=jnp.float32)[:, None] / NFRAC
    taps = jnp.arange(8, dtype=jnp.float32)[None, :]
    place = taps - 3.0 - frac
    return jnp.sinc(place) * (0.5 + 0.5 * jnp.cos(jnp.pi * place / 4.5))


ROWS = 160
EDGE = 128


def resample_kernel(side, weights_ref, window_ref, coeff_ref, shift_ref, out_ref):
    step = pl.program_id(1)
    first = pl.multiple_of(step * ROWS, ROWS)
    half = out_ref.shape[2]
    low = max(side * half - EDGE, 0)
    high = min(side * half + half + EDGE, window_ref.shape[2])
    window = window_ref[0, :, low:high].astype(jnp.float32)
    groups = ROWS // LOOK_AZ
    place = lax.broadcasted_iota(jnp.int32, (ROWS, window.shape[0]), 0)
    line = LOOK_AZ * (place % groups) + place // groups
    offset = lax.broadcasted_iota(jnp.int32, (ROWS, window.shape[0]), 1) - line
    taps = jnp.zeros((ROWS, window.shape[0]), jnp.float32)
    for tap in range(8):
        taps = jnp.where(offset == tap, weights_ref[tap], taps)
    along = jnp.dot(taps, window, precision=lax.Precision.HIGH, preferred_element_type=jnp.float32)
    zeros = jnp.zeros((ROWS, EDGE), jnp.float32)
    row = jnp.concatenate([zeros, along] if side == 0 else [along, zeros], axis=1)
    width = row.shape[1]
    shift = shift_ref[...]
    for bit in range(5):
        moved = pltpu.roll(row, width - (1 << bit), 1)
        row = jnp.where(((shift >> bit) & 1) == 1, moved, row)
    coeff = coeff_ref[...]
    result = None
    for tap in range(8):
        moved = pltpu.roll(row, width - (EDGE - 15 + tap), 1)[:, :half]
        term = coeff[:, tap : tap + 1] * moved
        result = term if result is None else result + term
    out_ref[0] = result.astype(out_ref.dtype)


def resample_half(side, weights, window, coeff, shift):
    nlines = coeff.shape[0]
    half = window.shape[2] // 2
    return pl.pallas_call(
        functools.partial(resample_kernel, side),
        grid=(2, nlines // ROWS),
        in_specs=[
            pl.BlockSpec(memory_space=pltpu.SMEM),
            pl.BlockSpec((1,) + window.shape[1:], lambda c, t: (c, 0, 0)),
            pl.BlockSpec((ROWS, 8), lambda c, t: (t, 0)),
            pl.BlockSpec((ROWS, 1), lambda c, t: (t, 0)),
        ],
        out_specs=pl.BlockSpec((1, ROWS, half), lambda c, t: (c, t, 0)),
        out_shape=jax.ShapeDtypeStruct((2, nlines, half), jnp.bfloat16),
        cost_estimate=pl.CostEstimate(
            flops=2 * nlines * half * 60, transcendentals=0, bytes_accessed=2 * nlines * half * 6
        ),
    )(weights, window, coeff, shift)


def resample_block(padded, shift_lines, kern_lines, shift_range, kern_range):
    table = kernel_table()
    nlines = shift_range.shape[0]
    border = OFFAZ + 4
    start = border + shift_lines - 3
    window = lax.dynamic_slice_in_dim(padded, start, nlines + 16, 1)
    weights = table[kern_lines]
    coeff = lines_in_look_order(jnp.take(table, kern_range, axis=0))
    shift = lines_in_look_order((shift_range + OFFRG)[:, None])
    left = resample_half(0, weights, window, coeff, shift)
    right = resample_half(1, weights, window, coeff, shift)
    return left, right


def lines_in_look_order(values):
    nlines = values.shape[0]
    return values.reshape(nlines // LOOK_AZ, LOOK_AZ, -1).transpose(1, 0, 2).reshape(nlines, -1)


CHUNK = 512


BLOCK = 1024


def looks_kernel(first_ref, second_ref, out_ref):
    rows = first_ref.shape[1]
    groups = rows // LOOK_AZ
    pooling = (
        lax.broadcasted_iota(jnp.int32, (CHUNK, CHUNK // LOOK_RG), 0) // LOOK_RG
        == lax.broadcasted_iota(jnp.int32, (CHUNK, CHUNK // LOOK_RG), 1)
    ).astype(jnp.float32)
    for low in range(0, first_ref.shape[2], CHUNK):
        first_re = first_ref[0, :, low : low + CHUNK].astype(jnp.float32)
        first_im = first_ref[1, :, low : low + CHUNK].astype(jnp.float32)
        second_re = second_ref[0, :, low : low + CHUNK].astype(jnp.float32)
        second_im = second_ref[1, :, low : low + CHUNK].astype(jnp.float32)
        real_part = first_re * second_re + first_im * second_im
        imag_part = first_im * second_re - first_re * second_im
        real_lines = real_part.reshape(LOOK_AZ, groups, CHUNK).sum(axis=0)
        imag_lines = imag_part.reshape(LOOK_AZ, groups, CHUNK).sum(axis=0)
        real_looks = jnp.dot(real_lines, pooling, precision=lax.Precision.HIGHEST, preferred_element_type=jnp.float32)
        imag_looks = jnp.dot(imag_lines, pooling, precision=lax.Precision.HIGHEST, preferred_element_type=jnp.float32)
        out = slice(low // LOOK_RG, (low + CHUNK) // LOOK_RG)
        out_ref[0, :, out] = real_looks / (LOOK_AZ * LOOK_RG)
        out_ref[1, :, out] = imag_looks / (LOOK_AZ * LOOK_RG)


def looks(first, second):
    nlines = first.shape[1]
    width = first.shape[2]
    groups = nlines // LOOK_AZ
    spec = pl.BlockSpec((2, nlines, BLOCK), lambda j: (0, 0, j))
    return pl.pallas_call(
        looks_kernel,
        grid=(width // BLOCK,),
        in_specs=[spec, spec],
        out_specs=pl.BlockSpec((2, groups, BLOCK // LOOK_RG), lambda j: (0, 0, j)),
        out_shape=jax.ShapeDtypeStruct((2, groups, width // LOOK_RG), jnp.float32),
        cost_estimate=pl.CostEstimate(
            flops=nlines * width * 40, transcendentals=0, bytes_accessed=2 * 2 * nlines * width * 2
        ),
    )(first, second)


def look_order(image):
    nlines = image.shape[1]
    groups = nlines // LOOK_AZ
    return image.reshape(2, groups, LOOK_AZ, image.shape[2]).transpose(0, 2, 1, 3).reshape(image.shape)


def conj(block):
    return jnp.stack([block[0], -block[1]])


def shards(slc, az_offset, az_kernel, rg_offset, rg_kernel, partners):
    padded = padded_2(slc, (("az", 2),), OFFAZ + 4, 9)
    own_left, own_right = resample_block(padded[0], az_offset[0], az_kernel[0], rg_offset[0], rg_kernel[0])
    date = lax.axis_index("date")
    even = date % 2 == 0

    left_2 = shifted(own_left, "date", 2)
    left_1 = swapped(jnp.where(even, left_2, own_left), "date")
    left_4 = shifted(left_2, "date", 2)
    right_2 = shifted(own_right, "date", -2)
    right_1 = swapped(jnp.where(even, own_right, right_2), "date")
    right_4 = shifted(right_2, "date", -2)
    ahead = {2: looks(own_left, left_2)}
    behind = {2: looks(own_right, right_2)}
    left_1, ahead[2] = lax.optimization_barrier((left_1, ahead[2]))
    right_1, behind[2] = lax.optimization_barrier((right_1, behind[2]))
    left_3 = shifted(left_1, "date", 2)
    right_3 = shifted(right_1, "date", -2)
    for s, other in ((1, left_1), (4, left_4), (3, left_3)):
        ahead[s] = looks(own_left, other)
    for s, other in ((1, right_1), (4, right_4), (3, right_3)):
        behind[s] = looks(own_right, other)
    count = lax.axis_size("date")
    target = lax.broadcasted_iota(jnp.int32, (count, 1, 1, 1), 0) - date
    sent = jnp.zeros((count,) + ahead[1].shape, jnp.float32)
    for s in range(1, GAP + 1):
        sent = jnp.where(target == s, ahead[s][None], sent)
        sent = jnp.where(target == -s, behind[s][None], sent)
    got = lax.all_to_all(sent, "date", 0, 0, tiled=True)
    full = {}
    for s in range(1, GAP + 1):
        right_of_ahead = conj(lax.dynamic_index_in_dim(got, jnp.minimum(date + s, count - 1), 0, keepdims=False))
        left_of_behind = conj(lax.dynamic_index_in_dim(got, jnp.maximum(date - s, 0), 0, keepdims=False))
        full[s] = jnp.concatenate([ahead[s], right_of_ahead], axis=2)
        full[-s] = jnp.concatenate([left_of_behind, behind[s]], axis=2)

    listed = partners[0]
    outputs = []
    for slot in range(PARTNERS):
        value = jnp.zeros_like(full[1])
        for step, block in full.items():
            value = jnp.where(listed[slot] == date + step, block, value)
        outputs.append(value)
    return jnp.stack(outputs)[None]


def solution(mesh):
    in_specs = (
        P("date", None, "az", None),
        P("date"),
        P("date"),
        P("date", "az"),
        P("date", "az"),
        P("date", None),
    )
    out_specs = P("date", None, None, "az", None)
    return jax.shard_map(shards, mesh=mesh, in_specs=in_specs, out_specs=out_specs, check_vma=False)
```

```python
import functools

import jax
import jax.numpy as jnp
from jax import lax
from jax.sharding import PartitionSpec as P
from jax.experimental import pallas as pl
from jax.experimental.pallas import tpu as pltpu

PARTNERS = 4
GAP = 4
OFFAZ = 12
OFFRG = 12
NFRAC = 64
LOOK_AZ = 20
LOOK_RG = 4


def padded_2(cells, sides, width, extra):
    for axis, dim in sides:
        count = lax.axis_size(axis)
        ends = count - 1
        head = lax.slice_in_dim(cells, 0, width + extra, axis=dim)
        tail = lax.slice_in_dim(cells, cells.shape[dim] - width, cells.shape[dim], axis=dim)
        cells = jnp.concatenate(
            [
                lax.ppermute(tail, axis, [(i, (i + 1) % count) for i in range(ends)]),
                cells,
                lax.ppermute(head, axis, [((i + 1) % count, i) for i in range(ends)]),
            ],
            axis=dim,
        )
    return cells


def shifted(block, axis, distance):
    count = lax.axis_size(axis)
    route = [(i + distance, i) for i in range(count) if 0 <= i + distance < count]
    return lax.ppermute(block, axis, route)


def swapped(block, axis):
    count = lax.axis_size(axis)
    return lax.ppermute(block, axis, [(i, i ^ 1) for i in range(count)])


def kernel_table():
    frac = jnp.arange(NFRAC, dtype=jnp.float32)[:, None] / NFRAC
    taps = jnp.arange(8, dtype=jnp.float32)[None, :]
    place = taps - 3.0 - frac
    return jnp.sinc(place) * (0.5 + 0.5 * jnp.cos(jnp.pi * place / 4.5))


ROWS = 160
EDGE = 128


def resample_kernel(side, weights_ref, window_ref, coeff_ref, shift_ref, out_ref):
    step = pl.program_id(1)
    first = pl.multiple_of(step * ROWS, ROWS)
    half = out_ref.shape[2]
    low = max(side * half - EDGE, 0)
    high = min(side * half + half + EDGE, window_ref.shape[2])
    window = window_ref[0, :, low:high].astype(jnp.float32)
    groups = ROWS // LOOK_AZ
    place = lax.broadcasted_iota(jnp.int32, (ROWS, window.shape[0]), 0)
    line = LOOK_AZ * (place % groups) + place // groups
    offset = lax.broadcasted_iota(jnp.int32, (ROWS, window.shape[0]), 1) - line
    taps = jnp.zeros((ROWS, window.shape[0]), jnp.float32)
    for tap in range(8):
        taps = jnp.where(offset == tap, weights_ref[tap], taps)
    along = jnp.dot(taps, window, precision=lax.Precision.HIGHEST, preferred_element_type=jnp.float32)
    zeros = jnp.zeros((ROWS, EDGE), jnp.float32)
    row = jnp.concatenate([zeros, along] if side == 0 else [along, zeros], axis=1)
    width = row.shape[1]
    shift = shift_ref[...]
    for bit in range(5):
        moved = pltpu.roll(row, width - (1 << bit), 1)
        row = jnp.where(((shift >> bit) & 1) == 1, moved, row)
    coeff = coeff_ref[...]
    result = None
    for tap in range(8):
        moved = pltpu.roll(row, width - (EDGE - 15 + tap), 1)[:, :half]
        term = coeff[:, tap : tap + 1] * moved
        result = term if result is None else result + term
    out_ref[0] = result.astype(out_ref.dtype)


def resample_half(side, weights, window, coeff, shift):
    nlines = coeff.shape[0]
    half = window.shape[2] // 2
    return pl.pallas_call(
        functools.partial(resample_kernel, side),
        grid=(2, nlines // ROWS),
        in_specs=[
            pl.BlockSpec(memory_space=pltpu.SMEM),
            pl.BlockSpec((1,) + window.shape[1:], lambda c, t: (c, 0, 0)),
            pl.BlockSpec((ROWS, 8), lambda c, t: (t, 0)),
            pl.BlockSpec((ROWS, 1), lambda c, t: (t, 0)),
        ],
        out_specs=pl.BlockSpec((1, ROWS, half), lambda c, t: (c, t, 0)),
        out_shape=jax.ShapeDtypeStruct((2, nlines, half), jnp.bfloat16),
        cost_estimate=pl.CostEstimate(
            flops=2 * nlines * half * 60, transcendentals=0, bytes_accessed=2 * nlines * half * 6
        ),
    )(weights, window, coeff, shift)


def resample_block(padded, shift_lines, kern_lines, shift_range, kern_range):
    table = kernel_table()
    nlines = shift_range.shape[0]
    border = OFFAZ + 4
    start = border + shift_lines - 3
    window = lax.dynamic_slice_in_dim(padded, start, nlines + 16, 1)
    weights = table[kern_lines]
    coeff = lines_in_look_order(jnp.take(table, kern_range, axis=0))
    shift = lines_in_look_order((shift_range + OFFRG)[:, None])
    left = resample_half(0, weights, window, coeff, shift)
    right = resample_half(1, weights, window, coeff, shift)
    return left, right


def lines_in_look_order(values):
    nlines = values.shape[0]
    return values.reshape(nlines // LOOK_AZ, LOOK_AZ, -1).transpose(1, 0, 2).reshape(nlines, -1)


CHUNK = 512


BLOCK = 1024


def looks_kernel(*refs):
    count = len(refs) // 3
    pooling = (
        lax.broadcasted_iota(jnp.int32, (CHUNK, CHUNK // LOOK_RG), 0) // LOOK_RG
        == lax.broadcasted_iota(jnp.int32, (CHUNK, CHUNK // LOOK_RG), 1)
    ).astype(jnp.float32)
    for pair in range(count):
        first_ref, second_ref, out_ref = refs[2 * pair], refs[2 * pair + 1], refs[2 * count + pair]
        rows = first_ref.shape[1]
        groups = rows // LOOK_AZ
        for low in range(0, first_ref.shape[2], CHUNK):
            first_re = first_ref[0, :, low : low + CHUNK].astype(jnp.float32)
            first_im = first_ref[1, :, low : low + CHUNK].astype(jnp.float32)
            second_re = second_ref[0, :, low : low + CHUNK].astype(jnp.float32)
            second_im = second_ref[1, :, low : low + CHUNK].astype(jnp.float32)
            real_part = first_re * second_re + first_im * second_im
            imag_part = first_im * second_re - first_re * second_im
            real_lines = real_part.reshape(LOOK_AZ, groups, CHUNK).sum(axis=0)
            imag_lines = imag_part.reshape(LOOK_AZ, groups, CHUNK).sum(axis=0)
            real_looks = jnp.dot(real_lines, pooling, precision=lax.Precision.HIGHEST, preferred_element_type=jnp.float32)
            imag_looks = jnp.dot(imag_lines, pooling, precision=lax.Precision.HIGHEST, preferred_element_type=jnp.float32)
            out = slice(low // LOOK_RG, (low + CHUNK) // LOOK_RG)
            out_ref[0, :, out] = real_looks / (LOOK_AZ * LOOK_RG)
            out_ref[1, :, out] = imag_looks / (LOOK_AZ * LOOK_RG)


def looks_pairs(*arrays):
    nlines = arrays[0].shape[1]
    width = arrays[0].shape[2]
    groups = nlines // LOOK_AZ
    count = len(arrays) // 2
    spec = pl.BlockSpec((2, nlines, BLOCK), lambda j: (0, 0, j))
    out_spec = pl.BlockSpec((2, groups, BLOCK // LOOK_RG), lambda j: (0, 0, j))
    return pl.pallas_call(
        looks_kernel,
        grid=(width // BLOCK,),
        in_specs=[spec] * (2 * count),
        out_specs=[out_spec] * count,
        out_shape=[jax.ShapeDtypeStruct((2, groups, width // LOOK_RG), jnp.float32)] * count,
        cost_estimate=pl.CostEstimate(
            flops=count * nlines * width * 40, transcendentals=0, bytes_accessed=count * 2 * 2 * nlines * width * 2
        ),
    )(*arrays)


def looks(first, second):
    return looks_pairs(first, second)[0]


def look_order(image):
    nlines = image.shape[1]
    groups = nlines // LOOK_AZ
    return image.reshape(2, groups, LOOK_AZ, image.shape[2]).transpose(0, 2, 1, 3).reshape(image.shape)


def conj(block):
    return jnp.stack([block[0], -block[1]])


def shards(slc, az_offset, az_kernel, rg_offset, rg_kernel, partners):
    padded = padded_2(slc, (("az", 2),), OFFAZ + 4, 9)
    own_left, own_right = resample_block(padded[0], az_offset[0], az_kernel[0], rg_offset[0], rg_kernel[0])
    date = lax.axis_index("date")
    even = date % 2 == 0

    left_2 = shifted(own_left, "date", 2)
    left_1 = swapped(jnp.where(even, left_2, own_left), "date")
    left_4 = shifted(left_2, "date", 2)
    right_2 = shifted(own_right, "date", -2)
    right_1 = swapped(jnp.where(even, own_right, right_2), "date")
    right_4 = shifted(right_2, "date", -2)
    ahead = {2: looks(own_left, left_2)}
    behind = {2: looks(own_right, right_2)}
    left_1, ahead[2] = lax.optimization_barrier((left_1, ahead[2]))
    right_1, behind[2] = lax.optimization_barrier((right_1, behind[2]))
    left_3 = shifted(left_1, "date", 2)
    right_3 = shifted(right_1, "date", -2)
    for s, other in ((1, left_1), (4, left_4)):
        ahead[s] = looks(own_left, other)
    for s, other in ((1, right_1), (4, right_4)):
        behind[s] = looks(own_right, other)
    ahead[3], behind[3] = looks_pairs(own_left, left_3, own_right, right_3)
    count = lax.axis_size("date")
    target = lax.broadcasted_iota(jnp.int32, (count, 1, 1, 1), 0) - date
    sent = jnp.zeros((count,) + ahead[1].shape, jnp.float32)
    for s in range(1, GAP + 1):
        sent = jnp.where(target == s, ahead[s][None], sent)
        sent = jnp.where(target == -s, behind[s][None], sent)
    got = lax.all_to_all(sent, "date", 0, 0, tiled=True)
    full = {}
    for s in range(1, GAP + 1):
        right_of_ahead = conj(lax.dynamic_index_in_dim(got, jnp.minimum(date + s, count - 1), 0, keepdims=False))
        left_of_behind = conj(lax.dynamic_index_in_dim(got, jnp.maximum(date - s, 0), 0, keepdims=False))
        full[s] = jnp.concatenate([ahead[s], right_of_ahead], axis=2)
        full[-s] = jnp.concatenate([left_of_behind, behind[s]], axis=2)

    listed = partners[0]
    outputs = []
    for slot in range(PARTNERS):
        value = jnp.zeros_like(full[1])
        for step, block in full.items():
            value = jnp.where(listed[slot] == date + step, block, value)
        outputs.append(value)
    return jnp.stack(outputs)[None]


def solution(mesh):
    in_specs = (
        P("date", None, "az", None),
        P("date"),
        P("date"),
        P("date", "az"),
        P("date", "az"),
        P("date", None),
    )
    out_specs = P("date", None, None, "az", None)
    return jax.shard_map(shards, mesh=mesh, in_specs=in_specs, out_specs=out_specs, check_vma=False)
```

```python
import functools

import jax
import jax.numpy as jnp
from jax import lax
from jax.sharding import PartitionSpec as P
from jax.experimental import pallas as pl
from jax.experimental.pallas import tpu as pltpu

PARTNERS = 4
GAP = 4
OFFAZ = 12
OFFRG = 12
NFRAC = 64
LOOK_AZ = 20
LOOK_RG = 4


def padded_2(cells, sides, width, extra):
    for axis, dim in sides:
        count = lax.axis_size(axis)
        ends = count - 1
        head = lax.slice_in_dim(cells, 0, width + extra, axis=dim)
        tail = lax.slice_in_dim(cells, cells.shape[dim] - width, cells.shape[dim], axis=dim)
        cells = jnp.concatenate(
            [
                lax.ppermute(tail, axis, [(i, (i + 1) % count) for i in range(ends)]),
                cells,
                lax.ppermute(head, axis, [((i + 1) % count, i) for i in range(ends)]),
            ],
            axis=dim,
        )
    return cells


def shifted(block, axis, distance):
    count = lax.axis_size(axis)
    route = [(i + distance, i) for i in range(count) if 0 <= i + distance < count]
    return lax.ppermute(block, axis, route)


def swapped(block, axis):
    count = lax.axis_size(axis)
    return lax.ppermute(block, axis, [(i, i ^ 1) for i in range(count)])


def kernel_table():
    frac = jnp.arange(NFRAC, dtype=jnp.float32)[:, None] / NFRAC
    taps = jnp.arange(8, dtype=jnp.float32)[None, :]
    place = taps - 3.0 - frac
    return jnp.sinc(place) * (0.5 + 0.5 * jnp.cos(jnp.pi * place / 4.5))


ROWS = 160
EDGE = 128


def resample_kernel(side, weights_ref, window_ref, coeff_ref, shift_ref, out_ref):
    step = pl.program_id(1)
    first = pl.multiple_of(step * ROWS, ROWS)
    half = out_ref.shape[2]
    low = max(side * half - EDGE, 0)
    high = min(side * half + half + EDGE, window_ref.shape[2])
    window = window_ref[0, :, low:high].astype(jnp.float32)
    groups = ROWS // LOOK_AZ
    place = lax.broadcasted_iota(jnp.int32, (ROWS, window.shape[0]), 0)
    line = LOOK_AZ * (place % groups) + place // groups
    offset = lax.broadcasted_iota(jnp.int32, (ROWS, window.shape[0]), 1) - line
    taps = jnp.zeros((ROWS, window.shape[0]), jnp.float32)
    for tap in range(8):
        taps = jnp.where(offset == tap, weights_ref[tap], taps)
    along = jnp.dot(taps, window, precision=lax.Precision.HIGHEST, preferred_element_type=jnp.float32)
    zeros = jnp.zeros((ROWS, EDGE), jnp.float32)
    row = jnp.concatenate([zeros, along] if side == 0 else [along, zeros], axis=1)
    width = row.shape[1]
    shift = shift_ref[...]
    for bit in range(5):
        moved = pltpu.roll(row, width - (1 << bit), 1)
        row = jnp.where(((shift >> bit) & 1) == 1, moved, row)
    coeff = coeff_ref[...]
    result = None
    for tap in range(8):
        moved = pltpu.roll(row, width - (EDGE - 15 + tap), 1)[:, :half]
        term = coeff[:, tap : tap + 1] * moved
        result = term if result is None else result + term
    out_ref[0] = result.astype(out_ref.dtype)


def resample_half(side, weights, window, coeff, shift):
    nlines = coeff.shape[0]
    half = window.shape[2] // 2
    return pl.pallas_call(
        functools.partial(resample_kernel, side),
        grid=(2, nlines // ROWS),
        in_specs=[
            pl.BlockSpec(memory_space=pltpu.SMEM),
            pl.BlockSpec((1,) + window.shape[1:], lambda c, t: (c, 0, 0)),
            pl.BlockSpec((ROWS, 8), lambda c, t: (t, 0)),
            pl.BlockSpec((ROWS, 1), lambda c, t: (t, 0)),
        ],
        out_specs=pl.BlockSpec((1, ROWS, half), lambda c, t: (c, t, 0)),
        out_shape=jax.ShapeDtypeStruct((2, nlines, half), jnp.bfloat16),
        cost_estimate=pl.CostEstimate(
            flops=2 * nlines * half * 60, transcendentals=0, bytes_accessed=2 * nlines * half * 6
        ),
    )(weights, window, coeff, shift)


def resample_block(padded, shift_lines, kern_lines, shift_range, kern_range):
    table = kernel_table()
    nlines = shift_range.shape[0]
    border = OFFAZ + 4
    start = border + shift_lines - 3
    window = lax.dynamic_slice_in_dim(padded, start, nlines + 16, 1)
    weights = table[kern_lines]
    coeff = lines_in_look_order(jnp.take(table, kern_range, axis=0))
    shift = lines_in_look_order((shift_range + OFFRG)[:, None])
    left = resample_half(0, weights, window, coeff, shift)
    right = resample_half(1, weights, window, coeff, shift)
    return left, right


def lines_in_look_order(values):
    nlines = values.shape[0]
    return values.reshape(nlines // LOOK_AZ, LOOK_AZ, -1).transpose(1, 0, 2).reshape(nlines, -1)


CHUNK = 512


BLOCK = 1024


def looks_kernel(first_ref, second_ref, out_ref):
    rows = first_ref.shape[1]
    groups = rows // LOOK_AZ
    pooling = (
        lax.broadcasted_iota(jnp.int32, (CHUNK, CHUNK // LOOK_RG), 0) // LOOK_RG
        == lax.broadcasted_iota(jnp.int32, (CHUNK, CHUNK // LOOK_RG), 1)
    ).astype(jnp.float32)
    for low in range(0, first_ref.shape[2], CHUNK):
        first_re = first_ref[0, :, low : low + CHUNK].astype(jnp.float32)
        first_im = first_ref[1, :, low : low + CHUNK].astype(jnp.float32)
        second_re = second_ref[0, :, low : low + CHUNK].astype(jnp.float32)
        second_im = second_ref[1, :, low : low + CHUNK].astype(jnp.float32)
        real_part = first_re * second_re + first_im * second_im
        imag_part = first_im * second_re - first_re * second_im
        real_lines = real_part.reshape(LOOK_AZ, groups, CHUNK).sum(axis=0)
        imag_lines = imag_part.reshape(LOOK_AZ, groups, CHUNK).sum(axis=0)
        real_looks = jnp.dot(real_lines, pooling, precision=lax.Precision.HIGHEST, preferred_element_type=jnp.float32)
        imag_looks = jnp.dot(imag_lines, pooling, precision=lax.Precision.HIGHEST, preferred_element_type=jnp.float32)
        out = slice(low // LOOK_RG, (low + CHUNK) // LOOK_RG)
        out_ref[0, :, out] = real_looks / (LOOK_AZ * LOOK_RG)
        out_ref[1, :, out] = imag_looks / (LOOK_AZ * LOOK_RG)


def looks(first, second):
    nlines = first.shape[1]
    width = first.shape[2]
    groups = nlines // LOOK_AZ
    spec = pl.BlockSpec((2, nlines, BLOCK), lambda j: (0, 0, j))
    return pl.pallas_call(
        looks_kernel,
        grid=(width // BLOCK,),
        in_specs=[spec, spec],
        out_specs=pl.BlockSpec((2, groups, BLOCK // LOOK_RG), lambda j: (0, 0, j)),
        out_shape=jax.ShapeDtypeStruct((2, groups, width // LOOK_RG), jnp.float32),
        cost_estimate=pl.CostEstimate(
            flops=nlines * width * 40, transcendentals=0, bytes_accessed=2 * 2 * nlines * width * 2
        ),
    )(first, second)


def look_order(image):
    nlines = image.shape[1]
    groups = nlines // LOOK_AZ
    return image.reshape(2, groups, LOOK_AZ, image.shape[2]).transpose(0, 2, 1, 3).reshape(image.shape)


def conj(block):
    return jnp.stack([block[0], -block[1]])


def shards(slc, az_offset, az_kernel, rg_offset, rg_kernel, partners):
    padded = padded_2(slc, (("az", 2),), OFFAZ + 4, 9)
    own_left, own_right = resample_block(padded[0], az_offset[0], az_kernel[0], rg_offset[0], rg_kernel[0])
    date = lax.axis_index("date")
    even = date % 2 == 0

    left_2 = shifted(own_left, "date", 2)
    left_1 = swapped(jnp.where(even, left_2, own_left), "date")
    left_4 = shifted(left_2, "date", 2)
    right_2 = shifted(own_right, "date", -2)
    right_1 = swapped(jnp.where(even, own_right, right_2), "date")
    right_4 = shifted(right_2, "date", -2)
    ahead = {2: looks(own_left, left_2)}
    behind = {2: looks(own_right, right_2)}
    left_3 = shifted(left_1, "date", 2)
    right_3 = shifted(right_1, "date", -2)
    for s, other in ((1, left_1), (4, left_4), (3, left_3)):
        ahead[s] = looks(own_left, other)
    for s, other in ((1, right_1), (4, right_4), (3, right_3)):
        behind[s] = looks(own_right, other)
    count = lax.axis_size("date")
    target = lax.broadcasted_iota(jnp.int32, (count, 1, 1, 1), 0) - date
    sent = jnp.zeros((count,) + ahead[1].shape, jnp.float32)
    for s in range(1, GAP + 1):
        sent = jnp.where(target == s, ahead[s][None], sent)
        sent = jnp.where(target == -s, behind[s][None], sent)
    got = lax.all_to_all(sent, "date", 0, 0, tiled=True)
    full = {}
    for s in range(1, GAP + 1):
        right_of_ahead = conj(lax.dynamic_index_in_dim(got, jnp.minimum(date + s, count - 1), 0, keepdims=False))
        left_of_behind = conj(lax.dynamic_index_in_dim(got, jnp.maximum(date - s, 0), 0, keepdims=False))
        full[s] = jnp.concatenate([ahead[s], right_of_ahead], axis=2)
        full[-s] = jnp.concatenate([left_of_behind, behind[s]], axis=2)

    listed = partners[0]
    outputs = []
    for slot in range(PARTNERS):
        value = jnp.zeros_like(full[1])
        for step, block in full.items():
            value = jnp.where(listed[slot] == date + step, block, value)
        outputs.append(value)
    return jnp.stack(outputs)[None]


def solution(mesh):
    in_specs = (
        P("date", None, "az", None),
        P("date"),
        P("date"),
        P("date", "az"),
        P("date", "az"),
        P("date", None),
    )
    out_specs = P("date", None, None, "az", None)
    return jax.shard_map(shards, mesh=mesh, in_specs=in_specs, out_specs=out_specs, check_vma=False)
```
